32 devices in a mesh: pairs: 2 (over x), row: 16 (over z, y, core).
Axes of the slice: x: 2, y: 2, z: 4, core: 2. Of those that a mesh axis runs over, the one named last changes fastest.
Arguments:
- frame_one: bfloat16 [128, 512, 128], P(('pairs', 'row')), parts along dimension 0, may hold values from -100 to 100
- frame_two: bfloat16 [128, 512, 128], P(('pairs', 'row')), parts along dimension 0, may hold values from -20 to 20
- tile_lists: int32 [128, 9], P(('pairs', 'row')), parts along dimension 0, may hold values from -1 to 63, as said below
- conv_one: bfloat16 [3, 3, 128, 128], replicated, may hold values from -0.1875 to 0.1875
- conv_two: bfloat16 [3, 3, 128, 128], replicated, may hold values from -0.1875 to 0.1875
Outputs:
- refined: bfloat16 [128, 512, 128], P(('pairs', 'row')), parts along dimension 0
The draws below stay inside these ranges and needn't reach their ends.
There are 2 independent parts, one for each index of `pairs`. The reference program is written for one: setup_inputs(seed, part) draws one part's arguments, and reference() takes and returns one part's arrays. A program takes and returns all parts, laid end to end along the dimension named above; an argument that names none is the same for every part. Nothing has to cross between parts.
Inputs may be any that keep to these rules, and one draw needn't show every extreme that they name: `tile_lists`: each query tile names 1 to 9 frame-2 tiles in its first slots and -1 in the rest; some tile names 9. The lists of the 4 query tiles of one device never name two different tiles held by the same device; one tile may be named by several of them.
All inputs are finite; a program needn't handle non-finite values.
Results may differ from the reference program's by a relative error of at most 0.0021.
Values may be sent and summed in bfloat16 or wider, within the bound.
No kernel may reach another device: no remote copies, remote signals or barrier semaphores. Data moves between devices by JAX's collectives and lax.ppermute only.
A program may use at most 64 MiB of HBM per device.

```python
import jax
import jax.numpy as jnp
from jax import lax

C = 128
TR = 4
TC = 128
TPD = 4
LIST = 9
TILE = 512
TILES = 64
WIDTH = 512
HEIGHT = 64
N_ROW = 16


def lists_draw(key):
    base = jax.random.fold_in(key, 11)
    key_perm, key_pick, key_count = jax.random.split(base, 3)
    rank_scores = jax.random.randint(key_perm, (N_ROW, N_ROW), 0, 1 << 20) * N_ROW
    rank_scores = rank_scores + jnp.arange(N_ROW, dtype=jnp.int32)[None, :]
    owner_order = jnp.argsort(rank_scores, axis=1).astype(jnp.int32)
    owner_pick = jax.random.randint(key_pick, (N_ROW, N_ROW), 0, TPD)
    counts = jax.random.randint(key_count, (N_ROW, TPD), 6, LIST + 1)
    counts = counts.at[0, 0].set(LIST)
    counts = counts.at[N_ROW - 1, TPD - 1].set(1)
    slot_index = jnp.arange(LIST, dtype=jnp.int32)
    position = (jnp.arange(TPD, dtype=jnp.int32)[:, None] * LIST + slot_index[None, :]) % N_ROW
    owner_ids = owner_order[:, position]
    local_ids = jnp.take_along_axis(owner_pick, owner_ids.reshape(N_ROW, TPD * LIST), axis=1)
    local_ids = local_ids.reshape(N_ROW, TPD, LIST)
    tile_ids = owner_ids * TPD + local_ids
    tile_ids = jnp.where(slot_index[None, None, :] < counts[:, :, None], tile_ids, -1)
    return tile_ids.reshape(TILES, LIST).astype(jnp.int32)


def frames_draw(key):
    base = jax.random.fold_in(key, 23)
    key_one, key_two = jax.random.split(base, 2)
    first = jax.random.normal(key_one, (HEIGHT, WIDTH, C), jnp.float32)
    second = jax.random.normal(key_two, (HEIGHT, WIDTH, C), jnp.float32)
    return (jnp.clip(first, -100.0, 100.0), jnp.clip(second, -20.0, 20.0))


def draw_frame_one(key, part):
    return frames_draw(key)[0].astype(jnp.bfloat16)


def draw_frame_two(key, part):
    return frames_draw(key)[1].astype(jnp.bfloat16)


def draw_tile_lists(key, part):
    return lists_draw(key)


def gaussian(own_key, extent, width, bound, held_as=jnp.bfloat16):
    return jnp.clip(width * jax.random.normal(own_key, extent, jnp.float32), -bound, bound).astype(held_as)


def setup_inputs(seed: int = 0, part: int = 0) -> dict:
    streams_of = jax.random.split(jax.random.key(seed), 6)
    own_keys = jax.random.split(jax.random.fold_in(streams_of[5], part), 6)
    return {
        "frame_one": draw_frame_one(jax.random.fold_in(jax.random.fold_in(streams_of[5], part), 71), part),
        "frame_two": draw_frame_two(jax.random.fold_in(jax.random.fold_in(streams_of[5], part), 71), part),
        "tile_lists": draw_tile_lists(jax.random.fold_in(jax.random.fold_in(streams_of[5], part), 71), part),
        "conv_one": gaussian(streams_of[3], (3, 3, C, C), (9 * C) ** -0.5, 0.1875),
        "conv_two": gaussian(streams_of[4], (3, 3, C, C), (9 * C) ** -0.5, 0.1875),
    }


def to_tiles(frame):
    return frame.reshape(N_ROW, TR, TPD, TC, C).transpose(0, 2, 1, 3, 4).reshape(TILES, TILE, C)


def to_frame(tiles):
    return tiles.reshape(N_ROW, TPD, TR, TC, C).transpose(0, 2, 1, 3, 4).reshape(HEIGHT, WIDTH, C)


def convolve(image, weights):
    padded = jnp.pad(image, ((1, 1), (1, 1), (0, 0)))
    height_here = image.shape[0]
    width_here = image.shape[1]
    summed = jnp.zeros((height_here * width_here, C), jnp.float32)
    for row_shift in range(3):
        for col_shift in range(3):
            window = padded[row_shift:row_shift + height_here, col_shift:col_shift + width_here]
            window = window.reshape(height_here * width_here, C)
            summed = summed + jnp.dot(window, weights[row_shift, col_shift], preferred_element_type=jnp.float32)
    return summed.reshape(height_here, width_here, C)


def reference(frame_one, frame_two, tile_lists, conv_one, conv_two):
    queries = to_tiles(frame_one)
    keys_all = to_tiles(frame_two)
    scale = float(C) ** -0.5

    def attend_tile(item):
        query, listed = item
        valid = listed >= 0
        chosen = jnp.take(keys_all, jnp.maximum(listed, 0).astype(jnp.int32), axis=0).astype(jnp.float32)
        scores = jnp.einsum("qc,jkc->qjk", query.astype(jnp.float32), chosen) * scale
        scores = jnp.where(valid[None, :, None], scores, -1e30)
        peak = jnp.max(scores, axis=(1, 2), keepdims=True)
        probs = jnp.exp(scores - peak)
        total = jnp.sum(probs, axis=(1, 2))
        rounded = lax.optimization_barrier(probs.astype(jnp.bfloat16)).astype(jnp.float32)
        mixed = jnp.einsum("qjk,jkc->qc", rounded, chosen) / total[:, None]
        return mixed.astype(jnp.bfloat16)

    warped = to_frame(lax.map(attend_tile, (queries, tile_lists)))
    hidden = jax.nn.relu(convolve(warped, conv_one)).astype(jnp.bfloat16)
    refined = frame_one.astype(jnp.float32) + convolve(hidden, conv_two)
    return refined.astype(jnp.bfloat16)
```

```python
import functools

import jax
import jax.numpy as jnp
from jax import lax
from jax.experimental import pallas as pl
from jax.experimental.pallas import tpu as pltpu
from jax.sharding import PartitionSpec as P


def halo_rows(cells, axis, width):
    count = lax.axis_size(axis)
    ends = count - 1
    head = cells[:width]
    tail = cells[cells.shape[0] - width :]
    from_above = lax.ppermute(tail, axis, [(i, i + 1) for i in range(ends)])
    from_below = lax.ppermute(head, axis, [(i + 1, i) for i in range(ends)])
    return jnp.concatenate([from_above, cells, from_below], axis=0)


def convolve_rows(padded, weights, out_rows, out_cols):
    channels = padded.shape[2]
    summed = jnp.zeros((out_rows * out_cols, channels), jnp.float32)
    for row_shift in range(3):
        for col_shift in range(3):
            window = padded[row_shift : row_shift + out_rows, col_shift : col_shift + out_cols]
            window = window.reshape(out_rows * out_cols, channels)
            summed = summed + jnp.dot(
                window, weights[row_shift, col_shift], preferred_element_type=jnp.float32
            )
    return summed.reshape(out_rows, out_cols, channels)


def pad_columns(image):
    return jnp.pad(image, ((0, 0), (1, 1), (0, 0)))


def attend_kernel(owner_ref, count_ref, q_ref, k_ref, o_ref, s_ref, m_ref, t_ref, a_ref, *, scale):
    t = pl.program_id(0)
    n = count_ref[t]
    q = q_ref[0]
    m_ref[...] = jnp.full(m_ref.shape, -jnp.inf, jnp.float32)

    def score(j, carry):
        kt = k_ref[owner_ref[t, j]]
        s = lax.dot_general(
            q, kt, (((1,), (1,)), ((), ())), preferred_element_type=jnp.float32
        ) * scale
        s_ref[j] = s
        m_ref[...] = jnp.maximum(m_ref[...], jnp.max(s, axis=1, keepdims=True))
        return carry

    lax.fori_loop(0, n, score, 0)
    t_ref[...] = jnp.zeros(t_ref.shape, jnp.float32)
    a_ref[...] = jnp.zeros(a_ref.shape, jnp.float32)

    def mix(j, carry):
        p = jnp.exp(s_ref[j] - m_ref[...])
        t_ref[...] += jnp.sum(p, axis=1, keepdims=True)
        kt = k_ref[owner_ref[t, j]]
        a_ref[...] += jnp.dot(p.astype(jnp.bfloat16), kt, preferred_element_type=jnp.float32)
        return carry

    lax.fori_loop(0, n, mix, 0)
    o_ref[0] = (a_ref[...] / t_ref[...]).astype(o_ref.dtype)


def attend(query_tiles, received, slot_owner, counts, scale, qblk):
    tiles, tile_size, channels = query_tiles.shape
    owners, key_size, _ = received.shape
    slots = slot_owner.shape[1]
    grid_spec = pltpu.PrefetchScalarGridSpec(
        num_scalar_prefetch=2,
        grid=(tiles, tile_size // qblk),
        in_specs=[
            pl.BlockSpec((1, qblk, channels), lambda t, b, o, c: (t, b, 0)),
            pl.BlockSpec((owners, key_size, channels), lambda t, b, o, c: (0, 0, 0)),
        ],
        out_specs=pl.BlockSpec((1, qblk, channels), lambda t, b, o, c: (t, b, 0)),
        scratch_shapes=[
            pltpu.VMEM((slots, qblk, key_size), jnp.float32),
            pltpu.VMEM((qblk, 1), jnp.float32),
            pltpu.VMEM((qblk, 1), jnp.float32),
            pltpu.VMEM((qblk, channels), jnp.float32),
        ],
    )
    return pl.pallas_call(
        functools.partial(attend_kernel, scale=scale),
        grid_spec=grid_spec,
        out_shape=jax.ShapeDtypeStruct(query_tiles.shape, jnp.bfloat16),
        compiler_params=pltpu.CompilerParams(vmem_limit_bytes=48 * 1024 * 1024),
    )(slot_owner, counts, query_tiles, received)


def on_device(frame_one, frame_two, tile_lists, conv_one, conv_two):
    band_rows, band_width, channels = frame_one.shape
    per_device = tile_lists.shape[0]
    tile_cols = band_width // per_device
    tile_size = band_rows * tile_cols
    owners = lax.axis_size("row")
    scale = float(channels) ** (-0.5)

    def band_to_tiles(band):
        return (
            band.reshape(band_rows, per_device, tile_cols, channels)
            .transpose(1, 0, 2, 3)
            .reshape(per_device, tile_size, channels)
        )

    query_tiles = band_to_tiles(frame_one)
    own_keys = band_to_tiles(frame_two)
    valid = tile_lists >= 0
    slot_owner = jnp.where(valid, tile_lists // per_device, 0).astype(jnp.int32)
    counts = jnp.sum(valid.astype(jnp.int32), axis=1)
    owner_iota = jnp.arange(owners, dtype=jnp.int32)
    matches = (slot_owner[:, :, None] == owner_iota[None, None, :]) & valid[:, :, None]
    wanted = jnp.max(jnp.where(matches, (tile_lists % per_device)[:, :, None], -1), axis=(0, 1))
    asked = lax.all_to_all(
        wanted.reshape(owners, 1), "row", split_axis=0, concat_axis=0, tiled=True
    )[:, 0]
    picked = jnp.take(own_keys, jnp.maximum(asked, 0), axis=0)
    outgoing = jnp.where((asked >= 0)[:, None, None], picked, jnp.zeros_like(picked))
    received = lax.all_to_all(outgoing, "row", split_axis=0, concat_axis=0, tiled=True)

    warped_tiles = attend(query_tiles, received, slot_owner, counts, scale, 256)
    warped = (
        warped_tiles.reshape(per_device, band_rows, tile_cols, channels)
        .transpose(1, 0, 2, 3)
        .reshape(band_rows, band_width, channels)
    )
    me = lax.axis_index("row")
    extended = halo_rows(warped, "row", 2)
    hidden = jax.nn.relu(
        convolve_rows(pad_columns(extended), conv_one, band_rows + 2, band_width)
    ).astype(jnp.bfloat16)
    row_ids = jnp.arange(band_rows + 2)
    inside = ((row_ids > 0) | (me > 0)) & ((row_ids < band_rows + 1) | (me < owners - 1))
    hidden = jnp.where(inside[:, None, None], hidden, jnp.zeros_like(hidden))
    branch = convolve_rows(pad_columns(hidden), conv_two, band_rows, band_width)
    return (frame_one.astype(jnp.float32) + branch).astype(jnp.bfloat16)


def solution(mesh):
    in_specs = (
        P(("pairs", "row"), None, None),
        P(("pairs", "row"), None, None),
        P(("pairs", "row"), None),
        P(),
        P(),
    )
    out_specs = P(("pairs", "row"), None, None)
    return jax.shard_map(
        on_device, mesh=mesh, in_specs=in_specs, out_specs=out_specs, check_vma=False
    )
```

```python
import functools

import jax
import jax.numpy as jnp
from jax import lax
from jax.experimental import pallas as pl
from jax.experimental.pallas import tpu as pltpu
from jax.sharding import PartitionSpec as P


def halo_rows(cells, axis, width):
    count = lax.axis_size(axis)
    ends = count - 1
    head = cells[:width]
    tail = cells[cells.shape[0] - width :]
    from_above = lax.ppermute(tail, axis, [(i, i + 1) for i in range(ends)])
    from_below = lax.ppermute(head, axis, [(i + 1, i) for i in range(ends)])
    return jnp.concatenate([from_above, cells, from_below], axis=0)


def convolve_rows(padded, weights, out_rows, out_cols):
    channels = padded.shape[2]
    summed = jnp.zeros((out_rows * out_cols, channels), jnp.float32)
    for row_shift in range(3):
        for col_shift in range(3):
            window = padded[row_shift : row_shift + out_rows, col_shift : col_shift + out_cols]
            window = window.reshape(out_rows * out_cols, channels)
            summed = summed + jnp.dot(
                window, weights[row_shift, col_shift], preferred_element_type=jnp.float32
            )
    return summed.reshape(out_rows, out_cols, channels)


def pad_columns(image):
    return jnp.pad(image, ((0, 0), (1, 1), (0, 0)))


def attend_kernel(owner_ref, count_ref, q_ref, k_ref, m_in, t_in, a_in, m_out, t_out, a_out, s_ref, *, scale):
    t = pl.program_id(0)
    n = count_ref[t]
    qt = q_ref[0]
    m_old = m_in[0]

    def score(j, m):
        kc = k_ref[owner_ref[t, j]]
        s = jnp.dot(kc, qt, preferred_element_type=jnp.float32) * scale
        s_ref[j] = s
        return jnp.maximum(m, jnp.max(s, axis=0, keepdims=True))

    m_new = lax.fori_loop(0, n, score, m_old)
    alpha = jnp.exp(m_old - m_new)
    m_out[0] = m_new
    a_out[0] = a_in[0] * alpha

    def mix(j, tot):
        p = jnp.exp(s_ref[j] - m_new)
        kc = k_ref[owner_ref[t, j]]
        a_out[0] += lax.dot_general(
            kc, p.astype(jnp.bfloat16), (((0,), (0,)), ((), ())),
            preferred_element_type=jnp.float32,
        )
        return tot + jnp.sum(p, axis=0, keepdims=True)

    t_out[0] = lax.fori_loop(0, n, mix, t_in[0] * alpha)


def attend_chunk(state, query_t, chunk, slot_owner, counts, scale):
    tiles, channels, tile_size = query_t.shape
    owners, chunk_len, _ = chunk.shape
    slots = slot_owner.shape[1]
    m, tot, acc = state
    row_spec = pl.BlockSpec((1, 1, tile_size), lambda t, o, c: (t, 0, 0))
    acc_spec = pl.BlockSpec((1, channels, tile_size), lambda t, o, c: (t, 0, 0))
    grid_spec = pltpu.PrefetchScalarGridSpec(
        num_scalar_prefetch=2,
        grid=(tiles,),
        in_specs=[
            pl.BlockSpec((1, channels, tile_size), lambda t, o, c: (t, 0, 0)),
            pl.BlockSpec((owners, chunk_len, channels), lambda t, o, c: (0, 0, 0)),
            row_spec,
            row_spec,
            acc_spec,
        ],
        out_specs=[row_spec, row_spec, acc_spec],
        scratch_shapes=[pltpu.VMEM((slots, chunk_len, tile_size), jnp.float32)],
    )
    return pl.pallas_call(
        functools.partial(attend_kernel, scale=scale),
        grid_spec=grid_spec,
        out_shape=[
            jax.ShapeDtypeStruct(m.shape, jnp.float32),
            jax.ShapeDtypeStruct(tot.shape, jnp.float32),
            jax.ShapeDtypeStruct(acc.shape, jnp.float32),
        ],
        input_output_aliases={4: 0, 5: 1, 6: 2},
        compiler_params=pltpu.CompilerParams(vmem_limit_bytes=48 * 1024 * 1024),
    )(slot_owner, counts, query_t, chunk, m, tot, acc)


def on_device(frame_one, frame_two, tile_lists, conv_one, conv_two):
    band_rows, band_width, channels = frame_one.shape
    per_device = tile_lists.shape[0]
    tile_cols = band_width // per_device
    tile_size = band_rows * tile_cols
    owners = lax.axis_size("row")
    scale = float(channels) ** (-0.5)

    def band_to_tiles(band):
        return (
            band.reshape(band_rows, per_device, tile_cols, channels)
            .transpose(1, 0, 2, 3)
            .reshape(per_device, tile_size, channels)
        )

    query_tiles = band_to_tiles(frame_one)
    own_keys = band_to_tiles(frame_two)
    valid = tile_lists >= 0
    slot_owner = jnp.where(valid, tile_lists // per_device, 0).astype(jnp.int32)
    counts = jnp.sum(valid.astype(jnp.int32), axis=1)
    owner_iota = jnp.arange(owners, dtype=jnp.int32)
    matches = (slot_owner[:, :, None] == owner_iota[None, None, :]) & valid[:, :, None]
    wanted = jnp.max(jnp.where(matches, (tile_lists % per_device)[:, :, None], -1), axis=(0, 1))
    asked = lax.all_to_all(
        wanted.reshape(owners, 1), "row", split_axis=0, concat_axis=0, tiled=True
    )[:, 0]
    picked = jnp.take(own_keys, jnp.maximum(asked, 0), axis=0)
    outgoing = jnp.where((asked >= 0)[:, None, None], picked, jnp.zeros_like(picked))
    query_t = query_tiles.transpose(0, 2, 1)
    pieces = 4
    chunk_len = tile_size // pieces
    state = (
        jnp.full((per_device, 1, tile_size), -jnp.inf, jnp.float32),
        jnp.zeros((per_device, 1, tile_size), jnp.float32),
        jnp.zeros((per_device, channels, tile_size), jnp.float32),
    )
    previous = None
    for piece in range(pieces):
        sending = outgoing[:, piece * chunk_len : (piece + 1) * chunk_len]
        if previous is not None:
            previous, sending, state = lax.optimization_barrier((previous, sending, state))
        current = lax.all_to_all(sending, "row", split_axis=0, concat_axis=0, tiled=True)
        if previous is not None:
            state = attend_chunk(state, query_t, previous, slot_owner, counts, scale)
        previous = current
    state = attend_chunk(state, query_t, previous, slot_owner, counts, scale)
    warped_tiles = (state[2] / state[1]).astype(jnp.bfloat16).transpose(0, 2, 1)
    warped = (
        warped_tiles.reshape(per_device, band_rows, tile_cols, channels)
        .transpose(1, 0, 2, 3)
        .reshape(band_rows, band_width, channels)
    )
    me = lax.axis_index("row")
    extended = halo_rows(warped, "row", 2)
    hidden = jax.nn.relu(
        convolve_rows(pad_columns(extended), conv_one, band_rows + 2, band_width)
    ).astype(jnp.bfloat16)
    row_ids = jnp.arange(band_rows + 2)
    inside = ((row_ids > 0) | (me > 0)) & ((row_ids < band_rows + 1) | (me < owners - 1))
    hidden = jnp.where(inside[:, None, None], hidden, jnp.zeros_like(hidden))
    branch = convolve_rows(pad_columns(hidden), conv_two, band_rows, band_width)
    return (frame_one.astype(jnp.float32) + branch).astype(jnp.bfloat16)


def solution(mesh):
    in_specs = (
        P(("pairs", "row"), None, None),
        P(("pairs", "row"), None, None),
        P(("pairs", "row"), None),
        P(),
        P(),
    )
    out_specs = P(("pairs", "row"), None, None)
    return jax.shard_map(
        on_device, mesh=mesh, in_specs=in_specs, out_specs=out_specs, check_vma=False
    )
```

```python
import jax
import jax.numpy as jnp
from jax import lax
from jax.sharding import PartitionSpec as P


def halo_rows(cells, axis, width):
    count = lax.axis_size(axis)
    ends = count - 1
    head = cells[:width]
    tail = cells[cells.shape[0] - width :]
    from_above = lax.ppermute(tail, axis, [(i, i + 1) for i in range(ends)])
    from_below = lax.ppermute(head, axis, [(i + 1, i) for i in range(ends)])
    return jnp.concatenate([from_above, cells, from_below], axis=0)


def convolve_rows(padded, weights, out_rows, out_cols):
    channels = padded.shape[2]
    summed = jnp.zeros((out_rows * out_cols, channels), jnp.float32)
    for row_shift in range(3):
        for col_shift in range(3):
            window = padded[row_shift : row_shift + out_rows, col_shift : col_shift + out_cols]
            window = window.reshape(out_rows * out_cols, channels)
            summed = summed + jnp.dot(
                window, weights[row_shift, col_shift], preferred_element_type=jnp.float32
            )
    return summed.reshape(out_rows, out_cols, channels)


def pad_columns(image):
    return jnp.pad(image, ((0, 0), (1, 1), (0, 0)))


def attend_chunk(state, queries, chunk, slot_owner, valid, scale):
    peak_old, total_old, mixed_old = state
    chosen = jnp.take(chunk, slot_owner, axis=0)
    scores = jnp.einsum("tqc,tjkc->tqjk", queries, chosen, preferred_element_type=jnp.float32) * scale
    scores = jnp.where(valid[:, None, :, None], scores, -1e30)
    peak = jnp.maximum(peak_old, jnp.max(scores, axis=(2, 3)))
    alpha = jnp.exp(peak_old - peak)
    probs = jnp.exp(scores - peak[:, :, None, None])
    total = total_old * alpha + jnp.sum(probs, axis=(2, 3))
    mixed = mixed_old * alpha[:, :, None] + jnp.einsum(
        "tqjk,tjkc->tqc", probs.astype(jnp.bfloat16), chosen, preferred_element_type=jnp.float32
    )
    return peak, total, mixed


def on_device(frame_one, frame_two, tile_lists, conv_one, conv_two):
    band_rows, band_width, channels = frame_one.shape
    per_device = tile_lists.shape[0]
    tile_cols = band_width // per_device
    tile_size = band_rows * tile_cols
    owners = lax.axis_size("row")
    scale = float(channels) ** (-0.5)

    def band_to_tiles(band):
        return (
            band.reshape(band_rows, per_device, tile_cols, channels)
            .transpose(1, 0, 2, 3)
            .reshape(per_device, tile_size, channels)
        )

    query_tiles = band_to_tiles(frame_one)
    own_keys = band_to_tiles(frame_two)
    valid = tile_lists >= 0
    slot_owner = jnp.where(valid, tile_lists // per_device, 0).astype(jnp.int32)
    owner_iota = jnp.arange(owners, dtype=jnp.int32)
    matches = (slot_owner[:, :, None] == owner_iota[None, None, :]) & valid[:, :, None]
    wanted = jnp.max(jnp.where(matches, (tile_lists % per_device)[:, :, None], -1), axis=(0, 1))
    asked = lax.all_to_all(
        wanted.reshape(owners, 1), "row", split_axis=0, concat_axis=0, tiled=True
    )[:, 0]
    picked = jnp.take(own_keys, jnp.maximum(asked, 0), axis=0)
    outgoing = jnp.where((asked >= 0)[:, None, None], picked, jnp.zeros_like(picked))
    pieces = 4
    chunk_len = tile_size // pieces
    state = (
        jnp.full((per_device, tile_size), -jnp.inf, jnp.float32),
        jnp.zeros((per_device, tile_size), jnp.float32),
        jnp.zeros((per_device, tile_size, channels), jnp.float32),
    )
    previous = None
    for piece in range(pieces):
        sending = outgoing[:, piece * chunk_len : (piece + 1) * chunk_len]
        if previous is not None:
            previous, sending, state = lax.optimization_barrier((previous, sending, state))
        current = lax.all_to_all(sending, "row", split_axis=0, concat_axis=0, tiled=True)
        if previous is not None:
            state = attend_chunk(state, query_tiles, previous, slot_owner, valid, scale)
        previous = current
    state = attend_chunk(state, query_tiles, previous, slot_owner, valid, scale)
    warped_tiles = (state[2] / state[1][:, :, None]).astype(jnp.bfloat16)
    warped = (
        warped_tiles.reshape(per_device, band_rows, tile_cols, channels)
        .transpose(1, 0, 2, 3)
        .reshape(band_rows, band_width, channels)
    )
    me = lax.axis_index("row")
    extended = halo_rows(warped, "row", 2)
    hidden = jax.nn.relu(
        convolve_rows(pad_columns(extended), conv_one, band_rows + 2, band_width)
    ).astype(jnp.bfloat16)
    row_ids = jnp.arange(band_rows + 2)
    inside = ((row_ids > 0) | (me > 0)) & ((row_ids < band_rows + 1) | (me < owners - 1))
    hidden = jnp.where(inside[:, None, None], hidden, jnp.zeros_like(hidden))
    branch = convolve_rows(pad_columns(hidden), conv_two, band_rows, band_width)
    return (frame_one.astype(jnp.float32) + branch).astype(jnp.bfloat16)


def solution(mesh):
    in_specs = (
        P(("pairs", "row"), None, None),
        P(("pairs", "row"), None, None),
        P(("pairs", "row"), None),
        P(),
        P(),
    )
    out_specs = P(("pairs", "row"), None, None)
    return jax.shard_map(
        on_device, mesh=mesh, in_specs=in_specs, out_specs=out_specs, check_vma=False
    )
```

```python
import functools

import jax
import jax.numpy as jnp
from jax import lax
from jax.experimental import pallas as pl
from jax.experimental.pallas import tpu as pltpu
from jax.sharding import PartitionSpec as P


def halo_rows(cells, axis, width):
    count = lax.axis_size(axis)
    ends = count - 1
    head = cells[:width]
    tail = cells[cells.shape[0] - width :]
    from_above = lax.ppermute(tail, axis, [(i, i + 1) for i in range(ends)])
    from_below = lax.ppermute(head, axis, [(i + 1, i) for i in range(ends)])
    return jnp.concatenate([from_above, cells, from_below], axis=0)


def convolve_rows(padded, weights, out_rows, out_cols):
    channels = padded.shape[2]
    summed = jnp.zeros((out_rows * out_cols, channels), jnp.float32)
    for row_shift in range(3):
        for col_shift in range(3):
            window = padded[row_shift : row_shift + out_rows, col_shift : col_shift + out_cols]
            window = window.reshape(out_rows * out_cols, channels)
            summed = summed + jnp.dot(
                window, weights[row_shift, col_shift], preferred_element_type=jnp.float32
            )
    return summed.reshape(out_rows, out_cols, channels)


def pad_columns(image):
    return jnp.pad(image, ((0, 0), (1, 1), (0, 0)))


def attend_kernel(owner_ref, count_ref, q_ref, k_ref, m_in, t_in, a_in, m_out, t_out, a_out, kall_ref, *, scale):
    t = pl.program_id(0)
    n = count_ref[t]
    slots = owner_ref.shape[1]
    span = k_ref.shape[1]
    lanes = 128
    for j in range(slots):
        kall_ref[j * span : (j + 1) * span, :] = k_ref[owner_ref[t, j]]
    q = q_ref[0]
    kall = kall_ref[...]
    s = lax.dot_general(q, kall, (((1,), (1,)), ((), ())), preferred_element_type=jnp.float32)
    penalty = [jnp.where(j < n, 0.0, jnp.inf).astype(jnp.float32) for j in range(slots)]
    blocks = [(j, j * span + c * lanes) for j in range(slots) for c in range(span // lanes)]
    mx = None
    for j, at in blocks:
        blk = s[:, at : at + lanes] - penalty[j]
        mx = blk if mx is None else jnp.maximum(mx, blk)
    m_old = m_in[0]
    m_new = jnp.maximum(m_old, jnp.max(mx, axis=1, keepdims=True) * scale)
    alpha = jnp.exp(m_old - m_new)
    mb = jnp.broadcast_to(m_new, (m_new.shape[0], lanes))
    shifted = [mb + penalty[j] for j in range(slots)]
    acc = None
    ps = []
    for j, at in blocks:
        p = jnp.exp(s[:, at : at + lanes] * scale - shifted[j])
        acc = p if acc is None else acc + p
        ps.append(p.astype(jnp.bfloat16))
    pb = jnp.concatenate(ps, axis=1)
    m_out[0] = m_new
    a_out[0] = a_in[0] * alpha + jnp.dot(pb, kall, preferred_element_type=jnp.float32)
    t_out[0] = t_in[0] * alpha + jnp.sum(acc, axis=1, keepdims=True)


def attend_chunk(state, queries, chunk, slot_owner, counts, scale):
    tiles, tile_size, channels = queries.shape
    owners, chunk_len, _ = chunk.shape
    slots = slot_owner.shape[1]
    m, tot, acc = state
    col_spec = pl.BlockSpec((1, tile_size, 1), lambda t, o, c: (t, 0, 0))
    acc_spec = pl.BlockSpec((1, tile_size, channels), lambda t, o, c: (t, 0, 0))
    grid_spec = pltpu.PrefetchScalarGridSpec(
        num_scalar_prefetch=2,
        grid=(tiles,),
        in_specs=[
            acc_spec,
            pl.BlockSpec((owners, chunk_len, channels), lambda t, o, c: (0, 0, 0)),
            col_spec,
            col_spec,
            acc_spec,
        ],
        out_specs=[col_spec, col_spec, acc_spec],
        scratch_shapes=[pltpu.VMEM((slots * chunk_len, channels), jnp.bfloat16)],
    )
    return pl.pallas_call(
        functools.partial(attend_kernel, scale=scale),
        grid_spec=grid_spec,
        out_shape=[
            jax.ShapeDtypeStruct(m.shape, jnp.float32),
            jax.ShapeDtypeStruct(tot.shape, jnp.float32),
            jax.ShapeDtypeStruct(acc.shape, jnp.float32),
        ],
        input_output_aliases={4: 0, 5: 1, 6: 2},
        compiler_params=pltpu.CompilerParams(vmem_limit_bytes=48 * 1024 * 1024),
    )(slot_owner, counts, queries, chunk, m, tot, acc)


def on_device(frame_one, frame_two, tile_lists, conv_one, conv_two):
    band_rows, band_width, channels = frame_one.shape
    per_device = tile_lists.shape[0]
    tile_cols = band_width // per_device
    tile_size = band_rows * tile_cols
    owners = lax.axis_size("row")
    scale = float(channels) ** (-0.5)

    def band_to_tiles(band):
        return (
            band.reshape(band_rows, per_device, tile_cols, channels)
            .transpose(1, 0, 2, 3)
            .reshape(per_device, tile_size, channels)
        )

    query_tiles = band_to_tiles(frame_one)
    own_keys = band_to_tiles(frame_two)
    valid = tile_lists >= 0
    slot_owner = jnp.where(valid, tile_lists // per_device, 0).astype(jnp.int32)
    counts = jnp.sum(valid.astype(jnp.int32), axis=1)
    owner_iota = jnp.arange(owners, dtype=jnp.int32)
    matches = (slot_owner[:, :, None] == owner_iota[None, None, :]) & valid[:, :, None]
    wanted = jnp.max(jnp.where(matches, (tile_lists % per_device)[:, :, None], -1), axis=(0, 1))
    asked = lax.all_to_all(
        wanted.reshape(owners, 1), "row", split_axis=0, concat_axis=0, tiled=True
    )[:, 0]
    picked = jnp.take(own_keys, jnp.maximum(asked, 0), axis=0)
    outgoing = jnp.where((asked >= 0)[:, None, None], picked, jnp.zeros_like(picked))
    pieces = 2
    chunk_len = tile_size // pieces
    state = (
        jnp.full((per_device, tile_size, 1), -jnp.inf, jnp.float32),
        jnp.zeros((per_device, tile_size, 1), jnp.float32),
        jnp.zeros((per_device, tile_size, channels), jnp.float32),
    )
    previous = None
    for piece in range(pieces):
        sending = outgoing[:, piece * chunk_len : (piece + 1) * chunk_len]
        if previous is not None:
            previous, sending, state = lax.optimization_barrier((previous, sending, state))
        current = lax.all_to_all(sending, "row", split_axis=0, concat_axis=0, tiled=True)
        if previous is not None:
            state = attend_chunk(state, query_tiles, previous, slot_owner, counts, scale)
        previous = current
    state = attend_chunk(state, query_tiles, previous, slot_owner, counts, scale)
    warped_tiles = (state[2] / state[1]).astype(jnp.bfloat16)
    warped = (
        warped_tiles.reshape(per_device, band_rows, tile_cols, channels)
        .transpose(1, 0, 2, 3)
        .reshape(band_rows, band_width, channels)
    )
    me = lax.axis_index("row")
    extended = halo_rows(warped, "row", 2)
    hidden = jax.nn.relu(
        convolve_rows(pad_columns(extended), conv_one, band_rows + 2, band_width)
    ).astype(jnp.bfloat16)
    row_ids = jnp.arange(band_rows + 2)
    inside = ((row_ids > 0) | (me > 0)) & ((row_ids < band_rows + 1) | (me < owners - 1))
    hidden = jnp.where(inside[:, None, None], hidden, jnp.zeros_like(hidden))
    branch = convolve_rows(pad_columns(hidden), conv_two, band_rows, band_width)
    return (frame_one.astype(jnp.float32) + branch).astype(jnp.bfloat16)


def solution(mesh):
    in_specs = (
        P(("pairs", "row"), None, None),
        P(("pairs", "row"), None, None),
        P(("pairs", "row"), None),
        P(),
        P(),
    )
    out_specs = P(("pairs", "row"), None, None)
    return jax.shard_map(
        on_device, mesh=mesh, in_specs=in_specs, out_specs=out_specs, check_vma=False
    )
```

```python
import functools

import jax
import jax.numpy as jnp
from jax import lax
from jax.experimental import pallas as pl
from jax.experimental.pallas import tpu as pltpu
from jax.sharding import PartitionSpec as P


def halo_rows(cells, axis, width):
    count = lax.axis_size(axis)
    ends = count - 1
    head = cells[:width]
    tail = cells[cells.shape[0] - width :]
    from_above = lax.ppermute(tail, axis, [(i, i + 1) for i in range(ends)])
    from_below = lax.ppermute(head, axis, [(i + 1, i) for i in range(ends)])
    return jnp.concatenate([from_above, cells, from_below], axis=0)


def convolve_rows(padded, weights, out_rows, out_cols):
    channels = padded.shape[2]
    summed = jnp.zeros((out_rows * out_cols, channels), jnp.float32)
    for row_shift in range(3):
        for col_shift in range(3):
            window = padded[row_shift : row_shift + out_rows, col_shift : col_shift + out_cols]
            window = window.reshape(out_rows * out_cols, channels)
            summed = summed + jnp.dot(
                window, weights[row_shift, col_shift], preferred_element_type=jnp.float32
            )
    return summed.reshape(out_rows, out_cols, channels)


def pad_columns(image):
    return jnp.pad(image, ((0, 0), (1, 1), (0, 0)))


def attend_kernel(owner_ref, count_ref, q_ref, k_ref, m_in, t_in, a_in, m_out, t_out, a_out, kall_ref, *, scale):
    t = pl.program_id(0)
    n = count_ref[t]
    slots = owner_ref.shape[1]
    span = k_ref.shape[1]
    lanes = 128
    for j in range(slots):
        kall_ref[j * span : (j + 1) * span, :] = k_ref[owner_ref[t, j]]
    q = q_ref[0]
    kall = kall_ref[...]
    s = lax.dot_general(q, kall, (((1,), (1,)), ((), ())), preferred_element_type=jnp.float32)
    penalty = [jnp.where(j < n, 0.0, jnp.inf).astype(jnp.float32) for j in range(slots)]
    blocks = [(j, j * span + c * lanes) for j in range(slots) for c in range(span // lanes)]
    mx = None
    for j, at in blocks:
        blk = s[:, at : at + lanes]
        mx = blk if mx is None else jnp.maximum(mx, blk)
    m_old = m_in[0]
    m_new = jnp.maximum(m_old, jnp.max(mx, axis=1, keepdims=True) * scale)
    alpha = jnp.exp(m_old - m_new)
    log2e = 1.4426950408889634
    mb = jnp.broadcast_to(m_new * log2e, (m_new.shape[0], lanes))
    shifted = [mb + penalty[j] for j in range(slots)]
    acc = None
    ps = []
    for j, at in blocks:
        p = jnp.exp2(s[:, at : at + lanes] * (scale * log2e) - shifted[j])
        acc = p if acc is None else acc + p
        ps.append(p.astype(jnp.bfloat16))
    pb = jnp.concatenate(ps, axis=1)
    m_out[0] = m_new
    a_out[0] = a_in[0] * alpha + jnp.dot(pb, kall, preferred_element_type=jnp.float32)
    t_out[0] = t_in[0] * alpha + jnp.sum(acc, axis=1, keepdims=True)


def attend_chunk(state, queries, chunk, slot_owner, counts, scale):
    tiles, tile_size, channels = queries.shape
    owners, chunk_len, _ = chunk.shape
    slots = slot_owner.shape[1]
    m, tot, acc = state
    col_spec = pl.BlockSpec((1, tile_size, 1), lambda t, o, c: (t, 0, 0))
    acc_spec = pl.BlockSpec((1, tile_size, channels), lambda t, o, c: (t, 0, 0))
    grid_spec = pltpu.PrefetchScalarGridSpec(
        num_scalar_prefetch=2,
        grid=(tiles,),
        in_specs=[
            acc_spec,
            pl.BlockSpec((owners, chunk_len, channels), lambda t, o, c: (0, 0, 0)),
            col_spec,
            col_spec,
            acc_spec,
        ],
        out_specs=[col_spec, col_spec, acc_spec],
        scratch_shapes=[pltpu.VMEM((slots * chunk_len, channels), jnp.bfloat16)],
    )
    return pl.pallas_call(
        functools.partial(attend_kernel, scale=scale),
        grid_spec=grid_spec,
        out_shape=[
            jax.ShapeDtypeStruct(m.shape, jnp.float32),
            jax.ShapeDtypeStruct(tot.shape, jnp.float32),
            jax.ShapeDtypeStruct(acc.shape, jnp.float32),
        ],
        input_output_aliases={4: 0, 5: 1, 6: 2},
        compiler_params=pltpu.CompilerParams(vmem_limit_bytes=48 * 1024 * 1024),
    )(slot_owner, counts, queries, chunk, m, tot, acc)


def on_device(frame_one, frame_two, tile_lists, conv_one, conv_two):
    band_rows, band_width, channels = frame_one.shape
    per_device = tile_lists.shape[0]
    tile_cols = band_width // per_device
    tile_size = band_rows * tile_cols
    owners = lax.axis_size("row")
    scale = float(channels) ** (-0.5)

    def band_to_tiles(band):
        return (
            band.reshape(band_rows, per_device, tile_cols, channels)
            .transpose(1, 0, 2, 3)
            .reshape(per_device, tile_size, channels)
        )

    query_tiles = band_to_tiles(frame_one)
    own_keys = band_to_tiles(frame_two)
    valid = tile_lists >= 0
    slot_owner = jnp.maximum(jnp.where(valid, tile_lists, tile_lists[:, :1]), 0) // per_device
    counts = jnp.sum(valid.astype(jnp.int32), axis=1)
    owner_iota = jnp.arange(owners, dtype=jnp.int32)
    matches = (slot_owner[:, :, None] == owner_iota[None, None, :]) & valid[:, :, None]
    wanted = jnp.max(jnp.where(matches, (tile_lists % per_device)[:, :, None], -1), axis=(0, 1))
    asked = lax.all_to_all(
        wanted.reshape(owners, 1), "row", split_axis=0, concat_axis=0, tiled=True
    )[:, 0]
    picked = jnp.take(own_keys, jnp.maximum(asked, 0), axis=0)
    outgoing = jnp.where((asked >= 0)[:, None, None], picked, jnp.zeros_like(picked))
    pieces = 2
    chunk_len = tile_size // pieces
    state = (
        jnp.full((per_device, tile_size, 1), -jnp.inf, jnp.float32),
        jnp.zeros((per_device, tile_size, 1), jnp.float32),
        jnp.zeros((per_device, tile_size, channels), jnp.float32),
    )
    previous = None
    for piece in range(pieces):
        sending = outgoing[:, piece * chunk_len : (piece + 1) * chunk_len]
        if previous is not None:
            previous, sending, state = lax.optimization_barrier((previous, sending, state))
        current = lax.all_to_all(sending, "row", split_axis=0, concat_axis=0, tiled=True)
        if previous is not None:
            state = attend_chunk(state, query_tiles, previous, slot_owner, counts, scale)
        previous = current
    state = attend_chunk(state, query_tiles, previous, slot_owner, counts, scale)
    warped_tiles = (state[2] / state[1]).astype(jnp.bfloat16)
    warped = (
        warped_tiles.reshape(per_device, band_rows, tile_cols, channels)
        .transpose(1, 0, 2, 3)
        .reshape(band_rows, band_width, channels)
    )
    me = lax.axis_index("row")
    extended = halo_rows(warped, "row", 2)
    hidden = jax.nn.relu(
        convolve_rows(pad_columns(extended), conv_one, band_rows + 2, band_width)
    ).astype(jnp.bfloat16)
    row_ids = jnp.arange(band_rows + 2)
    inside = ((row_ids > 0) | (me > 0)) & ((row_ids < band_rows + 1) | (me < owners - 1))
    hidden = jnp.where(inside[:, None, None], hidden, jnp.zeros_like(hidden))
    branch = convolve_rows(pad_columns(hidden), conv_two, band_rows, band_width)
    return (frame_one.astype(jnp.float32) + branch).astype(jnp.bfloat16)


def solution(mesh):
    in_specs = (
        P(("pairs", "row"), None, None),
        P(("pairs", "row"), None, None),
        P(("pairs", "row"), None),
        P(),
        P(),
    )
    out_specs = P(("pairs", "row"), None, None)
    return jax.shard_map(
        on_device, mesh=mesh, in_specs=in_specs, out_specs=out_specs, check_vma=False
    )
```

```python
import functools

import jax
import jax.numpy as jnp
from jax import lax
from jax.experimental import pallas as pl
from jax.experimental.pallas import tpu as pltpu
from jax.sharding import PartitionSpec as P


def halo_rows(cells, axis, width):
    count = lax.axis_size(axis)
    ends = count - 1
    head = cells[:width]
    tail = cells[cells.shape[0] - width :]
    from_above = lax.ppermute(tail, axis, [(i, i + 1) for i in range(ends)])
    from_below = lax.ppermute(head, axis, [(i + 1, i) for i in range(ends)])
    return jnp.concatenate([from_above, cells, from_below], axis=0)


def convolve_rows(padded, weights, out_rows, out_cols):
    channels = padded.shape[2]
    summed = jnp.zeros((out_rows * out_cols, channels), jnp.float32)
    for row_shift in range(3):
        for col_shift in range(3):
            window = padded[row_shift : row_shift + out_rows, col_shift : col_shift + out_cols]
            window = window.reshape(out_rows * out_cols, channels)
            summed = summed + jnp.dot(
                window, weights[row_shift, col_shift], preferred_element_type=jnp.float32
            )
    return summed.reshape(out_rows, out_cols, channels)


def pad_columns(image):
    return jnp.pad(image, ((0, 0), (1, 1), (0, 0)))


def attend_kernel(owner_ref, count_ref, q_ref, k_ref, m_in, t_in, a_in, m_out, t_out, a_out, kall_ref, *, scale):
    t = pl.program_id(0)
    n = count_ref[t]
    slots = owner_ref.shape[1]
    span = k_ref.shape[1]
    lanes = 128
    for j in range(slots):
        kall_ref[j * span : (j + 1) * span, :] = k_ref[owner_ref[t, j]]
    q = q_ref[0]
    kall = kall_ref[...]
    s = lax.dot_general(q, kall, (((1,), (1,)), ((), ())), preferred_element_type=jnp.float32)
    penalty = [jnp.where(j < n, 0.0, jnp.inf).astype(jnp.float32) for j in range(slots)]
    blocks = [(j, j * span + c * lanes) for j in range(slots) for c in range(span // lanes)]
    mx = None
    for j, at in blocks:
        blk = s[:, at : at + lanes]
        mx = blk if mx is None else jnp.maximum(mx, blk)
    m_old = m_in[0]
    m_new = jnp.maximum(m_old, jnp.max(mx, axis=1, keepdims=True) * scale)
    alpha = jnp.exp(m_old - m_new)
    log2e = 1.4426950408889634
    mb = jnp.broadcast_to(m_new * log2e, (m_new.shape[0], lanes))
    shifted = [mb + penalty[j] for j in range(slots)]
    acc = None
    ps = []
    for j, at in blocks:
        p = jnp.exp2(s[:, at : at + lanes] * (scale * log2e) - shifted[j])
        acc = p if acc is None else acc + p
        ps.append(p.astype(jnp.bfloat16))
    pb = jnp.concatenate(ps, axis=1)
    m_out[0] = m_new
    a_out[0] = a_in[0] * alpha + jnp.dot(pb, kall, preferred_element_type=jnp.float32)
    t_out[0] = t_in[0] * alpha + jnp.sum(acc, axis=1, keepdims=True)


def attend_chunk(state, queries, chunk, slot_owner, counts, scale):
    tiles, tile_size, channels = queries.shape
    owners, chunk_len, _ = chunk.shape
    slots = slot_owner.shape[1]
    m, tot, acc = state
    col_spec = pl.BlockSpec((1, tile_size, 1), lambda t, o, c: (t, 0, 0))
    acc_spec = pl.BlockSpec((1, tile_size, channels), lambda t, o, c: (t, 0, 0))
    grid_spec = pltpu.PrefetchScalarGridSpec(
        num_scalar_prefetch=2,
        grid=(tiles,),
        in_specs=[
            acc_spec,
            pl.BlockSpec((owners, chunk_len, channels), lambda t, o, c: (0, 0, 0)),
            col_spec,
            col_spec,
            acc_spec,
        ],
        out_specs=[col_spec, col_spec, acc_spec],
        scratch_shapes=[pltpu.VMEM((slots * chunk_len, channels), jnp.bfloat16)],
    )
    return pl.pallas_call(
        functools.partial(attend_kernel, scale=scale),
        grid_spec=grid_spec,
        out_shape=[
            jax.ShapeDtypeStruct(m.shape, jnp.float32),
            jax.ShapeDtypeStruct(tot.shape, jnp.float32),
            jax.ShapeDtypeStruct(acc.shape, jnp.float32),
        ],
        input_output_aliases={4: 0, 5: 1, 6: 2},
        compiler_params=pltpu.CompilerParams(vmem_limit_bytes=48 * 1024 * 1024),
    )(slot_owner, counts, queries, chunk, m, tot, acc)


def on_device(frame_one, frame_two, tile_lists, conv_one, conv_two):
    band_rows, band_width, channels = frame_one.shape
    per_device = tile_lists.shape[0]
    tile_cols = band_width // per_device
    tile_size = band_rows * tile_cols
    owners = lax.axis_size("row")
    scale = float(channels) ** (-0.5)

    def band_to_tiles(band):
        return (
            band.reshape(band_rows, per_device, tile_cols, channels)
            .transpose(1, 0, 2, 3)
            .reshape(per_device, tile_size, channels)
        )

    query_tiles = band_to_tiles(frame_one)
    own_keys = band_to_tiles(frame_two)
    valid = tile_lists >= 0
    slot_owner = jnp.maximum(jnp.where(valid, tile_lists, tile_lists[:, :1]), 0) // per_device
    counts = jnp.sum(valid.astype(jnp.int32), axis=1)
    owner_iota = jnp.arange(owners, dtype=jnp.int32)
    matches = (slot_owner[:, :, None] == owner_iota[None, None, :]) & valid[:, :, None]
    wanted = jnp.max(jnp.where(matches, (tile_lists % per_device)[:, :, None], -1), axis=(0, 1))
    asked = lax.all_to_all(
        wanted.reshape(owners, 1), "row", split_axis=0, concat_axis=0, tiled=True
    )[:, 0]
    outgoing = jnp.take(own_keys, jnp.maximum(asked, 0), axis=0)
    edges = [0, tile_size - tile_size // 4, tile_size]
    state = (
        jnp.full((per_device, tile_size, 1), -jnp.inf, jnp.float32),
        jnp.zeros((per_device, tile_size, 1), jnp.float32),
        jnp.zeros((per_device, tile_size, channels), jnp.float32),
    )
    previous = None
    for start, stop in zip(edges[:-1], edges[1:]):
        sending = outgoing[:, start:stop]
        if previous is not None:
            previous, sending, state = lax.optimization_barrier((previous, sending, state))
        current = lax.all_to_all(sending, "row", split_axis=0, concat_axis=0, tiled=True)
        if previous is not None:
            state = attend_chunk(state, query_tiles, previous, slot_owner, counts, scale)
        previous = current
    state = attend_chunk(state, query_tiles, previous, slot_owner, counts, scale)
    warped_tiles = (state[2] / state[1]).astype(jnp.bfloat16)
    warped = (
        warped_tiles.reshape(per_device, band_rows, tile_cols, channels)
        .transpose(1, 0, 2, 3)
        .reshape(band_rows, band_width, channels)
    )
    me = lax.axis_index("row")
    extended = halo_rows(warped, "row", 2)
    hidden = jax.nn.relu(
        convolve_rows(pad_columns(extended), conv_one, band_rows + 2, band_width)
    ).astype(jnp.bfloat16)
    row_ids = jnp.arange(band_rows + 2)
    inside = ((row_ids > 0) | (me > 0)) & ((row_ids < band_rows + 1) | (me < owners - 1))
    hidden = jnp.where(inside[:, None, None], hidden, jnp.zeros_like(hidden))
    branch = convolve_rows(pad_columns(hidden), conv_two, band_rows, band_width)
    return (frame_one.astype(jnp.float32) + branch).astype(jnp.bfloat16)


def solution(mesh):
    in_specs = (
        P(("pairs", "row"), None, None),
        P(("pairs", "row"), None, None),
        P(("pairs", "row"), None),
        P(),
        P(),
    )
    out_specs = P(("pairs", "row"), None, None)
    return jax.shard_map(
        on_device, mesh=mesh, in_specs=in_specs, out_specs=out_specs, check_vma=False
    )
```

```python
import functools

import jax
import jax.numpy as jnp
from jax import lax
from jax.experimental import pallas as pl
from jax.experimental.pallas import tpu as pltpu
from jax.sharding import PartitionSpec as P


def halo_rows(cells, axis, width):
    count = lax.axis_size(axis)
    ends = count - 1
    head = cells[:width]
    tail = cells[cells.shape[0] - width :]
    from_above = lax.ppermute(tail, axis, [(i, i + 1) for i in range(ends)])
    from_below = lax.ppermute(head, axis, [(i + 1, i) for i in range(ends)])
    return jnp.concatenate([from_above, cells, from_below], axis=0)


def convolve_rows(padded, weights, out_rows, out_cols):
    channels = padded.shape[2]
    summed = jnp.zeros((out_rows * out_cols, channels), jnp.float32)
    for row_shift in range(3):
        for col_shift in range(3):
            window = padded[row_shift : row_shift + out_rows, col_shift : col_shift + out_cols]
            window = window.reshape(out_rows * out_cols, channels)
            summed = summed + jnp.dot(
                window, weights[row_shift, col_shift], preferred_element_type=jnp.float32
            )
    return summed.reshape(out_rows, out_cols, channels)


def native_conv(rows, weights):
    out = lax.conv_general_dilated(
        rows[None],
        weights,
        window_strides=(1, 1),
        padding=((0, 0), (1, 1)),
        dimension_numbers=("NHWC", "HWIO", "NHWC"),
        preferred_element_type=jnp.float32,
    )
    return out[0]


def pad_columns(image):
    return jnp.pad(image, ((0, 0), (1, 1), (0, 0)))


def attend_kernel(owner_ref, count_ref, q_ref, k_ref, m_in, t_in, a_in, m_out, t_out, a_out, kall_ref, *, scale):
    t = pl.program_id(0)
    n = count_ref[t]
    slots = owner_ref.shape[1]
    span = k_ref.shape[1]
    lanes = 128
    for j in range(slots):
        kall_ref[j * span : (j + 1) * span, :] = k_ref[owner_ref[t, j]]
    q = q_ref[0]
    kall = kall_ref[...]
    s = lax.dot_general(q, kall, (((1,), (1,)), ((), ())), preferred_element_type=jnp.float32)
    penalty = [jnp.where(j < n, 0.0, jnp.inf).astype(jnp.float32) for j in range(slots)]
    blocks = [(j, j * span + c * lanes) for j in range(slots) for c in range(span // lanes)]
    mx = None
    for j, at in blocks:
        blk = s[:, at : at + lanes]
        mx = blk if mx is None else jnp.maximum(mx, blk)
    m_old = m_in[0]
    m_new = jnp.maximum(m_old, jnp.max(mx, axis=1, keepdims=True) * scale)
    alpha = jnp.exp(m_old - m_new)
    log2e = 1.4426950408889634
    mb = jnp.broadcast_to(m_new * log2e, (m_new.shape[0], lanes))
    shifted = [mb + penalty[j] for j in range(slots)]
    acc = None
    ps = []
    for j, at in blocks:
        p = jnp.exp2(s[:, at : at + lanes] * (scale * log2e) - shifted[j])
        acc = p if acc is None else acc + p
        ps.append(p.astype(jnp.bfloat16))
    pb = jnp.concatenate(ps, axis=1)
    m_out[0] = m_new
    a_out[0] = a_in[0] * alpha + jnp.dot(pb, kall, preferred_element_type=jnp.float32)
    t_out[0] = t_in[0] * alpha + jnp.sum(acc, axis=1, keepdims=True)


def attend_chunk(state, queries, chunk, slot_owner, counts, scale):
    tiles, tile_size, channels = queries.shape
    owners, chunk_len, _ = chunk.shape
    slots = slot_owner.shape[1]
    m, tot, acc = state
    col_spec = pl.BlockSpec((1, tile_size, 1), lambda t, o, c: (t, 0, 0))
    acc_spec = pl.BlockSpec((1, tile_size, channels), lambda t, o, c: (t, 0, 0))
    grid_spec = pltpu.PrefetchScalarGridSpec(
        num_scalar_prefetch=2,
        grid=(tiles,),
        in_specs=[
            acc_spec,
            pl.BlockSpec((owners, chunk_len, channels), lambda t, o, c: (0, 0, 0)),
            col_spec,
            col_spec,
            acc_spec,
        ],
        out_specs=[col_spec, col_spec, acc_spec],
        scratch_shapes=[pltpu.VMEM((slots * chunk_len, channels), jnp.bfloat16)],
    )
    return pl.pallas_call(
        functools.partial(attend_kernel, scale=scale),
        grid_spec=grid_spec,
        out_shape=[
            jax.ShapeDtypeStruct(m.shape, jnp.float32),
            jax.ShapeDtypeStruct(tot.shape, jnp.float32),
            jax.ShapeDtypeStruct(acc.shape, jnp.float32),
        ],
        input_output_aliases={4: 0, 5: 1, 6: 2},
        compiler_params=pltpu.CompilerParams(vmem_limit_bytes=48 * 1024 * 1024),
    )(slot_owner, counts, queries, chunk, m, tot, acc)


def on_device(frame_one, frame_two, tile_lists, conv_one, conv_two):
    band_rows, band_width, channels = frame_one.shape
    per_device = tile_lists.shape[0]
    tile_cols = band_width // per_device
    tile_size = band_rows * tile_cols
    owners = lax.axis_size("row")
    scale = float(channels) ** (-0.5)

    def band_to_tiles(band):
        return (
            band.reshape(band_rows, per_device, tile_cols, channels)
            .transpose(1, 0, 2, 3)
            .reshape(per_device, tile_size, channels)
        )

    query_tiles = band_to_tiles(frame_one)
    own_keys = band_to_tiles(frame_two)
    valid = tile_lists >= 0
    slot_owner = jnp.maximum(jnp.where(valid, tile_lists, tile_lists[:, :1]), 0) // per_device
    counts = jnp.sum(valid.astype(jnp.int32), axis=1)
    owner_iota = jnp.arange(owners, dtype=jnp.int32)
    matches = (slot_owner[:, :, None] == owner_iota[None, None, :]) & valid[:, :, None]
    wanted = jnp.max(jnp.where(matches, (tile_lists % per_device)[:, :, None], -1), axis=(0, 1))
    asked = lax.all_to_all(
        wanted.reshape(owners, 1), "row", split_axis=0, concat_axis=0, tiled=True
    )[:, 0]
    picked = jnp.take(own_keys, jnp.maximum(asked, 0), axis=0)
    outgoing = jnp.where((asked >= 0)[:, None, None], picked, jnp.zeros_like(picked))
    pieces = 2
    chunk_len = tile_size // pieces
    state = (
        jnp.full((per_device, tile_size, 1), -jnp.inf, jnp.float32),
        jnp.zeros((per_device, tile_size, 1), jnp.float32),
        jnp.zeros((per_device, tile_size, channels), jnp.float32),
    )
    previous = None
    for piece in range(pieces):
        sending = outgoing[:, piece * chunk_len : (piece + 1) * chunk_len]
        if previous is not None:
            previous, sending, state = lax.optimization_barrier((previous, sending, state))
        current = lax.all_to_all(sending, "row", split_axis=0, concat_axis=0, tiled=True)
        if previous is not None:
            state = attend_chunk(state, query_tiles, previous, slot_owner, counts, scale)
        previous = current
    state = attend_chunk(state, query_tiles, previous, slot_owner, counts, scale)
    warped_tiles = (state[2] / state[1]).astype(jnp.bfloat16)
    warped = (
        warped_tiles.reshape(per_device, band_rows, tile_cols, channels)
        .transpose(1, 0, 2, 3)
        .reshape(band_rows, band_width, channels)
    )
    me = lax.axis_index("row")
    extended = halo_rows(warped, "row", 2)
    hidden = jax.nn.relu(native_conv(extended, conv_one)).astype(jnp.bfloat16)
    row_ids = jnp.arange(band_rows + 2)
    inside = ((row_ids > 0) | (me > 0)) & ((row_ids < band_rows + 1) | (me < owners - 1))
    hidden = jnp.where(inside[:, None, None], hidden, jnp.zeros_like(hidden))
    branch = native_conv(hidden, conv_two)
    return (frame_one.astype(jnp.float32) + branch).astype(jnp.bfloat16)


def solution(mesh):
    in_specs = (
        P(("pairs", "row"), None, None),
        P(("pairs", "row"), None, None),
        P(("pairs", "row"), None),
        P(),
        P(),
    )
    out_specs = P(("pairs", "row"), None, None)
    return jax.shard_map(
        on_device, mesh=mesh, in_specs=in_specs, out_specs=out_specs, check_vma=False
    )
```

```python
import functools

import jax
import jax.numpy as jnp
from jax import lax
from jax.experimental import pallas as pl
from jax.experimental.pallas import tpu as pltpu
from jax.sharding import PartitionSpec as P


def halo_rows(cells, axis, width):
    count = lax.axis_size(axis)
    ends = count - 1
    head = cells[:width]
    tail = cells[cells.shape[0] - width :]
    from_above = lax.ppermute(tail, axis, [(i, i + 1) for i in range(ends)])
    from_below = lax.ppermute(head, axis, [(i + 1, i) for i in range(ends)])
    return jnp.concatenate([from_above, cells, from_below], axis=0)


def convolve_rows(padded, weights, out_rows, out_cols):
    channels = padded.shape[2]
    summed = jnp.zeros((out_rows * out_cols, channels), jnp.float32)
    for row_shift in range(3):
        for col_shift in range(3):
            window = padded[row_shift : row_shift + out_rows, col_shift : col_shift + out_cols]
            window = window.reshape(out_rows * out_cols, channels)
            summed = summed + jnp.dot(
                window, weights[row_shift, col_shift], preferred_element_type=jnp.float32
            )
    return summed.reshape(out_rows, out_cols, channels)


def native_conv(rows, weights):
    out = lax.conv_general_dilated(
        rows[None],
        weights,
        window_strides=(1, 1),
        padding=((0, 0), (1, 1)),
        dimension_numbers=("NHWC", "HWIO", "NHWC"),
        preferred_element_type=jnp.float32,
    )
    return out[0]


def pad_columns(image):
    return jnp.pad(image, ((0, 0), (1, 1), (0, 0)))


def attend_kernel(owner_ref, count_ref, q_ref, k_ref, *refs, scale, first, last):
    if first:
        m_out, t_out, a_out, kall_ref = refs
    elif last:
        m_in, t_in, a_in, o_ref, kall_ref = refs
    else:
        m_in, t_in, a_in, m_out, t_out, a_out, kall_ref = refs
    t = pl.program_id(0)
    n = count_ref[t]
    slots = owner_ref.shape[1]
    span = k_ref.shape[1]
    lanes = 128
    for j in range(slots):
        kall_ref[j * span : (j + 1) * span, :] = k_ref[owner_ref[t, j]]
    q = q_ref[0]
    kall = kall_ref[...]
    s = lax.dot_general(q, kall, (((1,), (1,)), ((), ())), preferred_element_type=jnp.float32)
    penalty = [jnp.where(j < n, 0.0, jnp.inf).astype(jnp.float32) for j in range(slots)]
    blocks = [(j, j * span + c * lanes) for j in range(slots) for c in range(span // lanes)]
    mx = None
    for j, at in blocks:
        blk = s[:, at : at + lanes]
        mx = blk if mx is None else jnp.maximum(mx, blk)
    m_new = jnp.max(mx, axis=1, keepdims=True) * scale
    if not first:
        m_old = m_in[0]
        m_new = jnp.maximum(m_old, m_new)
        alpha = jnp.exp(m_old - m_new)
    log2e = 1.4426950408889634
    mb = jnp.broadcast_to(m_new * log2e, (m_new.shape[0], lanes))
    shifted = [mb + penalty[j] for j in range(slots)]
    acc = None
    ps = []
    for j, at in blocks:
        p = jnp.exp2(s[:, at : at + lanes] * (scale * log2e) - shifted[j])
        acc = p if acc is None else acc + p
        ps.append(p.astype(jnp.bfloat16))
    pb = jnp.concatenate(ps, axis=1)
    mixed = jnp.dot(pb, kall, preferred_element_type=jnp.float32)
    total = jnp.sum(acc, axis=1, keepdims=True)
    if not first:
        mixed = a_in[0] * alpha + mixed
        total = t_in[0] * alpha + total
    if last:
        o_ref[0] = (mixed / total).astype(o_ref.dtype)
    else:
        m_out[0] = m_new
        t_out[0] = total
        a_out[0] = mixed


def attend_chunk(state, queries, chunk, slot_owner, counts, scale, first, last):
    tiles, tile_size, channels = queries.shape
    owners, chunk_len, _ = chunk.shape
    slots = slot_owner.shape[1]
    col_spec = pl.BlockSpec((1, tile_size, 1), lambda t, o, c: (t, 0, 0))
    acc_spec = pl.BlockSpec((1, tile_size, channels), lambda t, o, c: (t, 0, 0))
    state_specs = [] if first else [col_spec, col_spec, acc_spec]
    if last:
        out_specs = acc_spec
        out_shape = jax.ShapeDtypeStruct(queries.shape, jnp.bfloat16)
    else:
        out_specs = [col_spec, col_spec, acc_spec]
        out_shape = [
            jax.ShapeDtypeStruct((tiles, tile_size, 1), jnp.float32),
            jax.ShapeDtypeStruct((tiles, tile_size, 1), jnp.float32),
            jax.ShapeDtypeStruct((tiles, tile_size, channels), jnp.float32),
        ]
    grid_spec = pltpu.PrefetchScalarGridSpec(
        num_scalar_prefetch=2,
        grid=(tiles,),
        in_specs=[
            acc_spec,
            pl.BlockSpec((owners, chunk_len, channels), lambda t, o, c: (0, 0, 0)),
        ]
        + state_specs,
        out_specs=out_specs,
        scratch_shapes=[pltpu.VMEM((slots * chunk_len, channels), jnp.bfloat16)],
    )
    return pl.pallas_call(
        functools.partial(attend_kernel, scale=scale, first=first, last=last),
        grid_spec=grid_spec,
        out_shape=out_shape,
        compiler_params=pltpu.CompilerParams(vmem_limit_bytes=48 * 1024 * 1024),
    )(slot_owner, counts, queries, chunk, *([] if first else state))


def on_device(frame_one, frame_two, tile_lists, conv_one, conv_two):
    band_rows, band_width, channels = frame_one.shape
    per_device = tile_lists.shape[0]
    tile_cols = band_width // per_device
    tile_size = band_rows * tile_cols
    owners = lax.axis_size("row")
    scale = float(channels) ** (-0.5)

    def band_to_tiles(band):
        return (
            band.reshape(band_rows, per_device, tile_cols, channels)
            .transpose(1, 0, 2, 3)
            .reshape(per_device, tile_size, channels)
        )

    query_tiles = band_to_tiles(frame_one)
    own_keys = band_to_tiles(frame_two)
    valid = tile_lists >= 0
    slot_owner = jnp.maximum(jnp.where(valid, tile_lists, tile_lists[:, :1]), 0) // per_device
    counts = jnp.sum(valid.astype(jnp.int32), axis=1)
    owner_iota = jnp.arange(owners, dtype=jnp.int32)
    matches = (slot_owner[:, :, None] == owner_iota[None, None, :]) & valid[:, :, None]
    wanted = jnp.max(jnp.where(matches, (tile_lists % per_device)[:, :, None], -1), axis=(0, 1))
    asked = lax.all_to_all(
        wanted.reshape(owners, 1), "row", split_axis=0, concat_axis=0, tiled=True
    )[:, 0]
    outgoing = jnp.take(own_keys, jnp.maximum(asked, 0), axis=0)
    edges = [0, tile_size // 2, tile_size]
    state = ()
    previous = None
    for index, (start, stop) in enumerate(zip(edges[:-1], edges[1:])):
        sending = outgoing[:, start:stop]
        if previous is not None:
            previous, sending, state = lax.optimization_barrier((previous, sending, state))
        current = lax.all_to_all(sending, "row", split_axis=0, concat_axis=0, tiled=True)
        if previous is not None:
            state = attend_chunk(state, query_tiles, previous, slot_owner, counts, scale, index == 1, False)
        previous = current
    warped_tiles = attend_chunk(
        state, query_tiles, previous, slot_owner, counts, scale, len(edges) == 2, True
    )
    warped = (
        warped_tiles.reshape(per_device, band_rows, tile_cols, channels)
        .transpose(1, 0, 2, 3)
        .reshape(band_rows, band_width, channels)
    )
    me = lax.axis_index("row")
    extended = halo_rows(warped, "row", 2)
    hidden = jax.nn.relu(native_conv(extended, conv_one)).astype(jnp.bfloat16)
    row_ids = jnp.arange(band_rows + 2)
    inside = ((row_ids > 0) | (me > 0)) & ((row_ids < band_rows + 1) | (me < owners - 1))
    hidden = jnp.where(inside[:, None, None], hidden, jnp.zeros_like(hidden))
    branch = native_conv(hidden, conv_two)
    return (frame_one.astype(jnp.float32) + branch).astype(jnp.bfloat16)


def solution(mesh):
    in_specs = (
        P(("pairs", "row"), None, None),
        P(("pairs", "row"), None, None),
        P(("pairs", "row"), None),
        P(),
        P(),
    )
    out_specs = P(("pairs", "row"), None, None)
    return jax.shard_map(
        on_device, mesh=mesh, in_specs=in_specs, out_specs=out_specs, check_vma=False
    )
```

```python
import functools

import jax
import jax.numpy as jnp
from jax import lax
from jax.experimental import pallas as pl
from jax.experimental.pallas import tpu as pltpu
from jax.sharding import PartitionSpec as P


def halo_rows(cells, axis, width):
    count = lax.axis_size(axis)
    ends = count - 1
    head = cells[:width]
    tail = cells[cells.shape[0] - width :]
    from_above = lax.ppermute(tail, axis, [(i, i + 1) for i in range(ends)])
    from_below = lax.ppermute(head, axis, [(i + 1, i) for i in range(ends)])
    return jnp.concatenate([from_above, cells, from_below], axis=0)


def convolve_rows(padded, weights, out_rows, out_cols):
    channels = padded.shape[2]
    summed = jnp.zeros((out_rows * out_cols, channels), jnp.float32)
    for row_shift in range(3):
        for col_shift in range(3):
            window = padded[row_shift : row_shift + out_rows, col_shift : col_shift + out_cols]
            window = window.reshape(out_rows * out_cols, channels)
            summed = summed + jnp.dot(
                window, weights[row_shift, col_shift], preferred_element_type=jnp.float32
            )
    return summed.reshape(out_rows, out_cols, channels)


def native_conv(rows, weights):
    out = lax.conv_general_dilated(
        rows[None],
        weights,
        window_strides=(1, 1),
        padding=((0, 0), (1, 1)),
        dimension_numbers=("NHWC", "HWIO", "NHWC"),
        preferred_element_type=jnp.float32,
    )
    return out[0]


def pad_columns(image):
    return jnp.pad(image, ((0, 0), (1, 1), (0, 0)))


def attend_kernel(owner_ref, count_ref, q_ref, k_ref, *refs, scale, first, last):
    if first:
        m_out, t_out, a_out, kall_ref = refs
    elif last:
        m_in, t_in, a_in, o_ref, kall_ref = refs
    else:
        m_in, t_in, a_in, m_out, t_out, a_out, kall_ref = refs
    t = pl.program_id(0)
    n = count_ref[t]
    slots = owner_ref.shape[1]
    span = k_ref.shape[1]
    lanes = 128
    for j in range(slots):
        kall_ref[j * span : (j + 1) * span, :] = k_ref[owner_ref[t, j]]
    q = q_ref[0]
    kall = kall_ref[...]
    s = lax.dot_general(q, kall, (((1,), (1,)), ((), ())), preferred_element_type=jnp.float32)
    penalty = [jnp.where(j < n, 0.0, jnp.inf).astype(jnp.float32) for j in range(slots)]
    blocks = [(j, j * span + c * lanes) for j in range(slots) for c in range(span // lanes)]
    mx = None
    for j, at in blocks:
        blk = s[:, at : at + lanes]
        mx = blk if mx is None else jnp.maximum(mx, blk)
    rows = q.shape[0]

    def column(row, width):
        return jnp.broadcast_to(row, (width, rows)).T

    m_new = jnp.max(mx.T, axis=0, keepdims=True) * scale
    if not first:
        m_old = m_in[0]
        m_new = jnp.maximum(m_old, m_new)
        alpha = jnp.exp(m_old - m_new)
    log2e = 1.4426950408889634
    mb = column(m_new * log2e, lanes)
    shifted = [mb + penalty[j] for j in range(slots)]
    acc = None
    ps = []
    for j, at in blocks:
        p = jnp.exp2(s[:, at : at + lanes] * (scale * log2e) - shifted[j])
        acc = p if acc is None else acc + p
        ps.append(p.astype(jnp.bfloat16))
    pb = jnp.concatenate(ps, axis=1)
    mixed = jnp.dot(pb, kall, preferred_element_type=jnp.float32)
    total = jnp.sum(acc.T, axis=0, keepdims=True)
    width = mixed.shape[1]
    if not first:
        mixed = a_in[0] * column(alpha, width) + mixed
        total = t_in[0] * alpha + total
    if last:
        o_ref[0] = (mixed / column(total, width)).astype(o_ref.dtype)
    else:
        m_out[0] = m_new
        t_out[0] = total
        a_out[0] = mixed


def attend_chunk(state, queries, chunk, slot_owner, counts, scale, first, last):
    tiles, tile_size, channels = queries.shape
    owners, chunk_len, _ = chunk.shape
    slots = slot_owner.shape[1]
    col_spec = pl.BlockSpec((1, 1, tile_size), lambda t, o, c: (t, 0, 0))
    acc_spec = pl.BlockSpec((1, tile_size, channels), lambda t, o, c: (t, 0, 0))
    state_specs = [] if first else [col_spec, col_spec, acc_spec]
    if last:
        out_specs = acc_spec
        out_shape = jax.ShapeDtypeStruct(queries.shape, jnp.bfloat16)
    else:
        out_specs = [col_spec, col_spec, acc_spec]
        out_shape = [
            jax.ShapeDtypeStruct((tiles, 1, tile_size), jnp.float32),
            jax.ShapeDtypeStruct((tiles, 1, tile_size), jnp.float32),
            jax.ShapeDtypeStruct((tiles, tile_size, channels), jnp.float32),
        ]
    grid_spec = pltpu.PrefetchScalarGridSpec(
        num_scalar_prefetch=2,
        grid=(tiles,),
        in_specs=[
            acc_spec,
            pl.BlockSpec((owners, chunk_len, channels), lambda t, o, c: (0, 0, 0)),
        ]
        + state_specs,
        out_specs=out_specs,
        scratch_shapes=[pltpu.VMEM((slots * chunk_len, channels), jnp.bfloat16)],
    )
    return pl.pallas_call(
        functools.partial(attend_kernel, scale=scale, first=first, last=last),
        grid_spec=grid_spec,
        out_shape=out_shape,
        compiler_params=pltpu.CompilerParams(vmem_limit_bytes=48 * 1024 * 1024),
    )(slot_owner, counts, queries, chunk, *([] if first else state))


def on_device(frame_one, frame_two, tile_lists, conv_one, conv_two):
    band_rows, band_width, channels = frame_one.shape
    per_device = tile_lists.shape[0]
    tile_cols = band_width // per_device
    tile_size = band_rows * tile_cols
    owners = lax.axis_size("row")
    scale = float(channels) ** (-0.5)

    def band_to_tiles(band):
        return (
            band.reshape(band_rows, per_device, tile_cols, channels)
            .transpose(1, 0, 2, 3)
            .reshape(per_device, tile_size, channels)
        )

    query_tiles = band_to_tiles(frame_one)
    own_keys = band_to_tiles(frame_two)
    valid = tile_lists >= 0
    slot_owner = jnp.maximum(jnp.where(valid, tile_lists, tile_lists[:, :1]), 0) // per_device
    counts = jnp.sum(valid.astype(jnp.int32), axis=1)
    owner_iota = jnp.arange(owners, dtype=jnp.int32)
    matches = (slot_owner[:, :, None] == owner_iota[None, None, :]) & valid[:, :, None]
    wanted = jnp.max(jnp.where(matches, (tile_lists % per_device)[:, :, None], -1), axis=(0, 1))
    asked = lax.all_to_all(
        wanted.reshape(owners, 1), "row", split_axis=0, concat_axis=0, tiled=True
    )[:, 0]
    outgoing = jnp.take(own_keys, jnp.maximum(asked, 0), axis=0)
    edges = [0, tile_size // 2, tile_size]
    state = ()
    previous = None
    for index, (start, stop) in enumerate(zip(edges[:-1], edges[1:])):
        sending = outgoing[:, start:stop]
        if previous is not None:
            previous, sending, state = lax.optimization_barrier((previous, sending, state))
        current = lax.all_to_all(sending, "row", split_axis=0, concat_axis=0, tiled=True)
        if previous is not None:
            state = attend_chunk(state, query_tiles, previous, slot_owner, counts, scale, index == 1, False)
        previous = current
    warped_tiles = attend_chunk(
        state, query_tiles, previous, slot_owner, counts, scale, len(edges) == 2, True
    )
    warped = (
        warped_tiles.reshape(per_device, band_rows, tile_cols, channels)
        .transpose(1, 0, 2, 3)
        .reshape(band_rows, band_width, channels)
    )
    me = lax.axis_index("row")
    extended = halo_rows(warped, "row", 2)
    hidden = jax.nn.relu(native_conv(extended, conv_one)).astype(jnp.bfloat16)
    row_ids = jnp.arange(band_rows + 2)
    inside = ((row_ids > 0) | (me > 0)) & ((row_ids < band_rows + 1) | (me < owners - 1))
    hidden = jnp.where(inside[:, None, None], hidden, jnp.zeros_like(hidden))
    branch = native_conv(hidden, conv_two)
    return (frame_one.astype(jnp.float32) + branch).astype(jnp.bfloat16)


def solution(mesh):
    in_specs = (
        P(("pairs", "row"), None, None),
        P(("pairs", "row"), None, None),
        P(("pairs", "row"), None),
        P(),
        P(),
    )
    out_specs = P(("pairs", "row"), None, None)
    return jax.shard_map(
        on_device, mesh=mesh, in_specs=in_specs, out_specs=out_specs, check_vma=False
    )
```

```python
import functools

import jax
import jax.numpy as jnp
from jax import lax
from jax.experimental import pallas as pl
from jax.experimental.pallas import tpu as pltpu
from jax.sharding import PartitionSpec as P


def halo_rows(cells, axis, width):
    count = lax.axis_size(axis)
    ends = count - 1
    head = cells[:width]
    tail = cells[cells.shape[0] - width :]
    from_above = lax.ppermute(tail, axis, [(i, i + 1) for i in range(ends)])
    from_below = lax.ppermute(head, axis, [(i + 1, i) for i in range(ends)])
    return jnp.concatenate([from_above, cells, from_below], axis=0)


def convolve_rows(padded, weights, out_rows, out_cols):
    channels = padded.shape[2]
    summed = jnp.zeros((out_rows * out_cols, channels), jnp.float32)
    for row_shift in range(3):
        for col_shift in range(3):
            window = padded[row_shift : row_shift + out_rows, col_shift : col_shift + out_cols]
            window = window.reshape(out_rows * out_cols, channels)
            summed = summed + jnp.dot(
                window, weights[row_shift, col_shift], preferred_element_type=jnp.float32
            )
    return summed.reshape(out_rows, out_cols, channels)


def native_conv(rows, weights):
    out = lax.conv_general_dilated(
        rows[None],
        weights,
        window_strides=(1, 1),
        padding=((0, 0), (1, 1)),
        dimension_numbers=("NHWC", "HWIO", "NHWC"),
        preferred_element_type=jnp.float32,
    )
    return out[0]


def pad_columns(image):
    return jnp.pad(image, ((0, 0), (1, 1), (0, 0)))


def attend_kernel(owner_ref, count_ref, q_ref, k_ref, *refs, scale, first, last):
    if first:
        m_out, t_out, a_out, kall_ref = refs
    elif last:
        m_in, t_in, a_in, o_ref, kall_ref = refs
    else:
        m_in, t_in, a_in, m_out, t_out, a_out, kall_ref = refs
    t = pl.program_id(0)
    n = count_ref[t]
    slots = owner_ref.shape[1]
    span = k_ref.shape[1]
    lanes = 128
    for j in range(slots):
        kall_ref[j * span : (j + 1) * span, :] = k_ref[owner_ref[t, j]]
    q = q_ref[0]
    kall = kall_ref[...]
    s = lax.dot_general(q, kall, (((1,), (1,)), ((), ())), preferred_element_type=jnp.float32)
    penalty = [jnp.where(j < n, 0.0, jnp.inf).astype(jnp.float32) for j in range(slots)]
    blocks = [(j, j * span + c * lanes) for j in range(slots) for c in range(span // lanes)]
    mx = None
    for j, at in blocks:
        blk = s[:, at : at + lanes]
        mx = blk if mx is None else jnp.maximum(mx, blk)
    rows = q.shape[0]

    def column(row, width):
        return jnp.broadcast_to(row, (width, rows)).T

    m_new = jnp.max(mx.T, axis=0, keepdims=True) * scale
    if not first:
        m_old = m_in[0]
        m_new = jnp.maximum(m_old, m_new)
        alpha = jnp.exp(m_old - m_new)
    log2e = 1.4426950408889634
    mb = column(m_new * log2e, lanes)
    shifted = [mb + penalty[j] for j in range(slots)]
    acc = None
    ps = []
    for j, at in blocks:
        p = jnp.exp2(s[:, at : at + lanes] * (scale * log2e) - shifted[j])
        acc = p if acc is None else acc + p
        ps.append(p.astype(jnp.bfloat16))
    pb = jnp.concatenate(ps, axis=1)
    mixed = jnp.dot(pb, kall, preferred_element_type=jnp.float32)
    total = jnp.sum(acc.T, axis=0, keepdims=True)
    width = mixed.shape[1]
    if not first:
        mixed = a_in[0] * column(alpha, width) + mixed
        total = t_in[0] * alpha + total
    if last:
        o_ref[0] = (mixed / column(total, width)).astype(o_ref.dtype)
    else:
        m_out[0] = m_new
        t_out[0] = total
        a_out[0] = mixed


def attend_chunk(state, queries, chunk, slot_owner, counts, scale, first, last):
    tiles, tile_size, channels = queries.shape
    owners, chunk_len, _ = chunk.shape
    slots = slot_owner.shape[1]
    col_spec = pl.BlockSpec((1, 1, tile_size), lambda t, o, c: (t, 0, 0))
    acc_spec = pl.BlockSpec((1, tile_size, channels), lambda t, o, c: (t, 0, 0))
    state_specs = [] if first else [col_spec, col_spec, acc_spec]
    if last:
        out_specs = acc_spec
        out_shape = jax.ShapeDtypeStruct(queries.shape, jnp.bfloat16)
    else:
        out_specs = [col_spec, col_spec, acc_spec]
        out_shape = [
            jax.ShapeDtypeStruct((tiles, 1, tile_size), jnp.float32),
            jax.ShapeDtypeStruct((tiles, 1, tile_size), jnp.float32),
            jax.ShapeDtypeStruct((tiles, tile_size, channels), jnp.float32),
        ]
    grid_spec = pltpu.PrefetchScalarGridSpec(
        num_scalar_prefetch=2,
        grid=(tiles,),
        in_specs=[
            acc_spec,
            pl.BlockSpec((owners, chunk_len, channels), lambda t, o, c: (0, 0, 0)),
        ]
        + state_specs,
        out_specs=out_specs,
        scratch_shapes=[pltpu.VMEM((slots * chunk_len, channels), jnp.bfloat16)],
    )
    return pl.pallas_call(
        functools.partial(attend_kernel, scale=scale, first=first, last=last),
        grid_spec=grid_spec,
        out_shape=out_shape,
        compiler_params=pltpu.CompilerParams(vmem_limit_bytes=48 * 1024 * 1024),
    )(slot_owner, counts, queries, chunk, *([] if first else state))


def on_device(frame_one, frame_two, tile_lists, conv_one, conv_two):
    band_rows, band_width, channels = frame_one.shape
    per_device = tile_lists.shape[0]
    tile_cols = band_width // per_device
    tile_size = band_rows * tile_cols
    owners = lax.axis_size("row")
    scale = float(channels) ** (-0.5)

    def band_to_tiles(band):
        return (
            band.reshape(band_rows, per_device, tile_cols, channels)
            .transpose(1, 0, 2, 3)
            .reshape(per_device, tile_size, channels)
        )

    query_tiles = band_to_tiles(frame_one)
    own_keys = band_to_tiles(frame_two)
    valid = tile_lists >= 0
    slot_owner = jnp.maximum(jnp.where(valid, tile_lists, tile_lists[:, :1]), 0) // per_device
    counts = jnp.sum(valid.astype(jnp.int32), axis=1)
    me = lax.axis_index("row")
    lists_everywhere = jnp.broadcast_to(tile_lists[None], (owners,) + tile_lists.shape)
    lists_of = lax.all_to_all(lists_everywhere, "row", split_axis=0, concat_axis=0, tiled=True)
    mine = (lists_of >= 0) & (lists_of // per_device == me)
    asked = jnp.max(jnp.where(mine, lists_of % per_device, 0), axis=(1, 2))
    outgoing = jnp.take(own_keys, asked, axis=0)
    edges = [0, tile_size // 2, tile_size]
    state = ()
    previous = None
    for index, (start, stop) in enumerate(zip(edges[:-1], edges[1:])):
        sending = outgoing[:, start:stop]
        if previous is not None:
            previous, sending, state = lax.optimization_barrier((previous, sending, state))
        current = lax.all_to_all(sending, "row", split_axis=0, concat_axis=0, tiled=True)
        if previous is not None:
            state = attend_chunk(state, query_tiles, previous, slot_owner, counts, scale, index == 1, False)
        previous = current
    warped_tiles = attend_chunk(
        state, query_tiles, previous, slot_owner, counts, scale, len(edges) == 2, True
    )
    warped = (
        warped_tiles.reshape(per_device, band_rows, tile_cols, channels)
        .transpose(1, 0, 2, 3)
        .reshape(band_rows, band_width, channels)
    )
    extended = halo_rows(warped, "row", 2)
    hidden = jax.nn.relu(native_conv(extended, conv_one)).astype(jnp.bfloat16)
    row_ids = jnp.arange(band_rows + 2)
    inside = ((row_ids > 0) | (me > 0)) & ((row_ids < band_rows + 1) | (me < owners - 1))
    hidden = jnp.where(inside[:, None, None], hidden, jnp.zeros_like(hidden))
    branch = native_conv(hidden, conv_two)
    return (frame_one.astype(jnp.float32) + branch).astype(jnp.bfloat16)


def solution(mesh):
    in_specs = (
        P(("pairs", "row"), None, None),
        P(("pairs", "row"), None, None),
        P(("pairs", "row"), None),
        P(),
        P(),
    )
    out_specs = P(("pairs", "row"), None, None)
    return jax.shard_map(
        on_device, mesh=mesh, in_specs=in_specs, out_specs=out_specs, check_vma=False
    )
```

```python
import functools

import jax
import jax.numpy as jnp
from jax import lax
from jax.experimental import pallas as pl
from jax.experimental.pallas import tpu as pltpu
from jax.sharding import PartitionSpec as P


def halo_rows(cells, axis, width):
    count = lax.axis_size(axis)
    ends = count - 1
    head = cells[:width]
    tail = cells[cells.shape[0] - width :]
    from_above = lax.ppermute(tail, axis, [(i, i + 1) for i in range(ends)])
    from_below = lax.ppermute(head, axis, [(i + 1, i) for i in range(ends)])
    return jnp.concatenate([from_above, cells, from_below], axis=0)


def convolve_rows(padded, weights, out_rows, out_cols):
    channels = padded.shape[2]
    summed = jnp.zeros((out_rows * out_cols, channels), jnp.float32)
    for row_shift in range(3):
        for col_shift in range(3):
            window = padded[row_shift : row_shift + out_rows, col_shift : col_shift + out_cols]
            window = window.reshape(out_rows * out_cols, channels)
            summed = summed + jnp.dot(
                window, weights[row_shift, col_shift], preferred_element_type=jnp.float32
            )
    return summed.reshape(out_rows, out_cols, channels)


def native_conv(rows, weights):
    out = lax.conv_general_dilated(
        rows[None],
        weights,
        window_strides=(1, 1),
        padding=((0, 0), (1, 1)),
        dimension_numbers=("NHWC", "HWIO", "NHWC"),
        preferred_element_type=jnp.float32,
    )
    return out[0]


def pad_columns(image):
    return jnp.pad(image, ((0, 0), (1, 1), (0, 0)))


def attend_kernel(owner_ref, count_ref, q_ref, k_ref, *refs, scale, first, last):
    if first:
        m_out, t_out, a_out, kall_ref = refs
    elif last:
        m_in, t_in, a_in, o_ref, kall_ref = refs
    else:
        m_in, t_in, a_in, m_out, t_out, a_out, kall_ref = refs
    t = pl.program_id(0)
    n = count_ref[t]
    slots = owner_ref.shape[1]
    span = k_ref.shape[1]
    lanes = 128
    for j in range(slots):
        kall_ref[j * span : (j + 1) * span, :] = k_ref[owner_ref[t, j]]
    q = q_ref[0]
    kall = kall_ref[...]
    s = lax.dot_general(q, kall, (((1,), (1,)), ((), ())), preferred_element_type=jnp.float32)
    penalty = [jnp.where(j < n, 0.0, jnp.inf).astype(jnp.float32) for j in range(slots)]
    blocks = [(j, j * span + c * lanes) for j in range(slots) for c in range(span // lanes)]
    mx = None
    for j, at in blocks:
        blk = s[:, at : at + lanes]
        mx = blk if mx is None else jnp.maximum(mx, blk)
    rows = q.shape[0]

    def column(row, width):
        return jnp.broadcast_to(row, (width, rows)).T

    m_new = jnp.max(mx.T, axis=0, keepdims=True) * scale
    if not first:
        m_old = m_in[0]
        m_new = jnp.maximum(m_old, m_new)
        alpha = jnp.exp(m_old - m_new)
    log2e = 1.4426950408889634
    mb = column(m_new * log2e, lanes)
    shifted = [mb + penalty[j] for j in range(slots)]
    acc = None
    ps = []
    for j, at in blocks:
        p = jnp.exp2(s[:, at : at + lanes] * (scale * log2e) - shifted[j])
        acc = p if acc is None else acc + p
        ps.append(p.astype(jnp.bfloat16))
    pb = jnp.concatenate(ps, axis=1)
    mixed = jnp.dot(pb, kall, preferred_element_type=jnp.float32)
    total = jnp.sum(acc.T, axis=0, keepdims=True)
    width = mixed.shape[1]
    if not first:
        mixed = a_in[0] * column(alpha, width) + mixed
        total = t_in[0] * alpha + total
    if last:
        o_ref[0] = (mixed / column(total, width)).astype(o_ref.dtype)
    else:
        m_out[0] = m_new
        t_out[0] = total
        a_out[0] = mixed


def attend_chunk(state, queries, chunk, slot_owner, counts, scale, first, last):
    tiles, tile_size, channels = queries.shape
    owners, chunk_len, _ = chunk.shape
    slots = slot_owner.shape[1]
    col_spec = pl.BlockSpec((1, 1, tile_size), lambda t, o, c: (t, 0, 0))
    acc_spec = pl.BlockSpec((1, tile_size, channels), lambda t, o, c: (t, 0, 0))
    state_specs = [] if first else [col_spec, col_spec, acc_spec]
    if last:
        out_specs = acc_spec
        out_shape = jax.ShapeDtypeStruct(queries.shape, jnp.bfloat16)
    else:
        out_specs = [col_spec, col_spec, acc_spec]
        out_shape = [
            jax.ShapeDtypeStruct((tiles, 1, tile_size), jnp.float32),
            jax.ShapeDtypeStruct((tiles, 1, tile_size), jnp.float32),
            jax.ShapeDtypeStruct((tiles, tile_size, channels), jnp.float32),
        ]
    grid_spec = pltpu.PrefetchScalarGridSpec(
        num_scalar_prefetch=2,
        grid=(tiles,),
        in_specs=[
            acc_spec,
            pl.BlockSpec((owners, chunk_len, channels), lambda t, o, c: (0, 0, 0)),
        ]
        + state_specs,
        out_specs=out_specs,
        scratch_shapes=[pltpu.VMEM((slots * chunk_len, channels), jnp.bfloat16)],
    )
    return pl.pallas_call(
        functools.partial(attend_kernel, scale=scale, first=first, last=last),
        grid_spec=grid_spec,
        out_shape=out_shape,
        compiler_params=pltpu.CompilerParams(vmem_limit_bytes=48 * 1024 * 1024),
    )(slot_owner, counts, queries, chunk, *([] if first else state))


def on_device(frame_one, frame_two, tile_lists, conv_one, conv_two):
    band_rows, band_width, channels = frame_one.shape
    per_device = tile_lists.shape[0]
    tile_cols = band_width // per_device
    tile_size = band_rows * tile_cols
    owners = lax.axis_size("row")
    scale = float(channels) ** (-0.5)

    def band_to_tiles(band):
        return (
            band.reshape(band_rows, per_device, tile_cols, channels)
            .transpose(1, 0, 2, 3)
            .reshape(per_device, tile_size, channels)
        )

    query_tiles = band_to_tiles(frame_one)
    own_keys = band_to_tiles(frame_two)
    valid = tile_lists >= 0
    slot_owner = jnp.maximum(jnp.where(valid, tile_lists, tile_lists[:, :1]), 0) // per_device
    counts = jnp.sum(valid.astype(jnp.int32), axis=1)
    me = lax.axis_index("row")
    flat_lists = tile_lists.reshape(1, -1)
    lists_everywhere = jnp.broadcast_to(flat_lists, (owners, flat_lists.shape[1]))
    lists_of = lax.all_to_all(lists_everywhere, "row", split_axis=0, concat_axis=0, tiled=True)
    mine = (lists_of >= 0) & (lists_of // per_device == me)
    asked = jnp.max(jnp.where(mine, lists_of % per_device, 0), axis=1)
    outgoing = jnp.take(own_keys, asked, axis=0)
    edges = [0, tile_size // 2, tile_size]
    state = ()
    previous = None
    for index, (start, stop) in enumerate(zip(edges[:-1], edges[1:])):
        sending = outgoing[:, start:stop]
        if previous is not None:
            previous, sending, state = lax.optimization_barrier((previous, sending, state))
        current = lax.all_to_all(sending, "row", split_axis=0, concat_axis=0, tiled=True)
        if previous is not None:
            state = attend_chunk(state, query_tiles, previous, slot_owner, counts, scale, index == 1, False)
        previous = current
    warped_tiles = attend_chunk(
        state, query_tiles, previous, slot_owner, counts, scale, len(edges) == 2, True
    )
    warped = (
        warped_tiles.reshape(per_device, band_rows, tile_cols, channels)
        .transpose(1, 0, 2, 3)
        .reshape(band_rows, band_width, channels)
    )
    extended = halo_rows(warped, "row", 2)
    hidden = jax.nn.relu(native_conv(extended, conv_one)).astype(jnp.bfloat16)
    row_ids = jnp.arange(band_rows + 2)
    inside = ((row_ids > 0) | (me > 0)) & ((row_ids < band_rows + 1) | (me < owners - 1))
    hidden = jnp.where(inside[:, None, None], hidden, jnp.zeros_like(hidden))
    branch = native_conv(hidden, conv_two)
    return (frame_one.astype(jnp.float32) + branch).astype(jnp.bfloat16)


def solution(mesh):
    in_specs = (
        P(("pairs", "row"), None, None),
        P(("pairs", "row"), None, None),
        P(("pairs", "row"), None),
        P(),
        P(),
    )
    out_specs = P(("pairs", "row"), None, None)
    return jax.shard_map(
        on_device, mesh=mesh, in_specs=in_specs, out_specs=out_specs, check_vma=False
    )
```

```python
import functools

import jax
import jax.numpy as jnp
from jax import lax
from jax.experimental import pallas as pl
from jax.experimental.pallas import tpu as pltpu
from jax.sharding import PartitionSpec as P


def halo_rows(cells, axis, width):
    count = lax.axis_size(axis)
    ends = count - 1
    head = cells[:width]
    tail = cells[cells.shape[0] - width :]
    from_above = lax.ppermute(tail, axis, [(i, i + 1) for i in range(ends)])
    from_below = lax.ppermute(head, axis, [(i + 1, i) for i in range(ends)])
    return jnp.concatenate([from_above, cells, from_below], axis=0)


def convolve_rows(padded, weights, out_rows, out_cols):
    channels = padded.shape[2]
    summed = jnp.zeros((out_rows * out_cols, channels), jnp.float32)
    for row_shift in range(3):
        for col_shift in range(3):
            window = padded[row_shift : row_shift + out_rows, col_shift : col_shift + out_cols]
            window = window.reshape(out_rows * out_cols, channels)
            summed = summed + jnp.dot(
                window, weights[row_shift, col_shift], preferred_element_type=jnp.float32
            )
    return summed.reshape(out_rows, out_cols, channels)


def native_conv(rows, weights):
    out = lax.conv_general_dilated(
        rows[None],
        weights,
        window_strides=(1, 1),
        padding=((0, 0), (1, 1)),
        dimension_numbers=("NHWC", "HWIO", "NHWC"),
        preferred_element_type=jnp.float32,
    )
    return out[0]


def pad_columns(image):
    return jnp.pad(image, ((0, 0), (1, 1), (0, 0)))


def attend_kernel(owner_ref, count_ref, q_ref, k_ref, *refs, scale, first, last):
    if first:
        m_out, t_out, a_out, kall_ref = refs
    elif last:
        m_in, t_in, a_in, o_ref, kall_ref = refs
    else:
        m_in, t_in, a_in, m_out, t_out, a_out, kall_ref = refs
    t = pl.program_id(0)
    n = count_ref[t]
    slots = owner_ref.shape[1]
    span = k_ref.shape[1]
    lanes = 128
    for j in range(slots):
        kall_ref[j * span : (j + 1) * span, :] = k_ref[owner_ref[t, j]]
    q = q_ref[0]
    kall = kall_ref[...]
    s = lax.dot_general(q, kall, (((1,), (1,)), ((), ())), preferred_element_type=jnp.float32)
    penalty = [jnp.where(j < n, 0.0, jnp.inf).astype(jnp.float32) for j in range(slots)]
    blocks = [(j, j * span + c * lanes) for j in range(slots) for c in range(span // lanes)]
    mx = None
    for j, at in blocks:
        blk = s[:, at : at + lanes]
        mx = blk if mx is None else jnp.maximum(mx, blk)
    rows = q.shape[0]

    def column(row, width):
        return jnp.broadcast_to(row, (width, rows)).T

    m_new = jnp.max(mx.T, axis=0, keepdims=True) * scale
    if not first:
        m_old = m_in[0]
        m_new = jnp.maximum(m_old, m_new)
        alpha = jnp.exp(m_old - m_new)
    log2e = 1.4426950408889634
    mb = column(m_new * log2e, lanes)
    shifted = [mb + penalty[j] for j in range(slots)]
    acc = None
    ps = []
    for j, at in blocks:
        p = jnp.exp2(s[:, at : at + lanes] * (scale * log2e) - shifted[j])
        acc = p if acc is None else acc + p
        ps.append(p.astype(jnp.bfloat16))
    pb = jnp.concatenate(ps, axis=1)
    mixed = jnp.dot(pb, kall, preferred_element_type=jnp.float32)
    total = jnp.sum(acc.T, axis=0, keepdims=True)
    width = mixed.shape[1]
    if not first:
        mixed = a_in[0] * column(alpha, width) + mixed
        total = t_in[0] * alpha + total
    if last:
        o_ref[0] = (mixed / column(total, width)).astype(o_ref.dtype)
    else:
        m_out[0] = m_new
        t_out[0] = total
        a_out[0] = mixed


def attend_chunk(state, queries, chunk, slot_owner, counts, scale, first, last):
    tiles, tile_size, channels = queries.shape
    owners, chunk_len, _ = chunk.shape
    slots = slot_owner.shape[1]
    col_spec = pl.BlockSpec((1, 1, tile_size), lambda t, o, c: (t, 0, 0))
    acc_spec = pl.BlockSpec((1, tile_size, channels), lambda t, o, c: (t, 0, 0))
    state_specs = [] if first else [col_spec, col_spec, acc_spec]
    if last:
        out_specs = acc_spec
        out_shape = jax.ShapeDtypeStruct(queries.shape, jnp.bfloat16)
    else:
        out_specs = [col_spec, col_spec, acc_spec]
        out_shape = [
            jax.ShapeDtypeStruct((tiles, 1, tile_size), jnp.float32),
            jax.ShapeDtypeStruct((tiles, 1, tile_size), jnp.float32),
            jax.ShapeDtypeStruct((tiles, tile_size, channels), jnp.float32),
        ]
    grid_spec = pltpu.PrefetchScalarGridSpec(
        num_scalar_prefetch=2,
        grid=(tiles,),
        in_specs=[
            acc_spec,
            pl.BlockSpec((owners, chunk_len, channels), lambda t, o, c: (0, 0, 0)),
        ]
        + state_specs,
        out_specs=out_specs,
        scratch_shapes=[pltpu.VMEM((slots * chunk_len, channels), jnp.bfloat16)],
    )
    return pl.pallas_call(
        functools.partial(attend_kernel, scale=scale, first=first, last=last),
        grid_spec=grid_spec,
        out_shape=out_shape,
        compiler_params=pltpu.CompilerParams(vmem_limit_bytes=48 * 1024 * 1024),
    )(slot_owner, counts, queries, chunk, *([] if first else state))


def on_device(frame_one, frame_two, tile_lists, conv_one, conv_two):
    band_rows, band_width, channels = frame_one.shape
    per_device = tile_lists.shape[0]
    tile_cols = band_width // per_device
    tile_size = band_rows * tile_cols
    owners = lax.axis_size("row")
    scale = float(channels) ** (-0.5)

    def band_to_tiles(band):
        return (
            band.reshape(band_rows, per_device, tile_cols, channels)
            .transpose(1, 0, 2, 3)
            .reshape(per_device, tile_size, channels)
        )

    query_tiles = band_to_tiles(frame_one)
    own_keys = band_to_tiles(frame_two)
    valid = tile_lists >= 0
    slot_owner = jnp.maximum(jnp.where(valid, tile_lists, tile_lists[:, :1]), 0) // per_device
    counts = jnp.sum(valid.astype(jnp.int32), axis=1)
    me = lax.axis_index("row")
    flat_lists = tile_lists.reshape(1, -1)
    lists_everywhere = jnp.broadcast_to(flat_lists, (owners, flat_lists.shape[1]))
    lists_of = lax.all_to_all(lists_everywhere, "row", split_axis=0, concat_axis=0, tiled=True)
    mine = (lists_of >= 0) & (lists_of // per_device == me)
    asked = jnp.max(jnp.where(mine, lists_of % per_device, 0), axis=1)
    edges = [0, tile_size // 2, tile_size]
    state = ()
    previous = None
    for index, (start, stop) in enumerate(zip(edges[:-1], edges[1:])):
        sending = jnp.take(own_keys[:, start:stop], asked, axis=0)
        if previous is not None:
            previous, sending, state = lax.optimization_barrier((previous, sending, state))
        current = lax.all_to_all(sending, "row", split_axis=0, concat_axis=0, tiled=True)
        if previous is not None:
            state = attend_chunk(state, query_tiles, previous, slot_owner, counts, scale, index == 1, False)
        previous = current
    warped_tiles = attend_chunk(
        state, query_tiles, previous, slot_owner, counts, scale, len(edges) == 2, True
    )
    warped = (
        warped_tiles.reshape(per_device, band_rows, tile_cols, channels)
        .transpose(1, 0, 2, 3)
        .reshape(band_rows, band_width, channels)
    )
    extended = halo_rows(warped, "row", 2)
    hidden = jax.nn.relu(native_conv(extended, conv_one)).astype(jnp.bfloat16)
    row_ids = jnp.arange(band_rows + 2)
    inside = ((row_ids > 0) | (me > 0)) & ((row_ids < band_rows + 1) | (me < owners - 1))
    hidden = jnp.where(inside[:, None, None], hidden, jnp.zeros_like(hidden))
    branch = native_conv(hidden, conv_two)
    return (frame_one.astype(jnp.float32) + branch).astype(jnp.bfloat16)


def solution(mesh):
    in_specs = (
        P(("pairs", "row"), None, None),
        P(("pairs", "row"), None, None),
        P(("pairs", "row"), None),
        P(),
        P(),
    )
    out_specs = P(("pairs", "row"), None, None)
    return jax.shard_map(
        on_device, mesh=mesh, in_specs=in_specs, out_specs=out_specs, check_vma=False
    )
```

```python
import functools

import jax
import jax.numpy as jnp
from jax import lax
from jax.experimental import pallas as pl
from jax.experimental.pallas import tpu as pltpu
from jax.sharding import PartitionSpec as P


def halo_rows(cells, axis, width):
    count = lax.axis_size(axis)
    even = lax.axis_index(axis) % 2 == 0
    head = cells[:width]
    tail = cells[cells.shape[0] - width :]
    same_chip = lax.ppermute(
        jnp.where(even, tail, head), axis, [(i, i ^ 1) for i in range(count)]
    )
    links = [(i, i + 1) for i in range(1, count - 1, 2)] + [(i + 1, i) for i in range(1, count - 1, 2)]
    across = lax.ppermute(jnp.where(even, head, tail), axis, links)
    from_above = jnp.where(even, across, same_chip)
    from_below = jnp.where(even, same_chip, across)
    return jnp.concatenate([from_above, cells, from_below], axis=0)


def convolve_rows(padded, weights, out_rows, out_cols):
    channels = padded.shape[2]
    summed = jnp.zeros((out_rows * out_cols, channels), jnp.float32)
    for row_shift in range(3):
        for col_shift in range(3):
            window = padded[row_shift : row_shift + out_rows, col_shift : col_shift + out_cols]
            window = window.reshape(out_rows * out_cols, channels)
            summed = summed + jnp.dot(
                window, weights[row_shift, col_shift], preferred_element_type=jnp.float32
            )
    return summed.reshape(out_rows, out_cols, channels)


def native_conv(rows, weights):
    out = lax.conv_general_dilated(
        rows[None],
        weights,
        window_strides=(1, 1),
        padding=((0, 0), (1, 1)),
        dimension_numbers=("NHWC", "HWIO", "NHWC"),
        preferred_element_type=jnp.float32,
    )
    return out[0]


def pad_columns(image):
    return jnp.pad(image, ((0, 0), (1, 1), (0, 0)))


def attend_kernel(owner_ref, count_ref, q_ref, k_ref, *refs, scale, first, last):
    if first:
        m_out, t_out, a_out, kall_ref = refs
    elif last:
        m_in, t_in, a_in, o_ref, kall_ref = refs
    else:
        m_in, t_in, a_in, m_out, t_out, a_out, kall_ref = refs
    t = pl.program_id(0)
    n = count_ref[t]
    slots = owner_ref.shape[1]
    span = k_ref.shape[1]
    lanes = 128
    for j in range(slots):
        kall_ref[j * span : (j + 1) * span, :] = k_ref[owner_ref[t, j]]
    q = q_ref[0]
    kall = kall_ref[...]
    s = lax.dot_general(q, kall, (((1,), (1,)), ((), ())), preferred_element_type=jnp.float32)
    penalty = [jnp.where(j < n, 0.0, jnp.inf).astype(jnp.float32) for j in range(slots)]
    blocks = [(j, j * span + c * lanes) for j in range(slots) for c in range(span // lanes)]
    mx = None
    for j, at in blocks:
        blk = s[:, at : at + lanes]
        mx = blk if mx is None else jnp.maximum(mx, blk)
    rows = q.shape[0]

    def column(row, width):
        return jnp.broadcast_to(row, (width, rows)).T

    m_new = jnp.max(mx.T, axis=0, keepdims=True) * scale
    if not first:
        m_old = m_in[0]
        m_new = jnp.maximum(m_old, m_new)
        alpha = jnp.exp(m_old - m_new)
    log2e = 1.4426950408889634
    mb = column(m_new * log2e, lanes)
    shifted = [mb + penalty[j] for j in range(slots)]
    acc = None
    ps = []
    for j, at in blocks:
        p = jnp.exp2(s[:, at : at + lanes] * (scale * log2e) - shifted[j])
        acc = p if acc is None else acc + p
        ps.append(p.astype(jnp.bfloat16))
    pb = jnp.concatenate(ps, axis=1)
    mixed = jnp.dot(pb, kall, preferred_element_type=jnp.float32)
    total = jnp.sum(acc.T, axis=0, keepdims=True)
    width = mixed.shape[1]
    if not first:
        mixed = a_in[0] * column(alpha, width) + mixed
        total = t_in[0] * alpha + total
    if last:
        o_ref[0] = (mixed / column(total, width)).astype(o_ref.dtype)
    else:
        m_out[0] = m_new
        t_out[0] = total
        a_out[0] = mixed


def attend_chunk(state, queries, chunk, slot_owner, counts, scale, first, last):
    tiles, tile_size, channels = queries.shape
    owners, chunk_len, _ = chunk.shape
    slots = slot_owner.shape[1]
    col_spec = pl.BlockSpec((1, 1, tile_size), lambda t, o, c: (t, 0, 0))
    acc_spec = pl.BlockSpec((1, tile_size, channels), lambda t, o, c: (t, 0, 0))
    state_specs = [] if first else [col_spec, col_spec, acc_spec]
    if last:
        out_specs = acc_spec
        out_shape = jax.ShapeDtypeStruct(queries.shape, jnp.bfloat16)
    else:
        out_specs = [col_spec, col_spec, acc_spec]
        out_shape = [
            jax.ShapeDtypeStruct((tiles, 1, tile_size), jnp.float32),
            jax.ShapeDtypeStruct((tiles, 1, tile_size), jnp.float32),
            jax.ShapeDtypeStruct((tiles, tile_size, channels), jnp.float32),
        ]
    grid_spec = pltpu.PrefetchScalarGridSpec(
        num_scalar_prefetch=2,
        grid=(tiles,),
        in_specs=[
            acc_spec,
            pl.BlockSpec((owners, chunk_len, channels), lambda t, o, c: (0, 0, 0)),
        ]
        + state_specs,
        out_specs=out_specs,
        scratch_shapes=[pltpu.VMEM((slots * chunk_len, channels), jnp.bfloat16)],
    )
    return pl.pallas_call(
        functools.partial(attend_kernel, scale=scale, first=first, last=last),
        grid_spec=grid_spec,
        out_shape=out_shape,
        compiler_params=pltpu.CompilerParams(vmem_limit_bytes=48 * 1024 * 1024),
    )(slot_owner, counts, queries, chunk, *([] if first else state))


def on_device(frame_one, frame_two, tile_lists, conv_one, conv_two):
    band_rows, band_width, channels = frame_one.shape
    per_device = tile_lists.shape[0]
    tile_cols = band_width // per_device
    tile_size = band_rows * tile_cols
    owners = lax.axis_size("row")
    scale = float(channels) ** (-0.5)

    def band_to_tiles(band):
        return (
            band.reshape(band_rows, per_device, tile_cols, channels)
            .transpose(1, 0, 2, 3)
            .reshape(per_device, tile_size, channels)
        )

    query_tiles = band_to_tiles(frame_one)
    own_keys = band_to_tiles(frame_two)
    valid = tile_lists >= 0
    slot_owner = jnp.maximum(jnp.where(valid, tile_lists, tile_lists[:, :1]), 0) // per_device
    counts = jnp.sum(valid.astype(jnp.int32), axis=1)
    me = lax.axis_index("row")
    flat_lists = tile_lists.reshape(1, -1)
    lists_everywhere = jnp.broadcast_to(flat_lists, (owners, flat_lists.shape[1]))
    lists_of = lax.all_to_all(lists_everywhere, "row", split_axis=0, concat_axis=0, tiled=True)
    mine = (lists_of >= 0) & (lists_of // per_device == me)
    asked = jnp.max(jnp.where(mine, lists_of % per_device, 0), axis=1)
    edges = [0, tile_size // 2, tile_size]
    state = ()
    previous = None
    for index, (start, stop) in enumerate(zip(edges[:-1], edges[1:])):
        sending = jnp.take(own_keys[:, start:stop], asked, axis=0)
        if previous is not None:
            previous, sending, state = lax.optimization_barrier((previous, sending, state))
        current = lax.all_to_all(sending, "row", split_axis=0, concat_axis=0, tiled=True)
        if previous is not None:
            state = attend_chunk(state, query_tiles, previous, slot_owner, counts, scale, index == 1, False)
        previous = current
    warped_tiles = attend_chunk(
        state, query_tiles, previous, slot_owner, counts, scale, len(edges) == 2, True
    )
    warped = (
        warped_tiles.reshape(per_device, band_rows, tile_cols, channels)
        .transpose(1, 0, 2, 3)
        .reshape(band_rows, band_width, channels)
    )
    extended = halo_rows(warped, "row", 2)
    hidden = jax.nn.relu(native_conv(extended, conv_one)).astype(jnp.bfloat16)
    row_ids = jnp.arange(band_rows + 2)
    inside = ((row_ids > 0) | (me > 0)) & ((row_ids < band_rows + 1) | (me < owners - 1))
    hidden = jnp.where(inside[:, None, None], hidden, jnp.zeros_like(hidden))
    branch = native_conv(hidden, conv_two)
    return (frame_one.astype(jnp.float32) + branch).astype(jnp.bfloat16)


def solution(mesh):
    in_specs = (
        P(("pairs", "row"), None, None),
        P(("pairs", "row"), None, None),
        P(("pairs", "row"), None),
        P(),
        P(),
    )
    out_specs = P(("pairs", "row"), None, None)
    return jax.shard_map(
        on_device, mesh=mesh, in_specs=in_specs, out_specs=out_specs, check_vma=False
    )
```

```python
import functools

import jax
import jax.numpy as jnp
from jax import lax
from jax.experimental import pallas as pl
from jax.experimental.pallas import tpu as pltpu
from jax.sharding import PartitionSpec as P


def halo_rows(cells, axis, width):
    count = lax.axis_size(axis)
    even = lax.axis_index(axis) % 2 == 0
    head = cells[:width]
    tail = cells[cells.shape[0] - width :]
    same_chip = lax.ppermute(
        jnp.where(even, tail, head), axis, [(i, i ^ 1) for i in range(count)]
    )
    links = [(i, i + 1) for i in range(1, count - 1, 2)] + [(i + 1, i) for i in range(1, count - 1, 2)]
    across = lax.ppermute(jnp.where(even, head, tail), axis, links)
    from_above = jnp.where(even, across, same_chip)
    from_below = jnp.where(even, same_chip, across)
    return jnp.concatenate([from_above, cells, from_below], axis=0)


def convolve_rows(padded, weights, out_rows, out_cols):
    channels = padded.shape[2]
    summed = jnp.zeros((out_rows * out_cols, channels), jnp.float32)
    for row_shift in range(3):
        for col_shift in range(3):
            window = padded[row_shift : row_shift + out_rows, col_shift : col_shift + out_cols]
            window = window.reshape(out_rows * out_cols, channels)
            summed = summed + jnp.dot(
                window, weights[row_shift, col_shift], preferred_element_type=jnp.float32
            )
    return summed.reshape(out_rows, out_cols, channels)


def native_conv(rows, weights):
    out = lax.conv_general_dilated(
        rows[None],
        weights,
        window_strides=(1, 1),
        padding=((0, 0), (1, 1)),
        dimension_numbers=("NHWC", "HWIO", "NHWC"),
        preferred_element_type=jnp.float32,
    )
    return out[0]


def pad_columns(image):
    return jnp.pad(image, ((0, 0), (1, 1), (0, 0)))


def attend_kernel(owner_ref, count_ref, q_ref, k_ref, *refs, scale, first, last):
    if first:
        m_out, t_out, a_out, kall_ref = refs
    elif last:
        m_in, t_in, a_in, o_ref, kall_ref = refs
    else:
        m_in, t_in, a_in, m_out, t_out, a_out, kall_ref = refs
    t = pl.program_id(0)
    n = count_ref[t]
    slots = owner_ref.shape[1]
    span = k_ref.shape[1]
    lanes = 128
    for j in range(slots):
        kall_ref[j * span : (j + 1) * span, :] = k_ref[owner_ref[t, j]]
    q = q_ref[0]
    kall = kall_ref[...]
    s = lax.dot_general(q, kall, (((1,), (1,)), ((), ())), preferred_element_type=jnp.float32)
    penalty = [jnp.where(j < n, 0.0, jnp.inf).astype(jnp.float32) for j in range(slots)]
    blocks = [(j, j * span + c * lanes) for j in range(slots) for c in range(span // lanes)]
    mx = None
    for j, at in blocks:
        blk = s[:, at : at + lanes]
        mx = blk if mx is None else jnp.maximum(mx, blk)
    rows = q.shape[0]

    def column(row, width):
        return jnp.broadcast_to(row, (width, rows)).T

    m_new = jnp.max(mx.T, axis=0, keepdims=True) * scale
    if not first:
        m_old = m_in[0]
        m_new = jnp.maximum(m_old, m_new)
        alpha = jnp.exp(m_old - m_new)
    log2e = 1.4426950408889634
    mb = column(m_new * log2e, lanes)
    shifted = [mb + penalty[j] for j in range(slots)]
    acc = None
    ps = []
    for j, at in blocks:
        p = jnp.exp2(s[:, at : at + lanes] * (scale * log2e) - shifted[j])
        acc = p if acc is None else acc + p
        ps.append(p.astype(jnp.bfloat16))
    pb = jnp.concatenate(ps, axis=1)
    mixed = jnp.dot(pb, kall, preferred_element_type=jnp.float32)
    total = jnp.sum(acc.T, axis=0, keepdims=True)
    width = mixed.shape[1]
    if not first:
        mixed = a_in[0] * column(alpha, width) + mixed
        total = t_in[0] * alpha + total
    if last:
        o_ref[0] = (mixed / column(total, width)).astype(o_ref.dtype)
    else:
        m_out[0] = m_new
        t_out[0] = total
        a_out[0] = mixed


def attend_chunk(state, queries, chunk, slot_owner, counts, scale, first, last):
    tiles, tile_size, channels = queries.shape
    owners, chunk_len, _ = chunk.shape
    slots = slot_owner.shape[1]
    col_spec = pl.BlockSpec((1, 1, tile_size), lambda t, o, c: (t, 0, 0))
    acc_spec = pl.BlockSpec((1, tile_size, channels), lambda t, o, c: (t, 0, 0))
    state_specs = [] if first else [col_spec, col_spec, acc_spec]
    if last:
        out_specs = acc_spec
        out_shape = jax.ShapeDtypeStruct(queries.shape, jnp.bfloat16)
    else:
        out_specs = [col_spec, col_spec, acc_spec]
        out_shape = [
            jax.ShapeDtypeStruct((tiles, 1, tile_size), jnp.float32),
            jax.ShapeDtypeStruct((tiles, 1, tile_size), jnp.float32),
            jax.ShapeDtypeStruct((tiles, tile_size, channels), jnp.float32),
        ]
    grid_spec = pltpu.PrefetchScalarGridSpec(
        num_scalar_prefetch=2,
        grid=(tiles,),
        in_specs=[
            acc_spec,
            pl.BlockSpec((owners, chunk_len, channels), lambda t, o, c: (0, 0, 0)),
        ]
        + state_specs,
        out_specs=out_specs,
        scratch_shapes=[pltpu.VMEM((slots * chunk_len, channels), jnp.bfloat16)],
    )
    return pl.pallas_call(
        functools.partial(attend_kernel, scale=scale, first=first, last=last),
        grid_spec=grid_spec,
        out_shape=out_shape,
        compiler_params=pltpu.CompilerParams(vmem_limit_bytes=48 * 1024 * 1024),
    )(slot_owner, counts, queries, chunk, *([] if first else state))


def attend_last_half(state, queries, chunk, slot_owner, counts, half, scale):
    tiles, tile_size, channels = queries.shape
    owners, chunk_len, _ = chunk.shape
    slots = slot_owner.shape[1]
    part = tile_size // 2
    row_spec = pl.BlockSpec((1, 1, part), lambda t, o, c, h: (t, 0, h[0]))
    acc_spec = pl.BlockSpec((1, part, channels), lambda t, o, c, h: (t, h[0], 0))
    grid_spec = pltpu.PrefetchScalarGridSpec(
        num_scalar_prefetch=3,
        grid=(tiles,),
        in_specs=[
            acc_spec,
            pl.BlockSpec((owners, chunk_len, channels), lambda t, o, c, h: (0, 0, 0)),
            row_spec,
            row_spec,
            acc_spec,
        ],
        out_specs=pl.BlockSpec((1, part, channels), lambda t, o, c, h: (t, 0, 0)),
        scratch_shapes=[pltpu.VMEM((slots * chunk_len, channels), jnp.bfloat16)],
    )

    def kernel(owner_ref, count_ref, half_ref, *refs):
        attend_kernel(owner_ref, count_ref, *refs, scale=scale, first=False, last=True)

    return pl.pallas_call(
        kernel,
        grid_spec=grid_spec,
        out_shape=jax.ShapeDtypeStruct((tiles, part, channels), jnp.bfloat16),
        compiler_params=pltpu.CompilerParams(vmem_limit_bytes=48 * 1024 * 1024),
    )(slot_owner, counts, half, queries, chunk, *state)


def on_device(frame_one, frame_two, tile_lists, conv_one, conv_two):
    band_rows, band_width, channels = frame_one.shape
    per_device = tile_lists.shape[0]
    tile_cols = band_width // per_device
    tile_size = band_rows * tile_cols
    owners = lax.axis_size("row")
    scale = float(channels) ** (-0.5)

    def band_to_tiles(band):
        return (
            band.reshape(band_rows, per_device, tile_cols, channels)
            .transpose(1, 0, 2, 3)
            .reshape(per_device, tile_size, channels)
        )

    query_tiles = band_to_tiles(frame_one)
    own_keys = band_to_tiles(frame_two)
    valid = tile_lists >= 0
    slot_owner = jnp.maximum(jnp.where(valid, tile_lists, tile_lists[:, :1]), 0) // per_device
    counts = jnp.sum(valid.astype(jnp.int32), axis=1)
    me = lax.axis_index("row")
    flat_lists = tile_lists.reshape(1, -1)
    lists_everywhere = jnp.broadcast_to(flat_lists, (owners, flat_lists.shape[1]))
    lists_of = lax.all_to_all(lists_everywhere, "row", split_axis=0, concat_axis=0, tiled=True)
    mine = (lists_of >= 0) & (lists_of // per_device == me)
    asked = jnp.max(jnp.where(mine, lists_of % per_device, 0), axis=1)
    edges = [0, tile_size // 2, tile_size]
    state = ()
    previous = None
    for index, (start, stop) in enumerate(zip(edges[:-1], edges[1:])):
        sending = jnp.take(own_keys[:, start:stop], asked, axis=0)
        if previous is not None:
            previous, sending, state = lax.optimization_barrier((previous, sending, state))
        current = lax.all_to_all(sending, "row", split_axis=0, concat_axis=0, tiled=True)
        if previous is not None:
            state = attend_chunk(state, query_tiles, previous, slot_owner, counts, scale, index == 1, False)
        previous = current
    even = me % 2 == 0
    crossing = jnp.where(even, 0, 1).astype(jnp.int32).reshape(1)
    staying = (1 - crossing).astype(jnp.int32)
    crossing_tiles = attend_last_half(state, query_tiles, previous, slot_owner, counts, crossing, scale)
    staying_tiles = attend_last_half(state, query_tiles, previous, slot_owner, counts, staying, scale)

    def to_rows(tiles):
        return tiles.reshape(per_device, -1, tile_cols, channels).transpose(1, 0, 2, 3).reshape(
            -1, band_width, channels
        )

    crossing_rows = to_rows(crossing_tiles)
    staying_rows = to_rows(staying_tiles)
    count = lax.axis_size("row")
    links = [(i, i + 1) for i in range(1, count - 1, 2)] + [(i + 1, i) for i in range(1, count - 1, 2)]
    across = lax.ppermute(crossing_rows, "row", links)
    same_chip = lax.ppermute(staying_rows, "row", [(i, i ^ 1) for i in range(count)])
    warped = jnp.where(
        even,
        jnp.concatenate([crossing_rows, staying_rows], axis=0),
        jnp.concatenate([staying_rows, crossing_rows], axis=0),
    )
    from_above = jnp.where(even, across, same_chip)
    from_below = jnp.where(even, same_chip, across)
    extended = jnp.concatenate([from_above, warped, from_below], axis=0)
    hidden = jax.nn.relu(native_conv(extended, conv_one)).astype(jnp.bfloat16)
    row_ids = jnp.arange(band_rows + 2)
    inside = ((row_ids > 0) | (me > 0)) & ((row_ids < band_rows + 1) | (me < owners - 1))
    hidden = jnp.where(inside[:, None, None], hidden, jnp.zeros_like(hidden))
    branch = native_conv(hidden, conv_two)
    return (frame_one.astype(jnp.float32) + branch).astype(jnp.bfloat16)


def solution(mesh):
    in_specs = (
        P(("pairs", "row"), None, None),
        P(("pairs", "row"), None, None),
        P(("pairs", "row"), None),
        P(),
        P(),
    )
    out_specs = P(("pairs", "row"), None, None)
    return jax.shard_map(
        on_device, mesh=mesh, in_specs=in_specs, out_specs=out_specs, check_vma=False
    )
```

```python
import functools

import jax
import jax.numpy as jnp
from jax import lax
from jax.experimental import pallas as pl
from jax.experimental.pallas import tpu as pltpu
from jax.sharding import PartitionSpec as P


def halo_rows(cells, axis, width):
    count = lax.axis_size(axis)
    even = lax.axis_index(axis) % 2 == 0
    head = cells[:width]
    tail = cells[cells.shape[0] - width :]
    same_chip = lax.ppermute(
        jnp.where(even, tail, head), axis, [(i, i ^ 1) for i in range(count)]
    )
    links = [(i, i + 1) for i in range(1, count - 1, 2)] + [(i + 1, i) for i in range(1, count - 1, 2)]
    across = lax.ppermute(jnp.where(even, head, tail), axis, links)
    from_above = jnp.where(even, across, same_chip)
    from_below = jnp.where(even, same_chip, across)
    return jnp.concatenate([from_above, cells, from_below], axis=0)


def convolve_rows(padded, weights, out_rows, out_cols):
    channels = padded.shape[2]
    summed = jnp.zeros((out_rows * out_cols, channels), jnp.float32)
    for row_shift in range(3):
        for col_shift in range(3):
            window = padded[row_shift : row_shift + out_rows, col_shift : col_shift + out_cols]
            window = window.reshape(out_rows * out_cols, channels)
            summed = summed + jnp.dot(
                window, weights[row_shift, col_shift], preferred_element_type=jnp.float32
            )
    return summed.reshape(out_rows, out_cols, channels)


def native_conv(rows, weights):
    out = lax.conv_general_dilated(
        rows[None],
        weights,
        window_strides=(1, 1),
        padding=((0, 0), (1, 1)),
        dimension_numbers=("NHWC", "HWIO", "NHWC"),
        preferred_element_type=jnp.float32,
    )
    return out[0]


def pad_columns(image):
    return jnp.pad(image, ((0, 0), (1, 1), (0, 0)))


def attend_kernel(owner_ref, count_ref, q_ref, k_ref, *refs, scale, first, last):
    if first:
        m_out, t_out, a_out, kall_ref = refs
    elif last:
        m_in, t_in, a_in, o_ref, kall_ref = refs
    else:
        m_in, t_in, a_in, m_out, t_out, a_out, kall_ref = refs
    t = pl.program_id(0)
    n = count_ref[t]
    slots = owner_ref.shape[1]
    span = k_ref.shape[1]
    lanes = 128
    for j in range(slots):
        kall_ref[j * span : (j + 1) * span, :] = k_ref[owner_ref[t, j]]
    q = q_ref[0]
    kall = kall_ref[...]
    s = lax.dot_general(q, kall, (((1,), (1,)), ((), ())), preferred_element_type=jnp.float32)
    penalty = [jnp.where(j < n, 0.0, jnp.inf).astype(jnp.float32) for j in range(slots)]
    blocks = [(j, j * span + c * lanes) for j in range(slots) for c in range(span // lanes)]
    mx = None
    for j, at in blocks:
        blk = s[:, at : at + lanes]
        mx = blk if mx is None else jnp.maximum(mx, blk)
    rows = q.shape[0]

    def column(row, width):
        return jnp.broadcast_to(row, (width, rows)).T

    m_new = jnp.max(mx.T, axis=0, keepdims=True) * scale
    if not first:
        m_old = m_in[0]
        m_new = jnp.maximum(m_old, m_new)
        alpha = jnp.exp(m_old - m_new)
    log2e = 1.4426950408889634
    mb = column(m_new * log2e, lanes)
    shifted = [mb + penalty[j] for j in range(slots)]
    acc = None
    ps = []
    for j, at in blocks:
        p = jnp.exp2(s[:, at : at + lanes] * (scale * log2e) - shifted[j])
        acc = p if acc is None else acc + p
        ps.append(p.astype(jnp.bfloat16))
    pb = jnp.concatenate(ps, axis=1)
    mixed = jnp.dot(pb, kall, preferred_element_type=jnp.float32)
    total = jnp.sum(acc.T, axis=0, keepdims=True)
    width = mixed.shape[1]
    if not first:
        mixed = a_in[0] * column(alpha, width) + mixed
        total = t_in[0] * alpha + total
    if last:
        o_ref[0] = (mixed / column(total, width)).astype(o_ref.dtype)
    else:
        m_out[0] = m_new
        t_out[0] = total
        a_out[0] = mixed


def attend_chunk(state, queries, chunk, slot_owner, counts, scale, first, last):
    tiles, tile_size, channels = queries.shape
    owners, chunk_len, _ = chunk.shape
    slots = slot_owner.shape[1]
    col_spec = pl.BlockSpec((1, 1, tile_size), lambda t, o, c: (t, 0, 0))
    acc_spec = pl.BlockSpec((1, tile_size, channels), lambda t, o, c: (t, 0, 0))
    state_specs = [] if first else [col_spec, col_spec, acc_spec]
    if last:
        out_specs = acc_spec
        out_shape = jax.ShapeDtypeStruct(queries.shape, jnp.bfloat16)
    else:
        out_specs = [col_spec, col_spec, acc_spec]
        out_shape = [
            jax.ShapeDtypeStruct((tiles, 1, tile_size), jnp.float32),
            jax.ShapeDtypeStruct((tiles, 1, tile_size), jnp.float32),
            jax.ShapeDtypeStruct((tiles, tile_size, channels), jnp.float32),
        ]
    grid_spec = pltpu.PrefetchScalarGridSpec(
        num_scalar_prefetch=2,
        grid=(tiles,),
        in_specs=[
            acc_spec,
            pl.BlockSpec((owners, chunk_len, channels), lambda t, o, c: (0, 0, 0)),
        ]
        + state_specs,
        out_specs=out_specs,
        scratch_shapes=[pltpu.VMEM((slots * chunk_len, channels), jnp.bfloat16)],
    )
    return pl.pallas_call(
        functools.partial(attend_kernel, scale=scale, first=first, last=last),
        grid_spec=grid_spec,
        out_shape=out_shape,
        compiler_params=pltpu.CompilerParams(vmem_limit_bytes=48 * 1024 * 1024),
    )(slot_owner, counts, queries, chunk, *([] if first else state))


def attend_last_half(state, queries, chunk, slot_owner, counts, half, scale):
    tiles, tile_size, channels = queries.shape
    owners, chunk_len, _ = chunk.shape
    slots = slot_owner.shape[1]
    part = tile_size // 2
    row_spec = pl.BlockSpec((1, 1, part), lambda t, o, c, h: (t, 0, h[0]))
    acc_spec = pl.BlockSpec((1, part, channels), lambda t, o, c, h: (t, h[0], 0))
    grid_spec = pltpu.PrefetchScalarGridSpec(
        num_scalar_prefetch=3,
        grid=(tiles,),
        in_specs=[
            acc_spec,
            pl.BlockSpec((owners, chunk_len, channels), lambda t, o, c, h: (0, 0, 0)),
            row_spec,
            row_spec,
            acc_spec,
        ],
        out_specs=pl.BlockSpec((1, part, channels), lambda t, o, c, h: (t, 0, 0)),
        scratch_shapes=[pltpu.VMEM((slots * chunk_len, channels), jnp.bfloat16)],
    )

    def kernel(owner_ref, count_ref, half_ref, *refs):
        attend_kernel(owner_ref, count_ref, *refs, scale=scale, first=False, last=True)

    return pl.pallas_call(
        kernel,
        grid_spec=grid_spec,
        out_shape=jax.ShapeDtypeStruct((tiles, part, channels), jnp.bfloat16),
        compiler_params=pltpu.CompilerParams(vmem_limit_bytes=48 * 1024 * 1024),
    )(slot_owner, counts, half, queries, chunk, *state)


def on_device(frame_one, frame_two, tile_lists, conv_one, conv_two):
    band_rows, band_width, channels = frame_one.shape
    per_device = tile_lists.shape[0]
    tile_cols = band_width // per_device
    tile_size = band_rows * tile_cols
    owners = lax.axis_size("row")
    scale = float(channels) ** (-0.5)

    def band_to_tiles(band):
        return (
            band.reshape(band_rows, per_device, tile_cols, channels)
            .transpose(1, 0, 2, 3)
            .reshape(per_device, tile_size, channels)
        )

    query_tiles = band_to_tiles(frame_one)
    own_keys = band_to_tiles(frame_two)
    valid = tile_lists >= 0
    slot_owner = jnp.maximum(jnp.where(valid, tile_lists, tile_lists[:, :1]), 0) // per_device
    counts = jnp.sum(valid.astype(jnp.int32), axis=1)
    me = lax.axis_index("row")
    flat_lists = tile_lists.reshape(1, -1)
    lists_everywhere = jnp.broadcast_to(flat_lists, (owners, flat_lists.shape[1]))
    lists_of = lax.all_to_all(lists_everywhere, "row", split_axis=0, concat_axis=0, tiled=True)
    mine = (lists_of >= 0) & (lists_of // per_device == me)
    asked = jnp.max(jnp.where(mine, lists_of % per_device, 0), axis=1)
    edges = [0, tile_size // 2, tile_size]
    state = ()
    previous = None
    for index, (start, stop) in enumerate(zip(edges[:-1], edges[1:])):
        sending = jnp.take(own_keys[:, start:stop], asked, axis=0)
        if previous is not None:
            previous, sending, state = lax.optimization_barrier((previous, sending, state))
        current = lax.all_to_all(sending, "row", split_axis=0, concat_axis=0, tiled=True)
        if previous is not None:
            state = attend_chunk(state, query_tiles, previous, slot_owner, counts, scale, index == 1, False)
        previous = current
    even = me % 2 == 0
    crossing = jnp.where(even, 0, 1).astype(jnp.int32).reshape(1)
    staying = (1 - crossing).astype(jnp.int32)
    crossing_tiles = attend_last_half(state, query_tiles, previous, slot_owner, counts, crossing, scale)
    staying_tiles = attend_last_half(state, query_tiles, previous, slot_owner, counts, staying, scale)

    def to_rows(tiles):
        return tiles.reshape(per_device, -1, tile_cols, channels).transpose(1, 0, 2, 3).reshape(
            -1, band_width, channels
        )

    crossing_rows = to_rows(crossing_tiles)
    staying_rows = to_rows(staying_tiles)
    count = lax.axis_size("row")
    links = [(i, i + 1) for i in range(1, count - 1, 2)] + [(i + 1, i) for i in range(1, count - 1, 2)]
    across = lax.ppermute(crossing_rows, "row", links)
    same_chip = lax.ppermute(staying_rows, "row", [(i, i ^ 1) for i in range(count)])
    half_rows = crossing_rows.shape[0]
    extended = jnp.zeros((band_rows + 2 * half_rows, band_width, channels), crossing_rows.dtype)
    outer = jnp.where(even, 0, band_rows + half_rows)
    inner = jnp.where(even, band_rows + half_rows, 0)
    for rows, at in (
        (crossing_rows, half_rows + crossing[0] * half_rows),
        (staying_rows, half_rows + staying[0] * half_rows),
        (across, outer),
        (same_chip, inner),
    ):
        extended = lax.dynamic_update_slice(extended, rows, (at, 0, 0))
    hidden = jax.nn.relu(native_conv(extended, conv_one)).astype(jnp.bfloat16)
    row_ids = jnp.arange(band_rows + 2)
    inside = ((row_ids > 0) | (me > 0)) & ((row_ids < band_rows + 1) | (me < owners - 1))
    hidden = jnp.where(inside[:, None, None], hidden, jnp.zeros_like(hidden))
    branch = native_conv(hidden, conv_two)
    return (frame_one.astype(jnp.float32) + branch).astype(jnp.bfloat16)


def solution(mesh):
    in_specs = (
        P(("pairs", "row"), None, None),
        P(("pairs", "row"), None, None),
        P(("pairs", "row"), None),
        P(),
        P(),
    )
    out_specs = P(("pairs", "row"), None, None)
    return jax.shard_map(
        on_device, mesh=mesh, in_specs=in_specs, out_specs=out_specs, check_vma=False
    )
```

```python
import functools

import jax
import jax.numpy as jnp
from jax import lax
from jax.experimental import pallas as pl
from jax.experimental.pallas import tpu as pltpu
from jax.sharding import PartitionSpec as P


def halo_rows(cells, axis, width):
    count = lax.axis_size(axis)
    even = lax.axis_index(axis) % 2 == 0
    head = cells[:width]
    tail = cells[cells.shape[0] - width :]
    same_chip = lax.ppermute(
        jnp.where(even, tail, head), axis, [(i, i ^ 1) for i in range(count)]
    )
    links = [(i, i + 1) for i in range(1, count - 1, 2)] + [(i + 1, i) for i in range(1, count - 1, 2)]
    across = lax.ppermute(jnp.where(even, head, tail), axis, links)
    from_above = jnp.where(even, across, same_chip)
    from_below = jnp.where(even, same_chip, across)
    return jnp.concatenate([from_above, cells, from_below], axis=0)


def convolve_rows(padded, weights, out_rows, out_cols):
    channels = padded.shape[2]
    summed = jnp.zeros((out_rows * out_cols, channels), jnp.float32)
    for row_shift in range(3):
        for col_shift in range(3):
            window = padded[row_shift : row_shift + out_rows, col_shift : col_shift + out_cols]
            window = window.reshape(out_rows * out_cols, channels)
            summed = summed + jnp.dot(
                window, weights[row_shift, col_shift], preferred_element_type=jnp.float32
            )
    return summed.reshape(out_rows, out_cols, channels)


def native_conv(rows, weights):
    out = lax.conv_general_dilated(
        rows[None],
        weights,
        window_strides=(1, 1),
        padding=((0, 0), (1, 1)),
        dimension_numbers=("NHWC", "HWIO", "NHWC"),
        preferred_element_type=jnp.float32,
    )
    return out[0]


def pad_columns(image):
    return jnp.pad(image, ((0, 0), (1, 1), (0, 0)))


def attend_kernel(owner_ref, count_ref, q_ref, k_ref, *refs, scale, first, last):
    if first and last:
        o_ref, kall_ref = refs
    elif first:
        m_out, t_out, a_out, kall_ref = refs
    elif last:
        m_in, t_in, a_in, o_ref, kall_ref = refs
    else:
        m_in, t_in, a_in, m_out, t_out, a_out, kall_ref = refs
    t = pl.program_id(0)
    n = count_ref[t]
    slots = owner_ref.shape[1]
    span = k_ref.shape[1]
    lanes = 128
    for j in range(slots):
        kall_ref[j * span : (j + 1) * span, :] = k_ref[owner_ref[t, j]]
    q = q_ref[0]
    kall = kall_ref[...]
    s = lax.dot_general(q, kall, (((1,), (1,)), ((), ())), preferred_element_type=jnp.float32)
    penalty = [jnp.where(j < n, 0.0, jnp.inf).astype(jnp.float32) for j in range(slots)]
    blocks = [(j, j * span + c * lanes) for j in range(slots) for c in range(span // lanes)]
    mx = None
    for j, at in blocks:
        blk = s[:, at : at + lanes]
        mx = blk if mx is None else jnp.maximum(mx, blk)
    rows = q.shape[0]

    def column(row, width):
        return jnp.broadcast_to(row, (width, rows)).T

    m_new = jnp.max(mx.T, axis=0, keepdims=True) * scale
    if not first:
        m_old = m_in[0]
        m_new = jnp.maximum(m_old, m_new)
        alpha = jnp.exp(m_old - m_new)
    log2e = 1.4426950408889634
    mb = column(m_new * log2e, lanes)
    shifted = [mb + penalty[j] for j in range(slots)]
    acc = None
    ps = []
    for j, at in blocks:
        p = jnp.exp2(s[:, at : at + lanes] * (scale * log2e) - shifted[j])
        acc = p if acc is None else acc + p
        ps.append(p.astype(jnp.bfloat16))
    pb = jnp.concatenate(ps, axis=1)
    mixed = jnp.dot(pb, kall, preferred_element_type=jnp.float32)
    total = jnp.sum(acc.T, axis=0, keepdims=True)
    width = mixed.shape[1]
    if not first:
        mixed = a_in[0] * column(alpha, width) + mixed
        total = t_in[0] * alpha + total
    if last:
        o_ref[0] = (mixed / column(total, width)).astype(o_ref.dtype)
    else:
        m_out[0] = m_new
        t_out[0] = total
        a_out[0] = mixed


def attend_chunk(state, queries, chunk, slot_owner, counts, scale, first, last):
    tiles, tile_size, channels = queries.shape
    owners, chunk_len, _ = chunk.shape
    slots = slot_owner.shape[1]
    col_spec = pl.BlockSpec((1, 1, tile_size), lambda t, o, c: (t, 0, 0))
    acc_spec = pl.BlockSpec((1, tile_size, channels), lambda t, o, c: (t, 0, 0))
    state_specs = [] if first else [col_spec, col_spec, acc_spec]
    if last:
        out_specs = acc_spec
        out_shape = jax.ShapeDtypeStruct(queries.shape, jnp.bfloat16)
    else:
        out_specs = [col_spec, col_spec, acc_spec]
        out_shape = [
            jax.ShapeDtypeStruct((tiles, 1, tile_size), jnp.float32),
            jax.ShapeDtypeStruct((tiles, 1, tile_size), jnp.float32),
            jax.ShapeDtypeStruct((tiles, tile_size, channels), jnp.float32),
        ]
    grid_spec = pltpu.PrefetchScalarGridSpec(
        num_scalar_prefetch=2,
        grid=(tiles,),
        in_specs=[
            acc_spec,
            pl.BlockSpec((owners, chunk_len, channels), lambda t, o, c: (0, 0, 0)),
        ]
        + state_specs,
        out_specs=out_specs,
        scratch_shapes=[pltpu.VMEM((slots * chunk_len, channels), jnp.bfloat16)],
    )
    return pl.pallas_call(
        functools.partial(attend_kernel, scale=scale, first=first, last=last),
        grid_spec=grid_spec,
        out_shape=out_shape,
        compiler_params=pltpu.CompilerParams(vmem_limit_bytes=48 * 1024 * 1024),
    )(slot_owner, counts, queries, chunk, *([] if first else state))


def attend_last_half(state, queries, chunk, slot_owner, counts, half, scale):
    first = len(state) == 0
    tiles, tile_size, channels = queries.shape
    owners, chunk_len, _ = chunk.shape
    slots = slot_owner.shape[1]
    part = tile_size // 2
    row_spec = pl.BlockSpec((1, 1, part), lambda t, o, c, h: (t, 0, h[0]))
    acc_spec = pl.BlockSpec((1, part, channels), lambda t, o, c, h: (t, h[0], 0))
    grid_spec = pltpu.PrefetchScalarGridSpec(
        num_scalar_prefetch=3,
        grid=(tiles,),
        in_specs=[
            acc_spec,
            pl.BlockSpec((owners, chunk_len, channels), lambda t, o, c, h: (0, 0, 0)),
        ]
        + ([] if first else [row_spec, row_spec, acc_spec]),
        out_specs=pl.BlockSpec((1, part, channels), lambda t, o, c, h: (t, 0, 0)),
        scratch_shapes=[pltpu.VMEM((slots * chunk_len, channels), jnp.bfloat16)],
    )

    def kernel(owner_ref, count_ref, half_ref, *refs):
        attend_kernel(owner_ref, count_ref, *refs, scale=scale, first=first, last=True)

    return pl.pallas_call(
        kernel,
        grid_spec=grid_spec,
        out_shape=jax.ShapeDtypeStruct((tiles, part, channels), jnp.bfloat16),
        compiler_params=pltpu.CompilerParams(vmem_limit_bytes=48 * 1024 * 1024),
    )(slot_owner, counts, half, queries, chunk, *state)


def on_device(frame_one, frame_two, tile_lists, conv_one, conv_two):
    band_rows, band_width, channels = frame_one.shape
    per_device = tile_lists.shape[0]
    tile_cols = band_width // per_device
    tile_size = band_rows * tile_cols
    owners = lax.axis_size("row")
    scale = float(channels) ** (-0.5)

    def band_to_tiles(band):
        return (
            band.reshape(band_rows, per_device, tile_cols, channels)
            .transpose(1, 0, 2, 3)
            .reshape(per_device, tile_size, channels)
        )

    query_tiles = band_to_tiles(frame_one)
    own_keys = band_to_tiles(frame_two)
    valid = tile_lists >= 0
    slot_owner = jnp.maximum(jnp.where(valid, tile_lists, tile_lists[:, :1]), 0) // per_device
    counts = jnp.sum(valid.astype(jnp.int32), axis=1)
    me = lax.axis_index("row")
    flat_lists = tile_lists.reshape(1, -1)
    lists_everywhere = jnp.broadcast_to(flat_lists, (owners, flat_lists.shape[1]))
    lists_of = lax.all_to_all(lists_everywhere, "row", split_axis=0, concat_axis=0, tiled=True)
    mine = (lists_of >= 0) & (lists_of // per_device == me)
    asked = jnp.max(jnp.where(mine, lists_of % per_device, 0), axis=1)
    edges = [0, tile_size]
    state = ()
    previous = None
    for index, (start, stop) in enumerate(zip(edges[:-1], edges[1:])):
        sending = jnp.take(own_keys[:, start:stop], asked, axis=0)
        if previous is not None:
            previous, sending, state = lax.optimization_barrier((previous, sending, state))
        current = lax.all_to_all(sending, "row", split_axis=0, concat_axis=0, tiled=True)
        if previous is not None:
            state = attend_chunk(state, query_tiles, previous, slot_owner, counts, scale, index == 1, False)
        previous = current
    even = me % 2 == 0
    crossing = jnp.where(even, 0, 1).astype(jnp.int32).reshape(1)
    staying = (1 - crossing).astype(jnp.int32)
    crossing_tiles = attend_last_half(state, query_tiles, previous, slot_owner, counts, crossing, scale)
    crossing_tiles, later_queries = lax.optimization_barrier((crossing_tiles, query_tiles))
    staying_tiles = attend_last_half(state, later_queries, previous, slot_owner, counts, staying, scale)

    def to_rows(tiles):
        return tiles.reshape(per_device, -1, tile_cols, channels).transpose(1, 0, 2, 3).reshape(
            -1, band_width, channels
        )

    crossing_rows = to_rows(crossing_tiles)
    staying_rows = to_rows(staying_tiles)
    count = lax.axis_size("row")
    links = [(i, i + 1) for i in range(1, count - 1, 2)] + [(i + 1, i) for i in range(1, count - 1, 2)]
    across = lax.ppermute(crossing_rows, "row", links)
    same_chip = lax.ppermute(staying_rows, "row", [(i, i ^ 1) for i in range(count)])
    warped = jnp.where(
        even,
        jnp.concatenate([crossing_rows, staying_rows], axis=0),
        jnp.concatenate([staying_rows, crossing_rows], axis=0),
    )
    from_above = jnp.where(even, across, same_chip)
    from_below = jnp.where(even, same_chip, across)
    extended = jnp.concatenate([from_above, warped, from_below], axis=0)
    hidden = jax.nn.relu(native_conv(extended, conv_one)).astype(jnp.bfloat16)
    row_ids = jnp.arange(band_rows + 2)
    inside = ((row_ids > 0) | (me > 0)) & ((row_ids < band_rows + 1) | (me < owners - 1))
    hidden = jnp.where(inside[:, None, None], hidden, jnp.zeros_like(hidden))
    branch = native_conv(hidden, conv_two)
    return (frame_one.astype(jnp.float32) + branch).astype(jnp.bfloat16)


def solution(mesh):
    in_specs = (
        P(("pairs", "row"), None, None),
        P(("pairs", "row"), None, None),
        P(("pairs", "row"), None),
        P(),
        P(),
    )
    out_specs = P(("pairs", "row"), None, None)
    return jax.shard_map(
        on_device, mesh=mesh, in_specs=in_specs, out_specs=out_specs, check_vma=False
    )
```

```python
import functools

import jax
import jax.numpy as jnp
from jax import lax
from jax.experimental import pallas as pl
from jax.experimental.pallas import tpu as pltpu
from jax.sharding import PartitionSpec as P


def halo_rows(cells, axis, width):
    count = lax.axis_size(axis)
    even = lax.axis_index(axis) % 2 == 0
    head = cells[:width]
    tail = cells[cells.shape[0] - width :]
    same_chip = lax.ppermute(
        jnp.where(even, tail, head), axis, [(i, i ^ 1) for i in range(count)]
    )
    links = [(i, i + 1) for i in range(1, count - 1, 2)] + [(i + 1, i) for i in range(1, count - 1, 2)]
    across = lax.ppermute(jnp.where(even, head, tail), axis, links)
    from_above = jnp.where(even, across, same_chip)
    from_below = jnp.where(even, same_chip, across)
    return jnp.concatenate([from_above, cells, from_below], axis=0)


def convolve_rows(padded, weights, out_rows, out_cols):
    channels = padded.shape[2]
    summed = jnp.zeros((out_rows * out_cols, channels), jnp.float32)
    for row_shift in range(3):
        for col_shift in range(3):
            window = padded[row_shift : row_shift + out_rows, col_shift : col_shift + out_cols]
            window = window.reshape(out_rows * out_cols, channels)
            summed = summed + jnp.dot(
                window, weights[row_shift, col_shift], preferred_element_type=jnp.float32
            )
    return summed.reshape(out_rows, out_cols, channels)


def native_conv(rows, weights):
    out = lax.conv_general_dilated(
        rows[None],
        weights,
        window_strides=(1, 1),
        padding=((0, 0), (1, 1)),
        dimension_numbers=("NHWC", "HWIO", "NHWC"),
        preferred_element_type=jnp.float32,
    )
    return out[0]


def pad_columns(image):
    return jnp.pad(image, ((0, 0), (1, 1), (0, 0)))


def attend_kernel(owner_ref, count_ref, q_ref, k_ref, *refs, scale, first, last):
    if first:
        m_out, t_out, a_out, kall_ref = refs
    elif last:
        m_in, t_in, a_in, o_ref, kall_ref = refs
    else:
        m_in, t_in, a_in, m_out, t_out, a_out, kall_ref = refs
    t = pl.program_id(0)
    n = count_ref[t]
    slots = owner_ref.shape[1]
    span = k_ref.shape[1]
    lanes = 128
    for j in range(slots):
        kall_ref[j * span : (j + 1) * span, :] = k_ref[owner_ref[t, j]]
    q = q_ref[0]
    kall = kall_ref[...]
    s = lax.dot_general(q, kall, (((1,), (1,)), ((), ())), preferred_element_type=jnp.float32)
    penalty = [jnp.where(j < n, 0.0, jnp.inf).astype(jnp.float32) for j in range(slots)]
    blocks = [(j, j * span + c * lanes) for j in range(slots) for c in range(span // lanes)]
    mx = None
    for j, at in blocks:
        blk = s[:, at : at + lanes]
        mx = blk if mx is None else jnp.maximum(mx, blk)
    rows = q.shape[0]

    def column(row, width):
        return jnp.broadcast_to(row, (width, rows)).T

    m_new = jnp.max(mx.T, axis=0, keepdims=True) * scale
    if not first:
        m_old = m_in[0]
        m_new = jnp.maximum(m_old, m_new)
        alpha = jnp.exp(m_old - m_new)
    log2e = 1.4426950408889634
    mb = column(m_new * log2e, lanes)
    shifted = [mb + penalty[j] for j in range(slots)]
    acc = None
    ps = []
    for j, at in blocks:
        p = jnp.exp2(s[:, at : at + lanes] * (scale * log2e) - shifted[j])
        acc = p if acc is None else acc + p
        ps.append(p.astype(jnp.bfloat16))
    pb = jnp.concatenate(ps, axis=1)
    mixed = jnp.dot(pb, kall, preferred_element_type=jnp.float32)
    total = jnp.sum(acc.T, axis=0, keepdims=True)
    width = mixed.shape[1]
    if not first:
        mixed = a_in[0] * column(alpha, width) + mixed
        total = t_in[0] * alpha + total
    if last:
        o_ref[0] = (mixed / column(total, width)).astype(o_ref.dtype)
    else:
        m_out[0] = m_new
        t_out[0] = total
        a_out[0] = mixed


def attend_chunk(state, queries, chunk, slot_owner, counts, scale, first, last):
    tiles, tile_size, channels = queries.shape
    owners, chunk_len, _ = chunk.shape
    slots = slot_owner.shape[1]
    col_spec = pl.BlockSpec((1, 1, tile_size), lambda t, o, c: (t, 0, 0))
    acc_spec = pl.BlockSpec((1, tile_size, channels), lambda t, o, c: (t, 0, 0))
    state_specs = [] if first else [col_spec, col_spec, acc_spec]
    if last:
        out_specs = acc_spec
        out_shape = jax.ShapeDtypeStruct(queries.shape, jnp.bfloat16)
    else:
        out_specs = [col_spec, col_spec, acc_spec]
        out_shape = [
            jax.ShapeDtypeStruct((tiles, 1, tile_size), jnp.float32),
            jax.ShapeDtypeStruct((tiles, 1, tile_size), jnp.float32),
            jax.ShapeDtypeStruct((tiles, tile_size, channels), jnp.float32),
        ]
    grid_spec = pltpu.PrefetchScalarGridSpec(
        num_scalar_prefetch=2,
        grid=(tiles,),
        in_specs=[
            acc_spec,
            pl.BlockSpec((owners, chunk_len, channels), lambda t, o, c: (0, 0, 0)),
        ]
        + state_specs,
        out_specs=out_specs,
        scratch_shapes=[pltpu.VMEM((slots * chunk_len, channels), jnp.bfloat16)],
    )
    return pl.pallas_call(
        functools.partial(attend_kernel, scale=scale, first=first, last=last),
        grid_spec=grid_spec,
        out_shape=out_shape,
        compiler_params=pltpu.CompilerParams(vmem_limit_bytes=48 * 1024 * 1024),
    )(slot_owner, counts, queries, chunk, *([] if first else state))


def attend_last_half(state, queries, chunk, slot_owner, counts, half, scale):
    tiles, tile_size, channels = queries.shape
    owners, chunk_len, _ = chunk.shape
    slots = slot_owner.shape[1]
    part = tile_size // 2
    row_spec = pl.BlockSpec((1, 1, part), lambda t, o, c, h: (t, 0, h[0]))
    acc_spec = pl.BlockSpec((1, part, channels), lambda t, o, c, h: (t, h[0], 0))
    grid_spec = pltpu.PrefetchScalarGridSpec(
        num_scalar_prefetch=3,
        grid=(tiles,),
        in_specs=[
            acc_spec,
            pl.BlockSpec(memory_space=pltpu.MemorySpace.VMEM),
            row_spec,
            row_spec,
            acc_spec,
        ],
        out_specs=pl.BlockSpec((1, part, channels), lambda t, o, c, h: (t, 0, 0)),
        scratch_shapes=[pltpu.VMEM((slots * chunk_len, channels), jnp.bfloat16)],
    )

    def kernel(owner_ref, count_ref, half_ref, *refs):
        attend_kernel(owner_ref, count_ref, *refs, scale=scale, first=False, last=True)

    return pl.pallas_call(
        kernel,
        grid_spec=grid_spec,
        out_shape=jax.ShapeDtypeStruct((tiles, part, channels), jnp.bfloat16),
        compiler_params=pltpu.CompilerParams(vmem_limit_bytes=48 * 1024 * 1024),
    )(slot_owner, counts, half, queries, chunk, *state)


def on_device(frame_one, frame_two, tile_lists, conv_one, conv_two):
    band_rows, band_width, channels = frame_one.shape
    per_device = tile_lists.shape[0]
    tile_cols = band_width // per_device
    tile_size = band_rows * tile_cols
    owners = lax.axis_size("row")
    scale = float(channels) ** (-0.5)

    def band_to_tiles(band):
        return (
            band.reshape(band_rows, per_device, tile_cols, channels)
            .transpose(1, 0, 2, 3)
            .reshape(per_device, tile_size, channels)
        )

    query_tiles = band_to_tiles(frame_one)
    own_keys = band_to_tiles(frame_two)
    valid = tile_lists >= 0
    slot_owner = jnp.maximum(jnp.where(valid, tile_lists, tile_lists[:, :1]), 0) // per_device
    counts = jnp.sum(valid.astype(jnp.int32), axis=1)
    me = lax.axis_index("row")
    flat_lists = tile_lists.reshape(1, -1)
    lists_everywhere = jnp.broadcast_to(flat_lists, (owners, flat_lists.shape[1]))
    lists_of = lax.all_to_all(lists_everywhere, "row", split_axis=0, concat_axis=0, tiled=True)
    mine = (lists_of >= 0) & (lists_of // per_device == me)
    asked = jnp.max(jnp.where(mine, lists_of % per_device, 0), axis=1)
    edges = [0, tile_size // 2, tile_size]
    state = ()
    previous = None
    for index, (start, stop) in enumerate(zip(edges[:-1], edges[1:])):
        sending = jnp.take(own_keys[:, start:stop], asked, axis=0)
        if previous is not None:
            previous, sending, state = lax.optimization_barrier((previous, sending, state))
        current = lax.all_to_all(sending, "row", split_axis=0, concat_axis=0, tiled=True)
        if previous is not None:
            state = attend_chunk(state, query_tiles, previous, slot_owner, counts, scale, index == 1, False)
        previous = current
    even = me % 2 == 0
    crossing = jnp.where(even, 0, 1).astype(jnp.int32).reshape(1)
    staying = (1 - crossing).astype(jnp.int32)
    crossing_tiles = attend_last_half(state, query_tiles, previous, slot_owner, counts, crossing, scale)
    staying_tiles = attend_last_half(state, query_tiles, previous, slot_owner, counts, staying, scale)

    def to_rows(tiles):
        return tiles.reshape(per_device, -1, tile_cols, channels).transpose(1, 0, 2, 3).reshape(
            -1, band_width, channels
        )

    crossing_rows = to_rows(crossing_tiles)
    staying_rows = to_rows(staying_tiles)
    count = lax.axis_size("row")
    links = [(i, i + 1) for i in range(1, count - 1, 2)] + [(i + 1, i) for i in range(1, count - 1, 2)]
    across = lax.ppermute(crossing_rows, "row", links)
    same_chip = lax.ppermute(staying_rows, "row", [(i, i ^ 1) for i in range(count)])
    warped = jnp.where(
        even,
        jnp.concatenate([crossing_rows, staying_rows], axis=0),
        jnp.concatenate([staying_rows, crossing_rows], axis=0),
    )
    from_above = jnp.where(even, across, same_chip)
    from_below = jnp.where(even, same_chip, across)
    extended = jnp.concatenate([from_above, warped, from_below], axis=0)
    hidden = jax.nn.relu(native_conv(extended, conv_one)).astype(jnp.bfloat16)
    row_ids = jnp.arange(band_rows + 2)
    inside = ((row_ids > 0) | (me > 0)) & ((row_ids < band_rows + 1) | (me < owners - 1))
    hidden = jnp.where(inside[:, None, None], hidden, jnp.zeros_like(hidden))
    branch = native_conv(hidden, conv_two)
    return (frame_one.astype(jnp.float32) + branch).astype(jnp.bfloat16)


def solution(mesh):
    in_specs = (
        P(("pairs", "row"), None, None),
        P(("pairs", "row"), None, None),
        P(("pairs", "row"), None),
        P(),
        P(),
    )
    out_specs = P(("pairs", "row"), None, None)
    return jax.shard_map(
        on_device, mesh=mesh, in_specs=in_specs, out_specs=out_specs, check_vma=False
    )
```

```python
import functools

import jax
import jax.numpy as jnp
from jax import lax
from jax.experimental import pallas as pl
from jax.experimental.pallas import tpu as pltpu
from jax.sharding import PartitionSpec as P


def halo_rows(cells, axis, width):
    count = lax.axis_size(axis)
    even = lax.axis_index(axis) % 2 == 0
    head = cells[:width]
    tail = cells[cells.shape[0] - width :]
    same_chip = lax.ppermute(
        jnp.where(even, tail, head), axis, [(i, i ^ 1) for i in range(count)]
    )
    links = [(i, i + 1) for i in range(1, count - 1, 2)] + [(i + 1, i) for i in range(1, count - 1, 2)]
    across = lax.ppermute(jnp.where(even, head, tail), axis, links)
    from_above = jnp.where(even, across, same_chip)
    from_below = jnp.where(even, same_chip, across)
    return jnp.concatenate([from_above, cells, from_below], axis=0)


def convolve_rows(padded, weights, out_rows, out_cols):
    channels = padded.shape[2]
    summed = jnp.zeros((out_rows * out_cols, channels), jnp.float32)
    for row_shift in range(3):
        for col_shift in range(3):
            window = padded[row_shift : row_shift + out_rows, col_shift : col_shift + out_cols]
            window = window.reshape(out_rows * out_cols, channels)
            summed = summed + jnp.dot(
                window, weights[row_shift, col_shift], preferred_element_type=jnp.float32
            )
    return summed.reshape(out_rows, out_cols, channels)


def native_conv(rows, weights):
    out = lax.conv_general_dilated(
        rows[None],
        weights,
        window_strides=(1, 1),
        padding=((0, 0), (1, 1)),
        dimension_numbers=("NHWC", "HWIO", "NHWC"),
        preferred_element_type=jnp.float32,
    )
    return out[0]


def pad_columns(image):
    return jnp.pad(image, ((0, 0), (1, 1), (0, 0)))


def attend_kernel(owner_ref, count_ref, q_ref, k_ref, *refs, scale, first, last):
    if first:
        m_out, t_out, a_out, kall_ref = refs
    elif last:
        m_in, t_in, a_in, o_ref, kall_ref = refs
    else:
        m_in, t_in, a_in, m_out, t_out, a_out, kall_ref = refs
    t = pl.program_id(0)
    n = count_ref[t]
    slots = owner_ref.shape[1]
    span = k_ref.shape[1]
    lanes = 128
    for j in range(slots):
        kall_ref[j * span : (j + 1) * span, :] = k_ref[owner_ref[t, j]]
    q = q_ref[0]
    kall = kall_ref[...]
    s = lax.dot_general(q, kall, (((1,), (1,)), ((), ())), preferred_element_type=jnp.float32)
    penalty = [jnp.where(j < n, 0.0, jnp.inf).astype(jnp.float32) for j in range(slots)]
    blocks = [(j, j * span + c * lanes) for j in range(slots) for c in range(span // lanes)]
    mx = None
    for j, at in blocks:
        blk = s[:, at : at + lanes]
        mx = blk if mx is None else jnp.maximum(mx, blk)
    rows = q.shape[0]

    def column(row, width):
        return jnp.broadcast_to(row, (width, rows)).T

    m_new = jnp.max(mx.T, axis=0, keepdims=True) * scale
    if not first:
        m_old = m_in[0]
        m_new = jnp.maximum(m_old, m_new)
        alpha = jnp.exp(m_old - m_new)
    log2e = 1.4426950408889634
    mb = column(m_new * log2e, lanes)
    shifted = [mb + penalty[j] for j in range(slots)]
    acc = None
    ps = []
    for j, at in blocks:
        p = jnp.exp2(s[:, at : at + lanes] * (scale * log2e) - shifted[j])
        acc = p if acc is None else acc + p
        ps.append(p.astype(jnp.bfloat16))
    pb = jnp.concatenate(ps, axis=1)
    mixed = jnp.dot(pb, kall, preferred_element_type=jnp.float32)
    total = jnp.sum(acc.T, axis=0, keepdims=True)
    width = mixed.shape[1]
    if not first:
        mixed = a_in[0] * column(alpha, width) + mixed
        total = t_in[0] * alpha + total
    if last:
        o_ref[...] = (mixed / column(total, width)).astype(o_ref.dtype).reshape(o_ref.shape)
    else:
        m_out[0] = m_new
        t_out[0] = total
        a_out[0] = mixed


def attend_chunk(state, queries, chunk, slot_owner, counts, scale, first, last):
    tiles, tile_size, channels = queries.shape
    owners, chunk_len, _ = chunk.shape
    slots = slot_owner.shape[1]
    col_spec = pl.BlockSpec((1, 1, tile_size), lambda t, o, c: (t, 0, 0))
    acc_spec = pl.BlockSpec((1, tile_size, channels), lambda t, o, c: (t, 0, 0))
    state_specs = [] if first else [col_spec, col_spec, acc_spec]
    if last:
        out_specs = acc_spec
        out_shape = jax.ShapeDtypeStruct(queries.shape, jnp.bfloat16)
    else:
        out_specs = [col_spec, col_spec, acc_spec]
        out_shape = [
            jax.ShapeDtypeStruct((tiles, 1, tile_size), jnp.float32),
            jax.ShapeDtypeStruct((tiles, 1, tile_size), jnp.float32),
            jax.ShapeDtypeStruct((tiles, tile_size, channels), jnp.float32),
        ]
    grid_spec = pltpu.PrefetchScalarGridSpec(
        num_scalar_prefetch=2,
        grid=(tiles,),
        in_specs=[
            acc_spec,
            pl.BlockSpec((owners, chunk_len, channels), lambda t, o, c: (0, 0, 0)),
        ]
        + state_specs,
        out_specs=out_specs,
        scratch_shapes=[pltpu.VMEM((slots * chunk_len, channels), jnp.bfloat16)],
    )
    return pl.pallas_call(
        functools.partial(attend_kernel, scale=scale, first=first, last=last),
        grid_spec=grid_spec,
        out_shape=out_shape,
        compiler_params=pltpu.CompilerParams(vmem_limit_bytes=48 * 1024 * 1024),
    )(slot_owner, counts, queries, chunk, *([] if first else state))


def attend_last_half(state, queries, chunk, slot_owner, counts, half, scale, tile_cols):
    tiles, tile_size, channels = queries.shape
    owners, chunk_len, _ = chunk.shape
    slots = slot_owner.shape[1]
    part = tile_size // 2
    row_spec = pl.BlockSpec((1, 1, part), lambda t, o, c, h: (t, 0, h[0]))
    acc_spec = pl.BlockSpec((1, part, channels), lambda t, o, c, h: (t, h[0], 0))
    grid_spec = pltpu.PrefetchScalarGridSpec(
        num_scalar_prefetch=3,
        grid=(tiles,),
        in_specs=[
            acc_spec,
            pl.BlockSpec(memory_space=pltpu.MemorySpace.VMEM),
            row_spec,
            row_spec,
            acc_spec,
        ],
        out_specs=pl.BlockSpec((part // tile_cols, tile_cols, channels), lambda t, o, c, h: (0, t, 0)),
        scratch_shapes=[pltpu.VMEM((slots * chunk_len, channels), jnp.bfloat16)],
    )

    def kernel(owner_ref, count_ref, half_ref, *refs):
        attend_kernel(owner_ref, count_ref, *refs, scale=scale, first=False, last=True)

    return pl.pallas_call(
        kernel,
        grid_spec=grid_spec,
        out_shape=jax.ShapeDtypeStruct((part // tile_cols, tiles * tile_cols, channels), jnp.bfloat16),
        compiler_params=pltpu.CompilerParams(vmem_limit_bytes=48 * 1024 * 1024),
    )(slot_owner, counts, half, queries, chunk, *state)


def on_device(frame_one, frame_two, tile_lists, conv_one, conv_two):
    band_rows, band_width, channels = frame_one.shape
    per_device = tile_lists.shape[0]
    tile_cols = band_width // per_device
    tile_size = band_rows * tile_cols
    owners = lax.axis_size("row")
    scale = float(channels) ** (-0.5)

    def band_to_tiles(band):
        return (
            band.reshape(band_rows, per_device, tile_cols, channels)
            .transpose(1, 0, 2, 3)
            .reshape(per_device, tile_size, channels)
        )

    query_tiles = band_to_tiles(frame_one)
    own_keys = band_to_tiles(frame_two)
    valid = tile_lists >= 0
    slot_owner = jnp.maximum(jnp.where(valid, tile_lists, tile_lists[:, :1]), 0) // per_device
    counts = jnp.sum(valid.astype(jnp.int32), axis=1)
    me = lax.axis_index("row")
    flat_lists = tile_lists.reshape(1, -1)
    lists_everywhere = jnp.broadcast_to(flat_lists, (owners, flat_lists.shape[1]))
    lists_of = lax.all_to_all(lists_everywhere, "row", split_axis=0, concat_axis=0, tiled=True)
    mine = (lists_of >= 0) & (lists_of // per_device == me)
    asked = jnp.max(jnp.where(mine, lists_of % per_device, 0), axis=1)
    edges = [0, tile_size // 2, tile_size]
    state = ()
    previous = None
    for index, (start, stop) in enumerate(zip(edges[:-1], edges[1:])):
        sending = jnp.take(own_keys[:, start:stop], asked, axis=0)
        if previous is not None:
            previous, sending, state = lax.optimization_barrier((previous, sending, state))
        current = lax.all_to_all(sending, "row", split_axis=0, concat_axis=0, tiled=True)
        if previous is not None:
            state = attend_chunk(state, query_tiles, previous, slot_owner, counts, scale, index == 1, False)
        previous = current
    even = me % 2 == 0
    crossing = jnp.where(even, 0, 1).astype(jnp.int32).reshape(1)
    staying = (1 - crossing).astype(jnp.int32)
    crossing_rows = attend_last_half(
        state, query_tiles, previous, slot_owner, counts, crossing, scale, tile_cols
    )
    staying_rows = attend_last_half(
        state, query_tiles, previous, slot_owner, counts, staying, scale, tile_cols
    )

    count = lax.axis_size("row")
    links = [(i, i + 1) for i in range(1, count - 1, 2)] + [(i + 1, i) for i in range(1, count - 1, 2)]
    across = lax.ppermute(crossing_rows, "row", links)
    same_chip = lax.ppermute(staying_rows, "row", [(i, i ^ 1) for i in range(count)])
    warped = jnp.where(
        even,
        jnp.concatenate([crossing_rows, staying_rows], axis=0),
        jnp.concatenate([staying_rows, crossing_rows], axis=0),
    )
    from_above = jnp.where(even, across, same_chip)
    from_below = jnp.where(even, same_chip, across)
    extended = jnp.concatenate([from_above, warped, from_below], axis=0)
    hidden = jax.nn.relu(native_conv(extended, conv_one)).astype(jnp.bfloat16)
    row_ids = jnp.arange(band_rows + 2)
    inside = ((row_ids > 0) | (me > 0)) & ((row_ids < band_rows + 1) | (me < owners - 1))
    hidden = jnp.where(inside[:, None, None], hidden, jnp.zeros_like(hidden))
    branch = native_conv(hidden, conv_two)
    return (frame_one.astype(jnp.float32) + branch).astype(jnp.bfloat16)


def solution(mesh):
    in_specs = (
        P(("pairs", "row"), None, None),
        P(("pairs", "row"), None, None),
        P(("pairs", "row"), None),
        P(),
        P(),
    )
    out_specs = P(("pairs", "row"), None, None)
    return jax.shard_map(
        on_device, mesh=mesh, in_specs=in_specs, out_specs=out_specs, check_vma=False
    )
```

```python
import functools

import jax
import jax.numpy as jnp
from jax import lax
from jax.experimental import pallas as pl
from jax.experimental.pallas import tpu as pltpu
from jax.sharding import PartitionSpec as P


def halo_rows(cells, axis, width):
    count = lax.axis_size(axis)
    even = lax.axis_index(axis) % 2 == 0
    head = cells[:width]
    tail = cells[cells.shape[0] - width :]
    same_chip = lax.ppermute(
        jnp.where(even, tail, head), axis, [(i, i ^ 1) for i in range(count)]
    )
    links = [(i, i + 1) for i in range(1, count - 1, 2)] + [(i + 1, i) for i in range(1, count - 1, 2)]
    across = lax.ppermute(jnp.where(even, head, tail), axis, links)
    from_above = jnp.where(even, across, same_chip)
    from_below = jnp.where(even, same_chip, across)
    return jnp.concatenate([from_above, cells, from_below], axis=0)


def convolve_rows(padded, weights, out_rows, out_cols):
    channels = padded.shape[2]
    summed = jnp.zeros((out_rows * out_cols, channels), jnp.float32)
    for row_shift in range(3):
        for col_shift in range(3):
            window = padded[row_shift : row_shift + out_rows, col_shift : col_shift + out_cols]
            window = window.reshape(out_rows * out_cols, channels)
            summed = summed + jnp.dot(
                window, weights[row_shift, col_shift], preferred_element_type=jnp.float32
            )
    return summed.reshape(out_rows, out_cols, channels)


def native_conv(rows, weights):
    out = lax.conv_general_dilated(
        rows[None],
        weights,
        window_strides=(1, 1),
        padding=((0, 0), (1, 1)),
        dimension_numbers=("NHWC", "HWIO", "NHWC"),
        preferred_element_type=jnp.float32,
    )
    return out[0]


def pad_columns(image):
    return jnp.pad(image, ((0, 0), (1, 1), (0, 0)))


def attend_kernel(owner_ref, count_ref, q_ref, k_ref, *refs, scale, first, last):
    if first:
        m_out, t_out, a_out, kall_ref = refs
    elif last:
        m_in, t_in, a_in, o_ref, kall_ref = refs
    else:
        m_in, t_in, a_in, m_out, t_out, a_out, kall_ref = refs
    t = pl.program_id(0)
    n = count_ref[t]
    slots = owner_ref.shape[1]
    span = k_ref.shape[1]
    lanes = 128
    for j in range(slots):
        kall_ref[j * span : (j + 1) * span, :] = k_ref[owner_ref[t, j]]
    q = q_ref[0]
    kall = kall_ref[...]
    s = lax.dot_general(q, kall, (((1,), (1,)), ((), ())), preferred_element_type=jnp.float32)
    penalty = [jnp.where(j < n, 0.0, jnp.inf).astype(jnp.float32) for j in range(slots)]
    blocks = [(j, j * span + c * lanes) for j in range(slots) for c in range(span // lanes)]
    mx = None
    for j, at in blocks:
        blk = s[:, at : at + lanes]
        mx = blk if mx is None else jnp.maximum(mx, blk)
    rows = q.shape[0]

    def column(row, width):
        return jnp.broadcast_to(row, (width, rows)).T

    m_new = jnp.max(mx.T, axis=0, keepdims=True) * scale
    if not first:
        m_old = m_in[0]
        m_new = jnp.maximum(m_old, m_new)
        alpha = jnp.exp(m_old - m_new)
    log2e = 1.4426950408889634
    mb = column(m_new * log2e, lanes)
    shifted = [mb + penalty[j] for j in range(slots)]
    acc = None
    ps = []
    for j, at in blocks:
        p = jnp.exp2(s[:, at : at + lanes] * (scale * log2e) - shifted[j])
        acc = p if acc is None else acc + p
        ps.append(p.astype(jnp.bfloat16))
    pb = jnp.concatenate(ps, axis=1)
    mixed = jnp.dot(pb, kall, preferred_element_type=jnp.float32)
    total = jnp.sum(acc.T, axis=0, keepdims=True)
    width = mixed.shape[1]
    if not first:
        mixed = a_in[0] * column(alpha, width) + mixed
        total = t_in[0] * alpha + total
    if last:
        o_ref[0] = (mixed / column(total, width)).astype(o_ref.dtype)
    else:
        m_out[0] = m_new
        t_out[0] = total
        a_out[0] = mixed


def attend_chunk(state, queries, chunk, slot_owner, counts, scale, first, last):
    tiles, tile_size, channels = queries.shape
    owners, chunk_len, _ = chunk.shape
    slots = slot_owner.shape[1]
    col_spec = pl.BlockSpec((1, 1, tile_size), lambda t, o, c: (t, 0, 0))
    acc_spec = pl.BlockSpec((1, tile_size, channels), lambda t, o, c: (t, 0, 0))
    state_specs = [] if first else [col_spec, col_spec, acc_spec]
    if last:
        out_specs = acc_spec
        out_shape = jax.ShapeDtypeStruct(queries.shape, jnp.bfloat16)
    else:
        out_specs = [col_spec, col_spec, acc_spec]
        out_shape = [
            jax.ShapeDtypeStruct((tiles, 1, tile_size), jnp.float32),
            jax.ShapeDtypeStruct((tiles, 1, tile_size), jnp.float32),
            jax.ShapeDtypeStruct((tiles, tile_size, channels), jnp.float32),
        ]
    grid_spec = pltpu.PrefetchScalarGridSpec(
        num_scalar_prefetch=2,
        grid=(tiles,),
        in_specs=[
            acc_spec,
            pl.BlockSpec((owners, chunk_len, channels), lambda t, o, c: (0, 0, 0)),
        ]
        + state_specs,
        out_specs=out_specs,
        scratch_shapes=[pltpu.VMEM((slots * chunk_len, channels), jnp.bfloat16)],
    )
    return pl.pallas_call(
        functools.partial(attend_kernel, scale=scale, first=first, last=last),
        grid_spec=grid_spec,
        out_shape=out_shape,
        compiler_params=pltpu.CompilerParams(vmem_limit_bytes=48 * 1024 * 1024),
    )(slot_owner, counts, queries, chunk, *([] if first else state))


def attend_last_half(state, queries, chunk, slot_owner, counts, half, scale):
    tiles, tile_size, channels = queries.shape
    owners, chunk_len, _ = chunk.shape
    slots = slot_owner.shape[1]
    part = tile_size // 2
    row_spec = pl.BlockSpec((1, 1, part), lambda t, o, c, h: (t, 0, h[0]))
    acc_spec = pl.BlockSpec((1, part, channels), lambda t, o, c, h: (t, h[0], 0))
    grid_spec = pltpu.PrefetchScalarGridSpec(
        num_scalar_prefetch=3,
        grid=(tiles,),
        in_specs=[
            acc_spec,
            pl.BlockSpec(memory_space=pltpu.MemorySpace.VMEM),
            row_spec,
            row_spec,
            acc_spec,
        ],
        out_specs=pl.BlockSpec((1, part, channels), lambda t, o, c, h: (t, 0, 0)),
        scratch_shapes=[pltpu.VMEM((slots * chunk_len, channels), jnp.bfloat16)],
    )

    def kernel(owner_ref, count_ref, half_ref, *refs):
        attend_kernel(owner_ref, count_ref, *refs, scale=scale, first=False, last=True)

    return pl.pallas_call(
        kernel,
        grid_spec=grid_spec,
        out_shape=jax.ShapeDtypeStruct((tiles, part, channels), jnp.bfloat16),
        compiler_params=pltpu.CompilerParams(vmem_limit_bytes=48 * 1024 * 1024),
    )(slot_owner, counts, half, queries, chunk, *state)


def on_device(frame_one, frame_two, tile_lists, conv_one, conv_two):
    band_rows, band_width, channels = frame_one.shape
    per_device = tile_lists.shape[0]
    tile_cols = band_width // per_device
    tile_size = band_rows * tile_cols
    owners = lax.axis_size("row")
    scale = float(channels) ** (-0.5)

    def band_to_tiles(band):
        return (
            band.reshape(band_rows, per_device, tile_cols, channels)
            .transpose(1, 0, 2, 3)
            .reshape(per_device, tile_size, channels)
        )

    query_tiles = band_to_tiles(frame_one)
    own_keys = band_to_tiles(frame_two)
    valid = tile_lists >= 0
    slot_owner = jnp.maximum(jnp.where(valid, tile_lists, tile_lists[:, :1]), 0) // per_device
    counts = jnp.sum(valid.astype(jnp.int32), axis=1)
    me = lax.axis_index("row")
    flat_lists = tile_lists.reshape(1, -1)
    lists_everywhere = jnp.broadcast_to(flat_lists, (owners, flat_lists.shape[1]))
    lists_of = lax.all_to_all(lists_everywhere, "row", split_axis=0, concat_axis=0, tiled=True)
    mine = (lists_of >= 0) & (lists_of // per_device == me)
    asked = jnp.max(jnp.where(mine, lists_of % per_device, 0), axis=1)
    edges = [0, tile_size // 2, tile_size]
    state = ()
    previous = None
    for index, (start, stop) in enumerate(zip(edges[:-1], edges[1:])):
        sending = jnp.take(own_keys[:, start:stop], asked, axis=0)
        if previous is not None:
            previous, sending, state = lax.optimization_barrier((previous, sending, state))
        current = lax.all_to_all(sending, "row", split_axis=0, concat_axis=0, tiled=True)
        if previous is not None:
            state = attend_chunk(state, query_tiles, previous, slot_owner, counts, scale, index == 1, False)
        previous = current
    even = me % 2 == 0
    crossing = jnp.where(even, 0, 1).astype(jnp.int32).reshape(1)
    staying = (1 - crossing).astype(jnp.int32)
    crossing_tiles = attend_last_half(state, query_tiles, previous, slot_owner, counts, crossing, scale)
    staying_tiles = attend_last_half(state, query_tiles, previous, slot_owner, counts, staying, scale)

    def to_rows(tiles):
        return tiles.reshape(per_device, -1, tile_cols, channels).transpose(1, 0, 2, 3).reshape(
            -1, band_width, channels
        )

    crossing_rows = to_rows(crossing_tiles)
    staying_rows = to_rows(staying_tiles)
    count = lax.axis_size("row")
    links = [(i, i + 1) for i in range(1, count - 1, 2)] + [(i + 1, i) for i in range(1, count - 1, 2)]
    across = lax.ppermute(crossing_rows, "row", links)
    same_chip = lax.ppermute(staying_rows, "row", [(i, i ^ 1) for i in range(count)])
    warped = jnp.where(
        even,
        jnp.concatenate([crossing_rows, staying_rows], axis=0),
        jnp.concatenate([staying_rows, crossing_rows], axis=0),
    )
    from_above = jnp.where(even, across, same_chip)
    from_below = jnp.where(even, same_chip, across)
    extended = jnp.concatenate([from_above, warped, from_below], axis=0)
    hidden = jax.nn.relu(native_conv(extended, conv_one)).astype(jnp.bfloat16)
    row_ids = jnp.arange(band_rows + 2)
    inside = ((row_ids > 0) | (me > 0)) & ((row_ids < band_rows + 1) | (me < owners - 1))
    hidden = jnp.where(inside[:, None, None], hidden, jnp.zeros_like(hidden))
    taps = conv_two.shape[0]
    centre = (jnp.arange(taps)[:, None] == taps // 2) & (jnp.arange(taps)[None, :] == taps // 2)
    identity = (centre[:, :, None, None] & jnp.eye(channels, dtype=bool)[None, None]).astype(conv_two.dtype)
    weights = jnp.concatenate([conv_two, identity], axis=2)
    residual = jnp.pad(frame_one, ((1, 1), (0, 0), (0, 0)))
    stacked = jnp.concatenate([hidden, residual], axis=2)
    return native_conv(stacked, weights).astype(jnp.bfloat16)


def solution(mesh):
    in_specs = (
        P(("pairs", "row"), None, None),
        P(("pairs", "row"), None, None),
        P(("pairs", "row"), None),
        P(),
        P(),
    )
    out_specs = P(("pairs", "row"), None, None)
    return jax.shard_map(
        on_device, mesh=mesh, in_specs=in_specs, out_specs=out_specs, check_vma=False
    )
```

```python
import functools

import jax
import jax.numpy as jnp
from jax import lax
from jax.experimental import pallas as pl
from jax.experimental.pallas import tpu as pltpu
from jax.sharding import PartitionSpec as P


def halo_rows(cells, axis, width):
    count = lax.axis_size(axis)
    even = lax.axis_index(axis) % 2 == 0
    head = cells[:width]
    tail = cells[cells.shape[0] - width :]
    same_chip = lax.ppermute(
        jnp.where(even, tail, head), axis, [(i, i ^ 1) for i in range(count)]
    )
    links = [(i, i + 1) for i in range(1, count - 1, 2)] + [(i + 1, i) for i in range(1, count - 1, 2)]
    across = lax.ppermute(jnp.where(even, head, tail), axis, links)
    from_above = jnp.where(even, across, same_chip)
    from_below = jnp.where(even, same_chip, across)
    return jnp.concatenate([from_above, cells, from_below], axis=0)


def convolve_rows(padded, weights, out_rows, out_cols):
    channels = padded.shape[2]
    summed = jnp.zeros((out_rows * out_cols, channels), jnp.float32)
    for row_shift in range(3):
        for col_shift in range(3):
            window = padded[row_shift : row_shift + out_rows, col_shift : col_shift + out_cols]
            window = window.reshape(out_rows * out_cols, channels)
            summed = summed + jnp.dot(
                window, weights[row_shift, col_shift], preferred_element_type=jnp.float32
            )
    return summed.reshape(out_rows, out_cols, channels)


def native_conv(rows, weights):
    out = lax.conv_general_dilated(
        rows[None],
        weights,
        window_strides=(1, 1),
        padding=((0, 0), (1, 1)),
        dimension_numbers=("NHWC", "HWIO", "NHWC"),
        preferred_element_type=jnp.float32,
    )
    return out[0]


def pad_columns(image):
    return jnp.pad(image, ((0, 0), (1, 1), (0, 0)))


def attend_kernel(owner_ref, count_ref, q_ref, k_ref, *refs, scale, first, last):
    if first:
        m_out, t_out, a_out, kall_ref = refs
    elif last:
        m_in, t_in, a_in, o_ref, kall_ref = refs
    else:
        m_in, t_in, a_in, m_out, t_out, a_out, kall_ref = refs
    t = pl.program_id(0)
    n = count_ref[t]
    slots = owner_ref.shape[1]
    span = k_ref.shape[1]
    lanes = 128
    for j in range(slots):
        kall_ref[j * span : (j + 1) * span, :] = k_ref[owner_ref[t, j]]
    q = q_ref[0]
    kall = kall_ref[...]
    s = lax.dot_general(q, kall, (((1,), (1,)), ((), ())), preferred_element_type=jnp.float32)
    penalty = [jnp.where(j < n, 0.0, jnp.inf).astype(jnp.float32) for j in range(slots)]
    blocks = [(j, j * span + c * lanes) for j in range(slots) for c in range(span // lanes)]
    mx = None
    for j, at in blocks:
        blk = s[:, at : at + lanes]
        mx = blk if mx is None else jnp.maximum(mx, blk)
    rows = q.shape[0]

    def column(row, width):
        return jnp.broadcast_to(row, (width, rows)).T

    m_new = jnp.max(mx.T, axis=0, keepdims=True) * scale
    if not first:
        m_old = m_in[0]
        m_new = jnp.maximum(m_old, m_new)
        alpha = jnp.exp(m_old - m_new)
    log2e = 1.4426950408889634
    mb = column(m_new * log2e, lanes)
    shifted = [mb + penalty[j] for j in range(slots)]
    acc = None
    ps = []
    for j, at in blocks:
        p = jnp.exp2(s[:, at : at + lanes] * (scale * log2e) - shifted[j])
        acc = p if acc is None else acc + p
        ps.append(p.astype(jnp.bfloat16))
    pb = jnp.concatenate(ps, axis=1)
    mixed = jnp.dot(pb, kall, preferred_element_type=jnp.float32)
    total = jnp.sum(acc.T, axis=0, keepdims=True)
    width = mixed.shape[1]
    if not first:
        mixed = a_in[0] * column(alpha, width) + mixed
        total = t_in[0] * alpha + total
    if last:
        o_ref[0] = (mixed / column(total, width)).astype(o_ref.dtype)
    else:
        m_out[0] = m_new
        t_out[0] = total
        a_out[0] = mixed


def attend_chunk(state, queries, chunk, slot_owner, counts, scale, first, last):
    tiles, tile_size, channels = queries.shape
    owners, chunk_len, _ = chunk.shape
    slots = slot_owner.shape[1]
    col_spec = pl.BlockSpec((1, 1, tile_size), lambda t, o, c: (t, 0, 0))
    acc_spec = pl.BlockSpec((1, tile_size, channels), lambda t, o, c: (t, 0, 0))
    state_specs = [] if first else [col_spec, col_spec, acc_spec]
    if last:
        out_specs = acc_spec
        out_shape = jax.ShapeDtypeStruct(queries.shape, jnp.bfloat16)
    else:
        out_specs = [col_spec, col_spec, acc_spec]
        out_shape = [
            jax.ShapeDtypeStruct((tiles, 1, tile_size), jnp.float32),
            jax.ShapeDtypeStruct((tiles, 1, tile_size), jnp.float32),
            jax.ShapeDtypeStruct((tiles, tile_size, channels), jnp.float32),
        ]
    grid_spec = pltpu.PrefetchScalarGridSpec(
        num_scalar_prefetch=2,
        grid=(tiles,),
        in_specs=[
            acc_spec,
            pl.BlockSpec((owners, chunk_len, channels), lambda t, o, c: (0, 0, 0)),
        ]
        + state_specs,
        out_specs=out_specs,
        scratch_shapes=[pltpu.VMEM((slots * chunk_len, channels), jnp.bfloat16)],
    )
    return pl.pallas_call(
        functools.partial(attend_kernel, scale=scale, first=first, last=last),
        grid_spec=grid_spec,
        out_shape=out_shape,
        compiler_params=pltpu.CompilerParams(vmem_limit_bytes=48 * 1024 * 1024),
    )(slot_owner, counts, queries, chunk, *([] if first else state))


def attend_last_half(state, queries, chunk, slot_owner, counts, half, scale):
    tiles, tile_size, channels = queries.shape
    owners, chunk_len, _ = chunk.shape
    slots = slot_owner.shape[1]
    part = tile_size // 2
    row_spec = pl.BlockSpec((1, 1, part), lambda t, o, c, h: (t, 0, h[0]))
    acc_spec = pl.BlockSpec((1, part, channels), lambda t, o, c, h: (t, h[0], 0))
    grid_spec = pltpu.PrefetchScalarGridSpec(
        num_scalar_prefetch=3,
        grid=(tiles,),
        in_specs=[
            acc_spec,
            pl.BlockSpec(memory_space=pltpu.MemorySpace.VMEM),
            row_spec,
            row_spec,
            acc_spec,
        ],
        out_specs=pl.BlockSpec((1, part, channels), lambda t, o, c, h: (t, 0, 0)),
        scratch_shapes=[pltpu.VMEM((slots * chunk_len, channels), jnp.bfloat16)],
    )

    def kernel(owner_ref, count_ref, half_ref, *refs):
        attend_kernel(owner_ref, count_ref, *refs, scale=scale, first=False, last=True)

    return pl.pallas_call(
        kernel,
        grid_spec=grid_spec,
        out_shape=jax.ShapeDtypeStruct((tiles, part, channels), jnp.bfloat16),
        compiler_params=pltpu.CompilerParams(vmem_limit_bytes=48 * 1024 * 1024),
    )(slot_owner, counts, half, queries, chunk, *state)


def on_device(frame_one, frame_two, tile_lists, conv_one, conv_two):
    band_rows, band_width, channels = frame_one.shape
    per_device = tile_lists.shape[0]
    tile_cols = band_width // per_device
    tile_size = band_rows * tile_cols
    owners = lax.axis_size("row")
    scale = float(channels) ** (-0.5)

    def band_to_tiles(band):
        return (
            band.reshape(band_rows, per_device, tile_cols, channels)
            .transpose(1, 0, 2, 3)
            .reshape(per_device, tile_size, channels)
        )

    query_tiles = band_to_tiles(frame_one)
    own_keys = band_to_tiles(frame_two)
    valid = tile_lists >= 0
    slot_owner = jnp.maximum(jnp.where(valid, tile_lists, tile_lists[:, :1]), 0) // per_device
    counts = jnp.sum(valid.astype(jnp.int32), axis=1)
    me = lax.axis_index("row")
    flat_lists = tile_lists.reshape(1, -1)
    lists_everywhere = jnp.broadcast_to(flat_lists, (owners, flat_lists.shape[1]))
    lists_of = lax.all_to_all(lists_everywhere, "row", split_axis=0, concat_axis=0, tiled=True)
    mine = (lists_of >= 0) & (lists_of // per_device == me)
    asked = jnp.max(jnp.where(mine, lists_of % per_device, 0), axis=1)
    edges = [0, tile_size // 2, tile_size]
    state = ()
    previous = None
    for index, (start, stop) in enumerate(zip(edges[:-1], edges[1:])):
        sending = jnp.take(own_keys[:, start:stop], asked, axis=0, mode="clip")
        if previous is not None:
            previous, sending, state = lax.optimization_barrier((previous, sending, state))
        current = lax.all_to_all(sending, "row", split_axis=0, concat_axis=0, tiled=True)
        if previous is not None:
            state = attend_chunk(state, query_tiles, previous, slot_owner, counts, scale, index == 1, False)
        previous = current
    even = me % 2 == 0
    crossing = jnp.where(even, 0, 1).astype(jnp.int32).reshape(1)
    staying = (1 - crossing).astype(jnp.int32)
    crossing_tiles = attend_last_half(state, query_tiles, previous, slot_owner, counts, crossing, scale)
    staying_tiles = attend_last_half(state, query_tiles, previous, slot_owner, counts, staying, scale)

    def to_rows(tiles):
        return tiles.reshape(per_device, -1, tile_cols, channels).transpose(1, 0, 2, 3).reshape(
            -1, band_width, channels
        )

    crossing_rows = to_rows(crossing_tiles)
    staying_rows = to_rows(staying_tiles)
    count = lax.axis_size("row")
    links = [(i, i + 1) for i in range(1, count - 1, 2)] + [(i + 1, i) for i in range(1, count - 1, 2)]
    across = lax.ppermute(crossing_rows, "row", links)
    same_chip = lax.ppermute(staying_rows, "row", [(i, i ^ 1) for i in range(count)])
    warped = jnp.where(
        even,
        jnp.concatenate([crossing_rows, staying_rows], axis=0),
        jnp.concatenate([staying_rows, crossing_rows], axis=0),
    )
    from_above = jnp.where(even, across, same_chip)
    from_below = jnp.where(even, same_chip, across)
    extended = jnp.concatenate([from_above, warped, from_below], axis=0)
    hidden = jax.nn.relu(native_conv(extended, conv_one)).astype(jnp.bfloat16)
    row_ids = jnp.arange(band_rows + 2)
    inside = ((row_ids > 0) | (me > 0)) & ((row_ids < band_rows + 1) | (me < owners - 1))
    hidden = jnp.where(inside[:, None, None], hidden, jnp.zeros_like(hidden))
    branch = native_conv(hidden, conv_two)
    return (frame_one.astype(jnp.float32) + branch).astype(jnp.bfloat16)


def solution(mesh):
    in_specs = (
        P(("pairs", "row"), None, None),
        P(("pairs", "row"), None, None),
        P(("pairs", "row"), None),
        P(),
        P(),
    )
    out_specs = P(("pairs", "row"), None, None)
    return jax.shard_map(
        on_device, mesh=mesh, in_specs=in_specs, out_specs=out_specs, check_vma=False
    )
```

```python
import functools

import jax
import jax.numpy as jnp
from jax import lax
from jax.experimental import pallas as pl
from jax.experimental.pallas import tpu as pltpu
from jax.sharding import PartitionSpec as P


def halo_rows(cells, axis, width):
    count = lax.axis_size(axis)
    even = lax.axis_index(axis) % 2 == 0
    head = cells[:width]
    tail = cells[cells.shape[0] - width :]
    same_chip = lax.ppermute(
        jnp.where(even, tail, head), axis, [(i, i ^ 1) for i in range(count)]
    )
    links = [(i, i + 1) for i in range(1, count - 1, 2)] + [(i + 1, i) for i in range(1, count - 1, 2)]
    across = lax.ppermute(jnp.where(even, head, tail), axis, links)
    from_above = jnp.where(even, across, same_chip)
    from_below = jnp.where(even, same_chip, across)
    return jnp.concatenate([from_above, cells, from_below], axis=0)


def convolve_rows(padded, weights, out_rows, out_cols):
    channels = padded.shape[2]
    summed = jnp.zeros((out_rows * out_cols, channels), jnp.float32)
    for row_shift in range(3):
        for col_shift in range(3):
            window = padded[row_shift : row_shift + out_rows, col_shift : col_shift + out_cols]
            window = window.reshape(out_rows * out_cols, channels)
            summed = summed + jnp.dot(
                window, weights[row_shift, col_shift], preferred_element_type=jnp.float32
            )
    return summed.reshape(out_rows, out_cols, channels)


def native_conv(rows, weights):
    out = lax.conv_general_dilated(
        rows[None],
        weights,
        window_strides=(1, 1),
        padding=((0, 0), (1, 1)),
        dimension_numbers=("NHWC", "HWIO", "NHWC"),
        preferred_element_type=jnp.float32,
    )
    return out[0]


def pad_columns(image):
    return jnp.pad(image, ((0, 0), (1, 1), (0, 0)))


def attend_kernel(owner_ref, count_ref, q_ref, k_ref, *refs, scale, first, last):
    if first:
        m_out, t_out, a_out, kall_ref = refs
    elif last:
        m_in, t_in, a_in, o_ref, kall_ref = refs
    else:
        m_in, t_in, a_in, m_out, t_out, a_out, kall_ref = refs
    t = pl.program_id(0)
    n = count_ref[t]
    slots = owner_ref.shape[1]
    span = k_ref.shape[1]
    lanes = 128
    for j in range(slots):
        kall_ref[j * span : (j + 1) * span, :] = k_ref[owner_ref[t, j]]
    q = q_ref[0]
    kall = kall_ref[...]
    s = lax.dot_general(q, kall, (((1,), (1,)), ((), ())), preferred_element_type=jnp.float32)
    penalty = [jnp.where(j < n, 0.0, jnp.inf).astype(jnp.float32) for j in range(slots)]
    blocks = [(j, j * span + c * lanes) for j in range(slots) for c in range(span // lanes)]
    mx = None
    for j, at in blocks:
        blk = s[:, at : at + lanes]
        mx = blk if mx is None else jnp.maximum(mx, blk)
    rows = q.shape[0]

    def column(row, width):
        return jnp.broadcast_to(row, (width, rows)).T

    m_new = jnp.max(mx.T, axis=0, keepdims=True) * scale
    if not first:
        m_old = m_in[0]
        m_new = jnp.maximum(m_old, m_new)
        alpha = jnp.exp(m_old - m_new)
    log2e = 1.4426950408889634
    mb = column(m_new * log2e, lanes)
    shifted = [mb + penalty[j] for j in range(slots)]
    acc = None
    ps = []
    for j, at in blocks:
        p = jnp.exp2(s[:, at : at + lanes] * (scale * log2e) - shifted[j])
        acc = p if acc is None else acc + p
        ps.append(p.astype(jnp.bfloat16))
    pb = jnp.concatenate(ps, axis=1)
    mixed = jnp.dot(pb, kall, preferred_element_type=jnp.float32)
    total = jnp.sum(acc.T, axis=0, keepdims=True)
    width = mixed.shape[1]
    if not first:
        mixed = a_in[0] * column(alpha, width) + mixed
        total = t_in[0] * alpha + total
    if last:
        o_ref[0] = (mixed / column(total, width)).astype(o_ref.dtype)
    else:
        m_out[0] = m_new
        t_out[0] = total
        a_out[0] = mixed


def attend_chunk(state, queries, chunk, slot_owner, counts, scale, first, last):
    tiles, tile_size, channels = queries.shape
    owners, chunk_len, _ = chunk.shape
    slots = slot_owner.shape[1]
    col_spec = pl.BlockSpec((1, 1, tile_size), lambda t, o, c: (t, 0, 0))
    acc_spec = pl.BlockSpec((1, tile_size, channels), lambda t, o, c: (t, 0, 0))
    state_specs = [] if first else [col_spec, col_spec, acc_spec]
    if last:
        out_specs = acc_spec
        out_shape = jax.ShapeDtypeStruct(queries.shape, jnp.bfloat16)
    else:
        out_specs = [col_spec, col_spec, acc_spec]
        out_shape = [
            jax.ShapeDtypeStruct((tiles, 1, tile_size), jnp.float32),
            jax.ShapeDtypeStruct((tiles, 1, tile_size), jnp.float32),
            jax.ShapeDtypeStruct((tiles, tile_size, channels), jnp.float32),
        ]
    grid_spec = pltpu.PrefetchScalarGridSpec(
        num_scalar_prefetch=2,
        grid=(tiles,),
        in_specs=[
            acc_spec,
            pl.BlockSpec((owners, chunk_len, channels), lambda t, o, c: (0, 0, 0)),
        ]
        + state_specs,
        out_specs=out_specs,
        scratch_shapes=[pltpu.VMEM((slots * chunk_len, channels), jnp.bfloat16)],
    )
    return pl.pallas_call(
        functools.partial(attend_kernel, scale=scale, first=first, last=last),
        grid_spec=grid_spec,
        out_shape=out_shape,
        compiler_params=pltpu.CompilerParams(vmem_limit_bytes=48 * 1024 * 1024),
    )(slot_owner, counts, queries, chunk, *([] if first else state))


def attend_last_half(state, queries, chunk, slot_owner, counts, half, scale):
    tiles, tile_size, channels = queries.shape
    owners, chunk_len, _ = chunk.shape
    slots = slot_owner.shape[1]
    part = tile_size // 2
    row_spec = pl.BlockSpec((1, 1, part), lambda t, o, c, h: (t, 0, h[0]))
    acc_spec = pl.BlockSpec((1, part, channels), lambda t, o, c, h: (t, h[0], 0))
    grid_spec = pltpu.PrefetchScalarGridSpec(
        num_scalar_prefetch=3,
        grid=(tiles,),
        in_specs=[
            acc_spec,
            pl.BlockSpec(memory_space=pltpu.MemorySpace.VMEM),
            row_spec,
            row_spec,
            acc_spec,
        ],
        out_specs=pl.BlockSpec((1, part, channels), lambda t, o, c, h: (t, 0, 0)),
        scratch_shapes=[pltpu.VMEM((slots * chunk_len, channels), jnp.bfloat16)],
    )

    def kernel(owner_ref, count_ref, half_ref, *refs):
        attend_kernel(owner_ref, count_ref, *refs, scale=scale, first=False, last=True)

    return pl.pallas_call(
        kernel,
        grid_spec=grid_spec,
        out_shape=jax.ShapeDtypeStruct((tiles, part, channels), jnp.bfloat16),
        compiler_params=pltpu.CompilerParams(vmem_limit_bytes=48 * 1024 * 1024),
    )(slot_owner, counts, half, queries, chunk, *state)


def on_device(frame_one, frame_two, tile_lists, conv_one, conv_two):
    band_rows, band_width, channels = frame_one.shape
    per_device = tile_lists.shape[0]
    tile_cols = band_width // per_device
    tile_size = band_rows * tile_cols
    owners = lax.axis_size("row")
    scale = float(channels) ** (-0.5)

    def band_to_tiles(band):
        return (
            band.reshape(band_rows, per_device, tile_cols, channels)
            .transpose(1, 0, 2, 3)
            .reshape(per_device, tile_size, channels)
        )

    query_tiles = band_to_tiles(frame_one)
    own_keys = band_to_tiles(frame_two)
    valid = tile_lists >= 0
    slot_owner = jnp.maximum(jnp.where(valid, tile_lists, tile_lists[:, :1]), 0) // per_device
    counts = jnp.sum(valid.astype(jnp.int32), axis=1)
    me = lax.axis_index("row")
    flat_lists = tile_lists.reshape(1, -1)
    lists_everywhere = jnp.broadcast_to(flat_lists, (owners, flat_lists.shape[1]))
    lists_of = lax.all_to_all(lists_everywhere, "row", split_axis=0, concat_axis=0, tiled=True)
    mine = (lists_of >= 0) & (lists_of // per_device == me)
    asked = jnp.max(jnp.where(mine, lists_of % per_device, 0), axis=1)
    edges = [0, tile_size // 2, tile_size]
    state = ()
    previous = None
    for index, (start, stop) in enumerate(zip(edges[:-1], edges[1:])):
        part = own_keys[:, start:stop]
        sending = jnp.broadcast_to(part[0][None], (owners,) + part.shape[1:])
        for local in range(1, per_device):
            sending = jnp.where((asked == local)[:, None, None], part[local][None], sending)
        if previous is not None:
            previous, sending, state = lax.optimization_barrier((previous, sending, state))
        current = lax.all_to_all(sending, "row", split_axis=0, concat_axis=0, tiled=True)
        if previous is not None:
            state = attend_chunk(state, query_tiles, previous, slot_owner, counts, scale, index == 1, False)
        previous = current
    even = me % 2 == 0
    crossing = jnp.where(even, 0, 1).astype(jnp.int32).reshape(1)
    staying = (1 - crossing).astype(jnp.int32)
    crossing_tiles = attend_last_half(state, query_tiles, previous, slot_owner, counts, crossing, scale)
    staying_tiles = attend_last_half(state, query_tiles, previous, slot_owner, counts, staying, scale)

    def to_rows(tiles):
        return tiles.reshape(per_device, -1, tile_cols, channels).transpose(1, 0, 2, 3).reshape(
            -1, band_width, channels
        )

    crossing_rows = to_rows(crossing_tiles)
    staying_rows = to_rows(staying_tiles)
    count = lax.axis_size("row")
    links = [(i, i + 1) for i in range(1, count - 1, 2)] + [(i + 1, i) for i in range(1, count - 1, 2)]
    across = lax.ppermute(crossing_rows, "row", links)
    same_chip = lax.ppermute(staying_rows, "row", [(i, i ^ 1) for i in range(count)])
    warped = jnp.where(
        even,
        jnp.concatenate([crossing_rows, staying_rows], axis=0),
        jnp.concatenate([staying_rows, crossing_rows], axis=0),
    )
    from_above = jnp.where(even, across, same_chip)
    from_below = jnp.where(even, same_chip, across)
    extended = jnp.concatenate([from_above, warped, from_below], axis=0)
    hidden = jax.nn.relu(native_conv(extended, conv_one)).astype(jnp.bfloat16)
    row_ids = jnp.arange(band_rows + 2)
    inside = ((row_ids > 0) | (me > 0)) & ((row_ids < band_rows + 1) | (me < owners - 1))
    hidden = jnp.where(inside[:, None, None], hidden, jnp.zeros_like(hidden))
    branch = native_conv(hidden, conv_two)
    return (frame_one.astype(jnp.float32) + branch).astype(jnp.bfloat16)


def solution(mesh):
    in_specs = (
        P(("pairs", "row"), None, None),
        P(("pairs", "row"), None, None),
        P(("pairs", "row"), None),
        P(),
        P(),
    )
    out_specs = P(("pairs", "row"), None, None)
    return jax.shard_map(
        on_device, mesh=mesh, in_specs=in_specs, out_specs=out_specs, check_vma=False
    )
```

```python
import functools

import jax
import jax.numpy as jnp
from jax import lax
from jax.experimental import pallas as pl
from jax.experimental.pallas import tpu as pltpu
from jax.sharding import PartitionSpec as P


def halo_rows(cells, axis, width):
    count = lax.axis_size(axis)
    even = lax.axis_index(axis) % 2 == 0
    head = cells[:width]
    tail = cells[cells.shape[0] - width :]
    same_chip = lax.ppermute(
        jnp.where(even, tail, head), axis, [(i, i ^ 1) for i in range(count)]
    )
    links = [(i, i + 1) for i in range(1, count - 1, 2)] + [(i + 1, i) for i in range(1, count - 1, 2)]
    across = lax.ppermute(jnp.where(even, head, tail), axis, links)
    from_above = jnp.where(even, across, same_chip)
    from_below = jnp.where(even, same_chip, across)
    return jnp.concatenate([from_above, cells, from_below], axis=0)


def convolve_rows(padded, weights, out_rows, out_cols):
    channels = padded.shape[2]
    summed = jnp.zeros((out_rows * out_cols, channels), jnp.float32)
    for row_shift in range(3):
        for col_shift in range(3):
            window = padded[row_shift : row_shift + out_rows, col_shift : col_shift + out_cols]
            window = window.reshape(out_rows * out_cols, channels)
            summed = summed + jnp.dot(
                window, weights[row_shift, col_shift], preferred_element_type=jnp.float32
            )
    return summed.reshape(out_rows, out_cols, channels)


def native_conv(rows, weights):
    out = lax.conv_general_dilated(
        rows[None],
        weights,
        window_strides=(1, 1),
        padding=((0, 0), (1, 1)),
        dimension_numbers=("NHWC", "HWIO", "NHWC"),
        preferred_element_type=jnp.float32,
    )
    return out[0]


def pad_columns(image):
    return jnp.pad(image, ((0, 0), (1, 1), (0, 0)))


def attend_kernel(owner_ref, count_ref, q_ref, k_ref, *refs, scale, first, last):
    if first:
        m_out, t_out, a_out, kall_ref = refs
    elif last:
        m_in, t_in, a_in, o_ref, kall_ref = refs
    else:
        m_in, t_in, a_in, m_out, t_out, a_out, kall_ref = refs
    t = pl.program_id(0)
    n = count_ref[t]
    slots = owner_ref.shape[1]
    span = k_ref.shape[1]
    lanes = 128
    for j in range(slots):
        kall_ref[j * span : (j + 1) * span, :] = k_ref[owner_ref[t, j]]
    q = q_ref[0]
    kall = kall_ref[...]
    s = lax.dot_general(q, kall, (((1,), (1,)), ((), ())), preferred_element_type=jnp.float32)
    penalty = [jnp.where(j < n, 0.0, jnp.inf).astype(jnp.float32) for j in range(slots)]
    blocks = [(j, j * span + c * lanes) for j in range(slots) for c in range(span // lanes)]
    mx = None
    for j, at in blocks:
        blk = s[:, at : at + lanes]
        mx = blk if mx is None else jnp.maximum(mx, blk)
    rows = q.shape[0]

    def column(row, width):
        return jnp.broadcast_to(row, (width, rows)).T

    m_new = jnp.max(mx.T, axis=0, keepdims=True) * scale
    if not first:
        m_old = m_in[0]
        m_new = jnp.maximum(m_old, m_new)
        alpha = jnp.exp(m_old - m_new)
    log2e = 1.4426950408889634
    mb = column(m_new * log2e, lanes)
    shifted = [mb + penalty[j] for j in range(slots)]
    acc = None
    ps = []
    for j, at in blocks:
        p = jnp.exp2(s[:, at : at + lanes] * (scale * log2e) - shifted[j])
        acc = p if acc is None else acc + p
        ps.append(p.astype(jnp.bfloat16))
    pb = jnp.concatenate(ps, axis=1)
    mixed = jnp.dot(pb, kall, preferred_element_type=jnp.float32)
    total = jnp.sum(acc.T, axis=0, keepdims=True)
    width = mixed.shape[1]
    if not first:
        mixed = a_in[0] * column(alpha, width) + mixed
        total = t_in[0] * alpha + total
    if last:
        o_ref[0] = (mixed / column(total, width)).astype(o_ref.dtype)
    else:
        m_out[0] = m_new
        t_out[0] = total
        a_out[0] = mixed


def attend_chunk(state, queries, chunk, slot_owner, counts, scale, first, last):
    tiles, tile_size, channels = queries.shape
    owners, chunk_len, _ = chunk.shape
    slots = slot_owner.shape[1]
    col_spec = pl.BlockSpec((1, 1, tile_size), lambda t, o, c: (t, 0, 0))
    acc_spec = pl.BlockSpec((1, tile_size, channels), lambda t, o, c: (t, 0, 0))
    state_specs = [] if first else [col_spec, col_spec, acc_spec]
    if last:
        out_specs = acc_spec
        out_shape = jax.ShapeDtypeStruct(queries.shape, jnp.bfloat16)
    else:
        out_specs = [col_spec, col_spec, acc_spec]
        out_shape = [
            jax.ShapeDtypeStruct((tiles, 1, tile_size), jnp.float32),
            jax.ShapeDtypeStruct((tiles, 1, tile_size), jnp.float32),
            jax.ShapeDtypeStruct((tiles, tile_size, channels), jnp.float32),
        ]
    grid_spec = pltpu.PrefetchScalarGridSpec(
        num_scalar_prefetch=2,
        grid=(tiles,),
        in_specs=[
            acc_spec,
            pl.BlockSpec((owners, chunk_len, channels), lambda t, o, c: (0, 0, 0)),
        ]
        + state_specs,
        out_specs=out_specs,
        scratch_shapes=[pltpu.VMEM((slots * chunk_len, channels), jnp.bfloat16)],
    )
    return pl.pallas_call(
        functools.partial(attend_kernel, scale=scale, first=first, last=last),
        grid_spec=grid_spec,
        out_shape=out_shape,
        compiler_params=pltpu.CompilerParams(vmem_limit_bytes=48 * 1024 * 1024),
    )(slot_owner, counts, queries, chunk, *([] if first else state))


def attend_last_half(state, queries, chunk, slot_owner, counts, half, scale):
    tiles, tile_size, channels = queries.shape
    owners, chunk_len, _ = chunk.shape
    slots = slot_owner.shape[1]
    part = tile_size // 2
    row_spec = pl.BlockSpec((1, 1, part), lambda t, o, c, h: (t, 0, h[0]))
    acc_spec = pl.BlockSpec((1, part, channels), lambda t, o, c, h: (t, h[0], 0))
    grid_spec = pltpu.PrefetchScalarGridSpec(
        num_scalar_prefetch=3,
        grid=(tiles,),
        in_specs=[
            acc_spec,
            pl.BlockSpec(memory_space=pltpu.MemorySpace.VMEM),
            row_spec,
            row_spec,
            acc_spec,
        ],
        out_specs=pl.BlockSpec((1, part, channels), lambda t, o, c, h: (t, 0, 0)),
        scratch_shapes=[pltpu.VMEM((slots * chunk_len, channels), jnp.bfloat16)],
    )

    def kernel(owner_ref, count_ref, half_ref, *refs):
        attend_kernel(owner_ref, count_ref, *refs, scale=scale, first=False, last=True)

    return pl.pallas_call(
        kernel,
        grid_spec=grid_spec,
        out_shape=jax.ShapeDtypeStruct((tiles, part, channels), jnp.bfloat16),
        compiler_params=pltpu.CompilerParams(vmem_limit_bytes=48 * 1024 * 1024),
    )(slot_owner, counts, half, queries, chunk, *state)


def on_device(frame_one, frame_two, tile_lists, conv_one, conv_two):
    band_rows, band_width, channels = frame_one.shape
    per_device = tile_lists.shape[0]
    tile_cols = band_width // per_device
    tile_size = band_rows * tile_cols
    owners = lax.axis_size("row")
    scale = float(channels) ** (-0.5)

    def band_to_tiles(band):
        return (
            band.reshape(band_rows, per_device, tile_cols, channels)
            .transpose(1, 0, 2, 3)
            .reshape(per_device, tile_size, channels)
        )

    query_tiles = band_to_tiles(frame_one)
    own_keys = band_to_tiles(frame_two)
    valid = tile_lists >= 0
    slot_owner = jnp.maximum(jnp.where(valid, tile_lists, tile_lists[:, :1]), 0) // per_device
    counts = jnp.sum(valid.astype(jnp.int32), axis=1)
    me = lax.axis_index("row")
    flat_lists = tile_lists.reshape(1, -1)
    lists_everywhere = jnp.broadcast_to(flat_lists, (owners, flat_lists.shape[1]))
    lists_of = lax.all_to_all(lists_everywhere, "row", split_axis=0, concat_axis=0, tiled=True)
    mine = (lists_of >= 0) & (lists_of // per_device == me)
    asked = jnp.max(jnp.where(mine, lists_of % per_device, 0), axis=1)
    edges = [0, tile_size // 2, tile_size]
    state = ()
    previous = None
    for index, (start, stop) in enumerate(zip(edges[:-1], edges[1:])):
        part = own_keys[:, start:stop]
        picks = asked
        if previous is not None:
            part, picks = lax.optimization_barrier((part, picks))
        sending = jnp.broadcast_to(part[0][None], (owners,) + part.shape[1:])
        for local in range(1, per_device):
            sending = jnp.where((picks == local)[:, None, None], part[local][None], sending)
        if previous is not None:
            previous, sending, state = lax.optimization_barrier((previous, sending, state))
        current = lax.all_to_all(sending, "row", split_axis=0, concat_axis=0, tiled=True)
        if previous is not None:
            state = attend_chunk(state, query_tiles, previous, slot_owner, counts, scale, index == 1, False)
        previous = current
    even = me % 2 == 0
    crossing = jnp.where(even, 0, 1).astype(jnp.int32).reshape(1)
    staying = (1 - crossing).astype(jnp.int32)
    crossing_tiles = attend_last_half(state, query_tiles, previous, slot_owner, counts, crossing, scale)
    staying_tiles = attend_last_half(state, query_tiles, previous, slot_owner, counts, staying, scale)

    def to_rows(tiles):
        return tiles.reshape(per_device, -1, tile_cols, channels).transpose(1, 0, 2, 3).reshape(
            -1, band_width, channels
        )

    crossing_rows = to_rows(crossing_tiles)
    staying_rows = to_rows(staying_tiles)
    count = lax.axis_size("row")
    links = [(i, i + 1) for i in range(1, count - 1, 2)] + [(i + 1, i) for i in range(1, count - 1, 2)]
    across = lax.ppermute(crossing_rows, "row", links)
    same_chip = lax.ppermute(staying_rows, "row", [(i, i ^ 1) for i in range(count)])
    warped = jnp.where(
        even,
        jnp.concatenate([crossing_rows, staying_rows], axis=0),
        jnp.concatenate([staying_rows, crossing_rows], axis=0),
    )
    from_above = jnp.where(even, across, same_chip)
    from_below = jnp.where(even, same_chip, across)
    extended = jnp.concatenate([from_above, warped, from_below], axis=0)
    hidden = jax.nn.relu(native_conv(extended, conv_one)).astype(jnp.bfloat16)
    row_ids = jnp.arange(band_rows + 2)
    inside = ((row_ids > 0) | (me > 0)) & ((row_ids < band_rows + 1) | (me < owners - 1))
    hidden = jnp.where(inside[:, None, None], hidden, jnp.zeros_like(hidden))
    branch = native_conv(hidden, conv_two)
    return (frame_one.astype(jnp.float32) + branch).astype(jnp.bfloat16)


def solution(mesh):
    in_specs = (
        P(("pairs", "row"), None, None),
        P(("pairs", "row"), None, None),
        P(("pairs", "row"), None),
        P(),
        P(),
    )
    out_specs = P(("pairs", "row"), None, None)
    return jax.shard_map(
        on_device, mesh=mesh, in_specs=in_specs, out_specs=out_specs, check_vma=False
    )
```

```python
import functools

import jax
import jax.numpy as jnp
from jax import lax
from jax.experimental import pallas as pl
from jax.experimental.pallas import tpu as pltpu
from jax.sharding import PartitionSpec as P


def halo_rows(cells, axis, width):
    count = lax.axis_size(axis)
    even = lax.axis_index(axis) % 2 == 0
    head = cells[:width]
    tail = cells[cells.shape[0] - width :]
    same_chip = lax.ppermute(
        jnp.where(even, tail, head), axis, [(i, i ^ 1) for i in range(count)]
    )
    links = [(i, i + 1) for i in range(1, count - 1, 2)] + [(i + 1, i) for i in range(1, count - 1, 2)]
    across = lax.ppermute(jnp.where(even, head, tail), axis, links)
    from_above = jnp.where(even, across, same_chip)
    from_below = jnp.where(even, same_chip, across)
    return jnp.concatenate([from_above, cells, from_below], axis=0)


def convolve_rows(padded, weights, out_rows, out_cols):
    channels = padded.shape[2]
    summed = jnp.zeros((out_rows * out_cols, channels), jnp.float32)
    for row_shift in range(3):
        for col_shift in range(3):
            window = padded[row_shift : row_shift + out_rows, col_shift : col_shift + out_cols]
            window = window.reshape(out_rows * out_cols, channels)
            summed = summed + jnp.dot(
                window, weights[row_shift, col_shift], preferred_element_type=jnp.float32
            )
    return summed.reshape(out_rows, out_cols, channels)


def native_conv(rows, weights):
    out = lax.conv_general_dilated(
        rows[None],
        weights,
        window_strides=(1, 1),
        padding=((0, 0), (1, 1)),
        dimension_numbers=("NHWC", "HWIO", "NHWC"),
        preferred_element_type=jnp.float32,
    )
    return out[0]


def pad_columns(image):
    return jnp.pad(image, ((0, 0), (1, 1), (0, 0)))


def attend_kernel(owner_ref, count_ref, q_ref, k_ref, *refs, scale, first, last):
    if first:
        m_out, t_out, a_out, kall_ref = refs
    elif last:
        m_in, t_in, a_in, o_ref, kall_ref = refs
    else:
        m_in, t_in, a_in, m_out, t_out, a_out, kall_ref = refs
    t = pl.program_id(0)
    n = count_ref[t]
    slots = owner_ref.shape[1]
    span = k_ref.shape[1]
    lanes = 128
    for j in range(slots):
        kall_ref[j * span : (j + 1) * span, :] = k_ref[owner_ref[t, j]]
    q = q_ref[0]
    kall = kall_ref[...]
    s = lax.dot_general(q, kall, (((1,), (1,)), ((), ())), preferred_element_type=jnp.float32)
    penalty = [jnp.where(j < n, 0.0, jnp.inf).astype(jnp.float32) for j in range(slots)]
    blocks = [(j, j * span + c * lanes) for j in range(slots) for c in range(span // lanes)]
    mx = None
    for j, at in blocks:
        blk = s[:, at : at + lanes]
        mx = blk if mx is None else jnp.maximum(mx, blk)
    rows = q.shape[0]

    def column(row, width):
        return jnp.broadcast_to(row, (width, rows)).T

    m_new = jnp.max(mx.T, axis=0, keepdims=True) * scale
    if not first:
        m_old = m_in[0]
        m_new = jnp.maximum(m_old, m_new)
        alpha = jnp.exp(m_old - m_new)
    log2e = 1.4426950408889634
    mb = column(m_new * log2e, lanes)
    shifted = [mb + penalty[j] for j in range(slots)]
    acc = None
    ps = []
    for j, at in blocks:
        p = jnp.exp2(s[:, at : at + lanes] * (scale * log2e) - shifted[j])
        acc = p if acc is None else acc + p
        ps.append(p.astype(jnp.bfloat16))
    pb = jnp.concatenate(ps, axis=1)
    mixed = jnp.dot(pb, kall, preferred_element_type=jnp.float32)
    total = jnp.sum(acc.T, axis=0, keepdims=True)
    width = mixed.shape[1]
    if not first:
        mixed = a_in[0] * column(alpha, width) + mixed
        total = t_in[0] * alpha + total
    if last:
        o_ref[0] = (mixed / column(total, width)).astype(o_ref.dtype)
    else:
        m_out[0] = m_new
        t_out[0] = total
        a_out[0] = mixed


def attend_chunk(state, queries, chunk, slot_owner, counts, scale, first, last):
    tiles, tile_size, channels = queries.shape
    owners, chunk_len, _ = chunk.shape
    slots = slot_owner.shape[1]
    col_spec = pl.BlockSpec((1, 1, tile_size), lambda t, o, c: (t, 0, 0))
    acc_spec = pl.BlockSpec((1, tile_size, channels), lambda t, o, c: (t, 0, 0))
    state_specs = [] if first else [col_spec, col_spec, acc_spec]
    if last:
        out_specs = acc_spec
        out_shape = jax.ShapeDtypeStruct(queries.shape, jnp.bfloat16)
    else:
        out_specs = [col_spec, col_spec, acc_spec]
        out_shape = [
            jax.ShapeDtypeStruct((tiles, 1, tile_size), jnp.float32),
            jax.ShapeDtypeStruct((tiles, 1, tile_size), jnp.float32),
            jax.ShapeDtypeStruct((tiles, tile_size, channels), jnp.float32),
        ]
    grid_spec = pltpu.PrefetchScalarGridSpec(
        num_scalar_prefetch=2,
        grid=(tiles,),
        in_specs=[
            acc_spec,
            pl.BlockSpec((owners, chunk_len, channels), lambda t, o, c: (0, 0, 0)),
        ]
        + state_specs,
        out_specs=out_specs,
        scratch_shapes=[pltpu.VMEM((slots * chunk_len, channels), jnp.bfloat16)],
    )
    return pl.pallas_call(
        functools.partial(attend_kernel, scale=scale, first=first, last=last),
        grid_spec=grid_spec,
        out_shape=out_shape,
        compiler_params=pltpu.CompilerParams(vmem_limit_bytes=48 * 1024 * 1024),
    )(slot_owner, counts, queries, chunk, *([] if first else state))


def attend_last_half(state, queries, chunk, slot_owner, counts, half, scale):
    tiles, tile_size, channels = queries.shape
    owners, chunk_len, _ = chunk.shape
    slots = slot_owner.shape[1]
    part = tile_size // 2
    row_spec = pl.BlockSpec((1, 1, part), lambda t, o, c, h: (t, 0, h[0]))
    acc_spec = pl.BlockSpec((1, part, channels), lambda t, o, c, h: (t, h[0], 0))
    grid_spec = pltpu.PrefetchScalarGridSpec(
        num_scalar_prefetch=3,
        grid=(tiles,),
        in_specs=[
            acc_spec,
            pl.BlockSpec(memory_space=pltpu.MemorySpace.VMEM),
            row_spec,
            row_spec,
            acc_spec,
        ],
        out_specs=pl.BlockSpec((1, part, channels), lambda t, o, c, h: (t, 0, 0)),
        scratch_shapes=[pltpu.VMEM((slots * chunk_len, channels), jnp.bfloat16)],
    )

    def kernel(owner_ref, count_ref, half_ref, *refs):
        attend_kernel(owner_ref, count_ref, *refs, scale=scale, first=False, last=True)

    return pl.pallas_call(
        kernel,
        grid_spec=grid_spec,
        out_shape=jax.ShapeDtypeStruct((tiles, part, channels), jnp.bfloat16),
        compiler_params=pltpu.CompilerParams(vmem_limit_bytes=48 * 1024 * 1024),
    )(slot_owner, counts, half, queries, chunk, *state)


def on_device(frame_one, frame_two, tile_lists, conv_one, conv_two):
    band_rows, band_width, channels = frame_one.shape
    per_device = tile_lists.shape[0]
    tile_cols = band_width // per_device
    tile_size = band_rows * tile_cols
    owners = lax.axis_size("row")
    scale = float(channels) ** (-0.5)

    def band_to_tiles(band):
        return (
            band.reshape(band_rows, per_device, tile_cols, channels)
            .transpose(1, 0, 2, 3)
            .reshape(per_device, tile_size, channels)
        )

    query_tiles = band_to_tiles(frame_one)
    own_keys = band_to_tiles(frame_two)
    valid = tile_lists >= 0
    slot_owner = jnp.maximum(jnp.where(valid, tile_lists, tile_lists[:, :1]), 0) // per_device
    counts = jnp.sum(valid.astype(jnp.int32), axis=1)
    me = lax.axis_index("row")
    flat_lists = tile_lists.reshape(1, -1)
    lists_everywhere = jnp.broadcast_to(flat_lists, (owners, flat_lists.shape[1]))
    lists_of = lax.all_to_all(lists_everywhere, "row", split_axis=0, concat_axis=0, tiled=True)
    lists_of, frame_one_late = lax.optimization_barrier((lists_of, frame_one))
    query_tiles = band_to_tiles(frame_one_late)
    mine = (lists_of >= 0) & (lists_of // per_device == me)
    asked = jnp.max(jnp.where(mine, lists_of % per_device, 0), axis=1)
    edges = [0, tile_size // 2, tile_size]
    state = ()
    previous = None
    for index, (start, stop) in enumerate(zip(edges[:-1], edges[1:])):
        part = own_keys[:, start:stop]
        sending = jnp.broadcast_to(part[0][None], (owners,) + part.shape[1:])
        for local in range(1, per_device):
            sending = jnp.where((asked == local)[:, None, None], part[local][None], sending)
        if previous is not None:
            previous, sending, state = lax.optimization_barrier((previous, sending, state))
        current = lax.all_to_all(sending, "row", split_axis=0, concat_axis=0, tiled=True)
        if previous is not None:
            state = attend_chunk(state, query_tiles, previous, slot_owner, counts, scale, index == 1, False)
        previous = current
    even = me % 2 == 0
    crossing = jnp.where(even, 0, 1).astype(jnp.int32).reshape(1)
    staying = (1 - crossing).astype(jnp.int32)
    crossing_tiles = attend_last_half(state, query_tiles, previous, slot_owner, counts, crossing, scale)
    staying_tiles = attend_last_half(state, query_tiles, previous, slot_owner, counts, staying, scale)

    def to_rows(tiles):
        return tiles.reshape(per_device, -1, tile_cols, channels).transpose(1, 0, 2, 3).reshape(
            -1, band_width, channels
        )

    crossing_rows = to_rows(crossing_tiles)
    staying_rows = to_rows(staying_tiles)
    count = lax.axis_size("row")
    links = [(i, i + 1) for i in range(1, count - 1, 2)] + [(i + 1, i) for i in range(1, count - 1, 2)]
    across = lax.ppermute(crossing_rows, "row", links)
    same_chip = lax.ppermute(staying_rows, "row", [(i, i ^ 1) for i in range(count)])
    warped = jnp.where(
        even,
        jnp.concatenate([crossing_rows, staying_rows], axis=0),
        jnp.concatenate([staying_rows, crossing_rows], axis=0),
    )
    from_above = jnp.where(even, across, same_chip)
    from_below = jnp.where(even, same_chip, across)
    extended = jnp.concatenate([from_above, warped, from_below], axis=0)
    hidden = jax.nn.relu(native_conv(extended, conv_one)).astype(jnp.bfloat16)
    row_ids = jnp.arange(band_rows + 2)
    inside = ((row_ids > 0) | (me > 0)) & ((row_ids < band_rows + 1) | (me < owners - 1))
    hidden = jnp.where(inside[:, None, None], hidden, jnp.zeros_like(hidden))
    branch = native_conv(hidden, conv_two)
    return (frame_one.astype(jnp.float32) + branch).astype(jnp.bfloat16)


def solution(mesh):
    in_specs = (
        P(("pairs", "row"), None, None),
        P(("pairs", "row"), None, None),
        P(("pairs", "row"), None),
        P(),
        P(),
    )
    out_specs = P(("pairs", "row"), None, None)
    return jax.shard_map(
        on_device, mesh=mesh, in_specs=in_specs, out_specs=out_specs, check_vma=False
    )
```

```python
import functools

import jax
import jax.numpy as jnp
from jax import lax
from jax.experimental import pallas as pl
from jax.experimental.pallas import tpu as pltpu
from jax.sharding import PartitionSpec as P


def halo_rows(cells, axis, width):
    count = lax.axis_size(axis)
    even = lax.axis_index(axis) % 2 == 0
    head = cells[:width]
    tail = cells[cells.shape[0] - width :]
    same_chip = lax.ppermute(
        jnp.where(even, tail, head), axis, [(i, i ^ 1) for i in range(count)]
    )
    links = [(i, i + 1) for i in range(1, count - 1, 2)] + [(i + 1, i) for i in range(1, count - 1, 2)]
    across = lax.ppermute(jnp.where(even, head, tail), axis, links)
    from_above = jnp.where(even, across, same_chip)
    from_below = jnp.where(even, same_chip, across)
    return jnp.concatenate([from_above, cells, from_below], axis=0)


def convolve_rows(padded, weights, out_rows, out_cols):
    channels = padded.shape[2]
    summed = jnp.zeros((out_rows * out_cols, channels), jnp.float32)
    for row_shift in range(3):
        for col_shift in range(3):
            window = padded[row_shift : row_shift + out_rows, col_shift : col_shift + out_cols]
            window = window.reshape(out_rows * out_cols, channels)
            summed = summed + jnp.dot(
                window, weights[row_shift, col_shift], preferred_element_type=jnp.float32
            )
    return summed.reshape(out_rows, out_cols, channels)


def native_conv(rows, weights):
    out = lax.conv_general_dilated(
        rows[None],
        weights,
        window_strides=(1, 1),
        padding=((0, 0), (1, 1)),
        dimension_numbers=("NHWC", "HWIO", "NHWC"),
        preferred_element_type=jnp.float32,
    )
    return out[0]


def pad_columns(image):
    return jnp.pad(image, ((0, 0), (1, 1), (0, 0)))


def attend_kernel(owner_ref, count_ref, q_ref, k_ref, *refs, scale, first, last):
    if first:
        m_out, t_out, a_out, kall_ref = refs
    elif last:
        m_in, t_in, a_in, o_ref, kall_ref = refs
    else:
        m_in, t_in, a_in, m_out, t_out, a_out, kall_ref = refs
    t = pl.program_id(0)
    n = count_ref[t]
    slots = owner_ref.shape[1]
    span = k_ref.shape[1]
    lanes = 128
    for j in range(slots):
        kall_ref[j * span : (j + 1) * span, :] = k_ref[owner_ref[t, j]]
    q = q_ref[0]
    kall = kall_ref[...]
    s = lax.dot_general(q, kall, (((1,), (1,)), ((), ())), preferred_element_type=jnp.float32)
    penalty = [jnp.where(j < n, 0.0, jnp.inf).astype(jnp.float32) for j in range(slots)]
    blocks = [(j, j * span + c * lanes) for j in range(slots) for c in range(span // lanes)]
    mx = None
    for j, at in blocks:
        blk = s[:, at : at + lanes]
        mx = blk if mx is None else jnp.maximum(mx, blk)
    rows = q.shape[0]

    def column(row, width):
        return jnp.broadcast_to(row, (width, rows)).T

    m_new = jnp.max(mx.T, axis=0, keepdims=True) * scale
    if not first:
        m_old = m_in[0]
        m_new = jnp.maximum(m_old, m_new)
        alpha = jnp.exp(m_old - m_new)
    log2e = 1.4426950408889634
    mb = column(m_new * log2e, lanes)
    shifted = [mb + penalty[j] for j in range(slots)]
    acc = None
    ps = []
    for j, at in blocks:
        p = jnp.exp2(s[:, at : at + lanes] * (scale * log2e) - shifted[j])
        acc = p if acc is None else acc + p
        ps.append(p.astype(jnp.bfloat16))
    pb = jnp.concatenate(ps, axis=1)
    mixed = jnp.dot(pb, kall, preferred_element_type=jnp.float32)
    total = jnp.sum(acc.T, axis=0, keepdims=True)
    width = mixed.shape[1]
    if not first:
        mixed = a_in[0] * column(alpha, width) + mixed
        total = t_in[0] * alpha + total
    if last:
        o_ref[0] = (mixed / column(total, width)).astype(o_ref.dtype)
    else:
        m_out[0] = m_new
        t_out[0] = total
        a_out[0] = mixed


def attend_chunk(state, queries, chunk, slot_owner, counts, scale, first, last):
    tiles, tile_size, channels = queries.shape
    owners, chunk_len, _ = chunk.shape
    slots = slot_owner.shape[1]
    col_spec = pl.BlockSpec((1, 1, tile_size), lambda t, o, c: (t, 0, 0))
    acc_spec = pl.BlockSpec((1, tile_size, channels), lambda t, o, c: (t, 0, 0))
    state_specs = [] if first else [col_spec, col_spec, acc_spec]
    if last:
        out_specs = acc_spec
        out_shape = jax.ShapeDtypeStruct(queries.shape, jnp.bfloat16)
    else:
        out_specs = [col_spec, col_spec, acc_spec]
        out_shape = [
            jax.ShapeDtypeStruct((tiles, 1, tile_size), jnp.float32),
            jax.ShapeDtypeStruct((tiles, 1, tile_size), jnp.float32),
            jax.ShapeDtypeStruct((tiles, tile_size, channels), jnp.float32),
        ]
    grid_spec = pltpu.PrefetchScalarGridSpec(
        num_scalar_prefetch=2,
        grid=(tiles,),
        in_specs=[
            acc_spec,
            pl.BlockSpec((owners, chunk_len, channels), lambda t, o, c: (0, 0, 0)),
        ]
        + state_specs,
        out_specs=out_specs,
        scratch_shapes=[pltpu.VMEM((slots * chunk_len, channels), jnp.bfloat16)],
    )
    return pl.pallas_call(
        functools.partial(attend_kernel, scale=scale, first=first, last=last),
        grid_spec=grid_spec,
        out_shape=out_shape,
        compiler_params=pltpu.CompilerParams(vmem_limit_bytes=24 * 1024 * 1024),
    )(slot_owner, counts, queries, chunk, *([] if first else state))


def attend_last_half(state, queries, chunk, slot_owner, counts, half, scale):
    tiles, tile_size, channels = queries.shape
    owners, chunk_len, _ = chunk.shape
    slots = slot_owner.shape[1]
    part = tile_size // 2
    row_spec = pl.BlockSpec((1, 1, part), lambda t, o, c, h: (t, 0, h[0]))
    acc_spec = pl.BlockSpec((1, part, channels), lambda t, o, c, h: (t, h[0], 0))
    grid_spec = pltpu.PrefetchScalarGridSpec(
        num_scalar_prefetch=3,
        grid=(tiles,),
        in_specs=[
            acc_spec,
            pl.BlockSpec(memory_space=pltpu.MemorySpace.VMEM),
            row_spec,
            row_spec,
            acc_spec,
        ],
        out_specs=pl.BlockSpec((1, part, channels), lambda t, o, c, h: (t, 0, 0)),
        scratch_shapes=[pltpu.VMEM((slots * chunk_len, channels), jnp.bfloat16)],
    )

    def kernel(owner_ref, count_ref, half_ref, *refs):
        attend_kernel(owner_ref, count_ref, *refs, scale=scale, first=False, last=True)

    return pl.pallas_call(
        kernel,
        grid_spec=grid_spec,
        out_shape=jax.ShapeDtypeStruct((tiles, part, channels), jnp.bfloat16),
        compiler_params=pltpu.CompilerParams(vmem_limit_bytes=24 * 1024 * 1024),
    )(slot_owner, counts, half, queries, chunk, *state)


def on_device(frame_one, frame_two, tile_lists, conv_one, conv_two):
    band_rows, band_width, channels = frame_one.shape
    per_device = tile_lists.shape[0]
    tile_cols = band_width // per_device
    tile_size = band_rows * tile_cols
    owners = lax.axis_size("row")
    scale = float(channels) ** (-0.5)

    def band_to_tiles(band):
        return (
            band.reshape(band_rows, per_device, tile_cols, channels)
            .transpose(1, 0, 2, 3)
            .reshape(per_device, tile_size, channels)
        )

    query_tiles = band_to_tiles(frame_one)
    own_keys = band_to_tiles(frame_two)
    valid = tile_lists >= 0
    slot_owner = jnp.maximum(jnp.where(valid, tile_lists, tile_lists[:, :1]), 0) // per_device
    counts = jnp.sum(valid.astype(jnp.int32), axis=1)
    me = lax.axis_index("row")
    flat_lists = tile_lists.reshape(1, -1)
    lists_everywhere = jnp.broadcast_to(flat_lists, (owners, flat_lists.shape[1]))
    lists_of = lax.all_to_all(lists_everywhere, "row", split_axis=0, concat_axis=0, tiled=True)
    mine = (lists_of >= 0) & (lists_of // per_device == me)
    asked = jnp.max(jnp.where(mine, lists_of % per_device, 0), axis=1)
    edges = [0, tile_size // 2, tile_size]
    state = ()
    previous = None
    for index, (start, stop) in enumerate(zip(edges[:-1], edges[1:])):
        part = own_keys[:, start:stop]
        sending = jnp.broadcast_to(part[0][None], (owners,) + part.shape[1:])
        for local in range(1, per_device):
            sending = jnp.where((asked == local)[:, None, None], part[local][None], sending)
        if previous is not None:
            previous, sending, state = lax.optimization_barrier((previous, sending, state))
        current = lax.all_to_all(sending, "row", split_axis=0, concat_axis=0, tiled=True)
        if previous is not None:
            state = attend_chunk(state, query_tiles, previous, slot_owner, counts, scale, index == 1, False)
        previous = current
    even = me % 2 == 0
    crossing = jnp.where(even, 0, 1).astype(jnp.int32).reshape(1)
    staying = (1 - crossing).astype(jnp.int32)
    crossing_tiles = attend_last_half(state, query_tiles, previous, slot_owner, counts, crossing, scale)
    staying_tiles = attend_last_half(state, query_tiles, previous, slot_owner, counts, staying, scale)

    def to_rows(tiles):
        return tiles.reshape(per_device, -1, tile_cols, channels).transpose(1, 0, 2, 3).reshape(
            -1, band_width, channels
        )

    crossing_rows = to_rows(crossing_tiles)
    staying_rows = to_rows(staying_tiles)
    count = lax.axis_size("row")
    links = [(i, i + 1) for i in range(1, count - 1, 2)] + [(i + 1, i) for i in range(1, count - 1, 2)]
    across = lax.ppermute(crossing_rows, "row", links)
    same_chip = lax.ppermute(staying_rows, "row", [(i, i ^ 1) for i in range(count)])
    warped = jnp.where(
        even,
        jnp.concatenate([crossing_rows, staying_rows], axis=0),
        jnp.concatenate([staying_rows, crossing_rows], axis=0),
    )
    from_above = jnp.where(even, across, same_chip)
    from_below = jnp.where(even, same_chip, across)
    extended = jnp.concatenate([from_above, warped, from_below], axis=0)
    hidden = jax.nn.relu(native_conv(extended, conv_one)).astype(jnp.bfloat16)
    row_ids = jnp.arange(band_rows + 2)
    inside = ((row_ids > 0) | (me > 0)) & ((row_ids < band_rows + 1) | (me < owners - 1))
    hidden = jnp.where(inside[:, None, None], hidden, jnp.zeros_like(hidden))
    branch = native_conv(hidden, conv_two)
    return (frame_one.astype(jnp.float32) + branch).astype(jnp.bfloat16)


def solution(mesh):
    in_specs = (
        P(("pairs", "row"), None, None),
        P(("pairs", "row"), None, None),
        P(("pairs", "row"), None),
        P(),
        P(),
    )
    out_specs = P(("pairs", "row"), None, None)
    return jax.shard_map(
        on_device, mesh=mesh, in_specs=in_specs, out_specs=out_specs, check_vma=False
    )
```

```python
import functools

import jax
import jax.numpy as jnp
from jax import lax
from jax.experimental import pallas as pl
from jax.experimental.pallas import tpu as pltpu
from jax.sharding import PartitionSpec as P


def halo_rows(cells, axis, width):
    count = lax.axis_size(axis)
    even = lax.axis_index(axis) % 2 == 0
    head = cells[:width]
    tail = cells[cells.shape[0] - width :]
    same_chip = lax.ppermute(
        jnp.where(even, tail, head), axis, [(i, i ^ 1) for i in range(count)]
    )
    links = [(i, i + 1) for i in range(1, count - 1, 2)] + [(i + 1, i) for i in range(1, count - 1, 2)]
    across = lax.ppermute(jnp.where(even, head, tail), axis, links)
    from_above = jnp.where(even, across, same_chip)
    from_below = jnp.where(even, same_chip, across)
    return jnp.concatenate([from_above, cells, from_below], axis=0)


def convolve_rows(padded, weights, out_rows, out_cols):
    channels = padded.shape[2]
    summed = jnp.zeros((out_rows * out_cols, channels), jnp.float32)
    for row_shift in range(3):
        for col_shift in range(3):
            window = padded[row_shift : row_shift + out_rows, col_shift : col_shift + out_cols]
            window = window.reshape(out_rows * out_cols, channels)
            summed = summed + jnp.dot(
                window, weights[row_shift, col_shift], preferred_element_type=jnp.float32
            )
    return summed.reshape(out_rows, out_cols, channels)


def native_conv(rows, weights):
    out = lax.conv_general_dilated(
        rows[None],
        weights,
        window_strides=(1, 1),
        padding=((0, 0), (1, 1)),
        dimension_numbers=("NHWC", "HWIO", "NHWC"),
        preferred_element_type=jnp.float32,
    )
    return out[0]


def pad_columns(image):
    return jnp.pad(image, ((0, 0), (1, 1), (0, 0)))


def attend_kernel(owner_ref, count_ref, q_ref, k_ref, *refs, scale, first, last):
    if first:
        m_out, t_out, a_out, kall_ref = refs
    elif last:
        m_in, t_in, a_in, o_ref, kall_ref = refs
    else:
        m_in, t_in, a_in, m_out, t_out, a_out, kall_ref = refs
    t = pl.program_id(0)
    n = count_ref[t]
    slots = owner_ref.shape[1]
    span = k_ref.shape[1]
    lanes = 128
    for j in range(slots):
        kall_ref[j * span : (j + 1) * span, :] = k_ref[owner_ref[t, j]]
    q = q_ref[0]
    kall = kall_ref[...]
    s = lax.dot_general(q, kall, (((1,), (1,)), ((), ())), preferred_element_type=jnp.float32)
    penalty = [jnp.where(j < n, 0.0, jnp.inf).astype(jnp.float32) for j in range(slots)]
    blocks = [(j, j * span + c * lanes) for j in range(slots) for c in range(span // lanes)]
    mx = None
    for j, at in blocks:
        blk = s[:, at : at + lanes]
        mx = blk if mx is None else jnp.maximum(mx, blk)
    rows = q.shape[0]

    def column(row, width):
        return jnp.broadcast_to(row, (width, rows)).T

    m_new = jnp.max(mx.T, axis=0, keepdims=True) * scale
    if not first:
        m_old = m_in[0]
        m_new = jnp.maximum(m_old, m_new)
        alpha = jnp.exp(m_old - m_new)
    log2e = 1.4426950408889634
    mb = column(m_new * log2e, lanes)
    shifted = [mb + penalty[j] for j in range(slots)]
    acc = None
    ps = []
    for j, at in blocks:
        p = jnp.exp2(s[:, at : at + lanes] * (scale * log2e) - shifted[j])
        acc = p if acc is None else acc + p
        ps.append(p.astype(jnp.bfloat16))
    pb = jnp.concatenate(ps, axis=1)
    mixed = jnp.dot(pb, kall, preferred_element_type=jnp.float32)
    total = jnp.sum(acc.T, axis=0, keepdims=True)
    width = mixed.shape[1]
    if not first:
        mixed = a_in[0] * column(alpha, width) + mixed
        total = t_in[0] * alpha + total
    if last:
        o_ref[...] = (mixed / column(total, width)).astype(o_ref.dtype).reshape(o_ref.shape)
    else:
        m_out[0] = m_new
        t_out[0] = total
        a_out[0] = mixed


def attend_chunk(state, queries, chunk, slot_owner, counts, scale, first, last):
    tiles, tile_size, channels = queries.shape
    owners, chunk_len, _ = chunk.shape
    slots = slot_owner.shape[1]
    col_spec = pl.BlockSpec((1, 1, tile_size), lambda t, o, c: (t, 0, 0))
    acc_spec = pl.BlockSpec((1, tile_size, channels), lambda t, o, c: (t, 0, 0))
    state_specs = [] if first else [col_spec, col_spec, acc_spec]
    if last:
        out_specs = acc_spec
        out_shape = jax.ShapeDtypeStruct(queries.shape, jnp.bfloat16)
    else:
        out_specs = [col_spec, col_spec, acc_spec]
        out_shape = [
            jax.ShapeDtypeStruct((tiles, 1, tile_size), jnp.float32),
            jax.ShapeDtypeStruct((tiles, 1, tile_size), jnp.float32),
            jax.ShapeDtypeStruct((tiles, tile_size, channels), jnp.float32),
        ]
    grid_spec = pltpu.PrefetchScalarGridSpec(
        num_scalar_prefetch=2,
        grid=(tiles,),
        in_specs=[
            acc_spec,
            pl.BlockSpec((owners, chunk_len, channels), lambda t, o, c: (0, 0, 0)),
        ]
        + state_specs,
        out_specs=out_specs,
        scratch_shapes=[pltpu.VMEM((slots * chunk_len, channels), jnp.bfloat16)],
    )
    return pl.pallas_call(
        functools.partial(attend_kernel, scale=scale, first=first, last=last),
        grid_spec=grid_spec,
        out_shape=out_shape,
        compiler_params=pltpu.CompilerParams(vmem_limit_bytes=48 * 1024 * 1024),
    )(slot_owner, counts, queries, chunk, *([] if first else state))


def attend_last_half(state, queries, chunk, slot_owner, counts, half, scale, tile_cols):
    tiles, tile_size, channels = queries.shape
    owners, chunk_len, _ = chunk.shape
    slots = slot_owner.shape[1]
    part = tile_size // 2
    row_spec = pl.BlockSpec((1, 1, part), lambda t, o, c, h: (t, 0, h[0]))
    acc_spec = pl.BlockSpec((1, part, channels), lambda t, o, c, h: (t, h[0], 0))
    grid_spec = pltpu.PrefetchScalarGridSpec(
        num_scalar_prefetch=3,
        grid=(tiles,),
        in_specs=[
            acc_spec,
            pl.BlockSpec(memory_space=pltpu.MemorySpace.VMEM),
            row_spec,
            row_spec,
            acc_spec,
        ],
        out_specs=pl.BlockSpec((part // tile_cols, tile_cols, channels), lambda t, o, c, h: (0, t, 0)),
        scratch_shapes=[pltpu.VMEM((slots * chunk_len, channels), jnp.bfloat16)],
    )

    def kernel(owner_ref, count_ref, half_ref, *refs):
        attend_kernel(owner_ref, count_ref, *refs, scale=scale, first=False, last=True)

    return pl.pallas_call(
        kernel,
        grid_spec=grid_spec,
        out_shape=jax.ShapeDtypeStruct((part // tile_cols, tiles * tile_cols, channels), jnp.bfloat16),
        compiler_params=pltpu.CompilerParams(vmem_limit_bytes=48 * 1024 * 1024),
    )(slot_owner, counts, half, queries, chunk, *state)


def on_device(frame_one, frame_two, tile_lists, conv_one, conv_two):
    band_rows, band_width, channels = frame_one.shape
    per_device = tile_lists.shape[0]
    tile_cols = band_width // per_device
    tile_size = band_rows * tile_cols
    owners = lax.axis_size("row")
    scale = float(channels) ** (-0.5)

    def band_to_tiles(band):
        return (
            band.reshape(band_rows, per_device, tile_cols, channels)
            .transpose(1, 0, 2, 3)
            .reshape(per_device, tile_size, channels)
        )

    query_tiles = band_to_tiles(frame_one)
    own_keys = band_to_tiles(frame_two)
    valid = tile_lists >= 0
    slot_owner = jnp.maximum(jnp.where(valid, tile_lists, tile_lists[:, :1]), 0) // per_device
    counts = jnp.sum(valid.astype(jnp.int32), axis=1)
    me = lax.axis_index("row")
    flat_lists = tile_lists.reshape(1, -1)
    lists_everywhere = jnp.broadcast_to(flat_lists, (owners, flat_lists.shape[1]))
    lists_of = lax.all_to_all(lists_everywhere, "row", split_axis=0, concat_axis=0, tiled=True)
    mine = (lists_of >= 0) & (lists_of // per_device == me)
    asked = jnp.max(jnp.where(mine, lists_of % per_device, 0), axis=1)
    edges = [0, tile_size // 2, tile_size]
    state = ()
    previous = None
    for index, (start, stop) in enumerate(zip(edges[:-1], edges[1:])):
        part = own_keys[:, start:stop]
        sending = jnp.broadcast_to(part[0][None], (owners,) + part.shape[1:])
        for local in range(1, per_device):
            sending = jnp.where((asked == local)[:, None, None], part[local][None], sending)
        if previous is not None:
            previous, sending, state = lax.optimization_barrier((previous, sending, state))
        current = lax.all_to_all(sending, "row", split_axis=0, concat_axis=0, tiled=True)
        if previous is not None:
            state = attend_chunk(state, query_tiles, previous, slot_owner, counts, scale, index == 1, False)
        previous = current
    even = me % 2 == 0
    crossing = jnp.where(even, 0, 1).astype(jnp.int32).reshape(1)
    staying = (1 - crossing).astype(jnp.int32)
    crossing_rows = attend_last_half(
        state, query_tiles, previous, slot_owner, counts, crossing, scale, tile_cols
    )
    staying_rows = attend_last_half(
        state, query_tiles, previous, slot_owner, counts, staying, scale, tile_cols
    )

    count = lax.axis_size("row")
    links = [(i, i + 1) for i in range(1, count - 1, 2)] + [(i + 1, i) for i in range(1, count - 1, 2)]
    across = lax.ppermute(crossing_rows, "row", links)
    same_chip = lax.ppermute(staying_rows, "row", [(i, i ^ 1) for i in range(count)])
    warped = jnp.where(
        even,
        jnp.concatenate([crossing_rows, staying_rows], axis=0),
        jnp.concatenate([staying_rows, crossing_rows], axis=0),
    )
    from_above = jnp.where(even, across, same_chip)
    from_below = jnp.where(even, same_chip, across)
    extended = jnp.concatenate([from_above, warped, from_below], axis=0)
    hidden = jax.nn.relu(native_conv(extended, conv_one)).astype(jnp.bfloat16)
    row_ids = jnp.arange(band_rows + 2)
    inside = ((row_ids > 0) | (me > 0)) & ((row_ids < band_rows + 1) | (me < owners - 1))
    hidden = jnp.where(inside[:, None, None], hidden, jnp.zeros_like(hidden))
    branch = native_conv(hidden, conv_two)
    return (frame_one.astype(jnp.float32) + branch).astype(jnp.bfloat16)


def solution(mesh):
    in_specs = (
        P(("pairs", "row"), None, None),
        P(("pairs", "row"), None, None),
        P(("pairs", "row"), None),
        P(),
        P(),
    )
    out_specs = P(("pairs", "row"), None, None)
    return jax.shard_map(
        on_device, mesh=mesh, in_specs=in_specs, out_specs=out_specs, check_vma=False
    )
```

```python
import functools

import jax
import jax.numpy as jnp
from jax import lax
from jax.experimental import pallas as pl
from jax.experimental.pallas import tpu as pltpu
from jax.sharding import PartitionSpec as P


def halo_rows(cells, axis, width):
    count = lax.axis_size(axis)
    even = lax.axis_index(axis) % 2 == 0
    head = cells[:width]
    tail = cells[cells.shape[0] - width :]
    same_chip = lax.ppermute(
        jnp.where(even, tail, head), axis, [(i, i ^ 1) for i in range(count)]
    )
    links = [(i, i + 1) for i in range(1, count - 1, 2)] + [(i + 1, i) for i in range(1, count - 1, 2)]
    across = lax.ppermute(jnp.where(even, head, tail), axis, links)
    from_above = jnp.where(even, across, same_chip)
    from_below = jnp.where(even, same_chip, across)
    return jnp.concatenate([from_above, cells, from_below], axis=0)


def convolve_rows(padded, weights, out_rows, out_cols):
    channels = padded.shape[2]
    summed = jnp.zeros((out_rows * out_cols, channels), jnp.float32)
    for row_shift in range(3):
        for col_shift in range(3):
            window = padded[row_shift : row_shift + out_rows, col_shift : col_shift + out_cols]
            window = window.reshape(out_rows * out_cols, channels)
            summed = summed + jnp.dot(
                window, weights[row_shift, col_shift], preferred_element_type=jnp.float32
            )
    return summed.reshape(out_rows, out_cols, channels)


def native_conv(rows, weights):
    out = lax.conv_general_dilated(
        rows[None],
        weights,
        window_strides=(1, 1),
        padding=((0, 0), (1, 1)),
        dimension_numbers=("NHWC", "HWIO", "NHWC"),
        preferred_element_type=jnp.float32,
    )
    return out[0]


def pad_columns(image):
    return jnp.pad(image, ((0, 0), (1, 1), (0, 0)))


def attend_kernel(owner_ref, count_ref, q_ref, k_ref, *refs, scale, first, last):
    if first:
        m_out, t_out, a_out, kall_ref = refs
    elif last:
        m_in, t_in, a_in, o_ref, kall_ref = refs
    else:
        m_in, t_in, a_in, m_out, t_out, a_out, kall_ref = refs
    t = pl.program_id(0)
    n = count_ref[t]
    slots = owner_ref.shape[1]
    span = k_ref.shape[1]
    lanes = 128
    for j in range(slots):
        kall_ref[j * span : (j + 1) * span, :] = k_ref[owner_ref[t, j]]
    q = q_ref[0]
    kall = kall_ref[...]
    s = lax.dot_general(q, kall, (((1,), (1,)), ((), ())), preferred_element_type=jnp.float32)
    penalty = [jnp.where(j < n, 0.0, jnp.inf).astype(jnp.float32) for j in range(slots)]
    blocks = [(j, j * span + c * lanes) for j in range(slots) for c in range(span // lanes)]
    mx = None
    for j, at in blocks:
        blk = s[:, at : at + lanes]
        mx = blk if mx is None else jnp.maximum(mx, blk)
    rows = q.shape[0]

    def column(row, width):
        return jnp.broadcast_to(row, (width, rows)).T

    m_new = jnp.max(mx.T, axis=0, keepdims=True) * scale
    if not first:
        m_old = m_in[0]
        m_new = jnp.maximum(m_old, m_new)
        alpha = jnp.exp(m_old - m_new)
    log2e = 1.4426950408889634
    mb = column(m_new * log2e, lanes)
    shifted = [mb + penalty[j] for j in range(slots)]
    acc = None
    ps = []
    for j, at in blocks:
        p = jnp.exp2(s[:, at : at + lanes] * (scale * log2e) - shifted[j])
        acc = p if acc is None else acc + p
        ps.append(p.astype(jnp.bfloat16))
    pb = jnp.concatenate(ps, axis=1)
    mixed = jnp.dot(pb, kall, preferred_element_type=jnp.float32)
    total = jnp.sum(acc.T, axis=0, keepdims=True)
    width = mixed.shape[1]
    if not first:
        mixed = a_in[0] * column(alpha, width) + mixed
        total = t_in[0] * alpha + total
    if last:
        o_ref[0] = (mixed / column(total, width)).astype(o_ref.dtype)
    else:
        m_out[0] = m_new
        t_out[0] = total
        a_out[0] = mixed


def attend_chunk(state, queries, chunk, slot_owner, counts, scale, first, last):
    tiles, tile_size, channels = queries.shape
    owners, chunk_len, _ = chunk.shape
    slots = slot_owner.shape[1]
    col_spec = pl.BlockSpec((1, 1, tile_size), lambda t, o, c: (t, 0, 0))
    acc_spec = pl.BlockSpec((1, tile_size, channels), lambda t, o, c: (t, 0, 0))
    state_specs = [] if first else [col_spec, col_spec, acc_spec]
    if last:
        out_specs = acc_spec
        out_shape = jax.ShapeDtypeStruct(queries.shape, jnp.bfloat16)
    else:
        out_specs = [col_spec, col_spec, acc_spec]
        out_shape = [
            jax.ShapeDtypeStruct((tiles, 1, tile_size), jnp.float32),
            jax.ShapeDtypeStruct((tiles, 1, tile_size), jnp.float32),
            jax.ShapeDtypeStruct((tiles, tile_size, channels), jnp.float32),
        ]
    grid_spec = pltpu.PrefetchScalarGridSpec(
        num_scalar_prefetch=2,
        grid=(tiles,),
        in_specs=[
            acc_spec,
            pl.BlockSpec((owners, chunk_len, channels), lambda t, o, c: (0, 0, 0)),
        ]
        + state_specs,
        out_specs=out_specs,
        scratch_shapes=[pltpu.VMEM((slots * chunk_len, channels), jnp.bfloat16)],
    )
    return pl.pallas_call(
        functools.partial(attend_kernel, scale=scale, first=first, last=last),
        grid_spec=grid_spec,
        out_shape=out_shape,
        compiler_params=pltpu.CompilerParams(vmem_limit_bytes=48 * 1024 * 1024),
    )(slot_owner, counts, queries, chunk, *([] if first else state))


def attend_last_half(state, queries, chunk, slot_owner, counts, half, scale):
    tiles, tile_size, channels = queries.shape
    owners, chunk_len, _ = chunk.shape
    slots = slot_owner.shape[1]
    part = tile_size // 2
    row_spec = pl.BlockSpec((1, 1, part), lambda t, o, c, h: (t, 0, h[0]))
    acc_spec = pl.BlockSpec((1, part, channels), lambda t, o, c, h: (t, h[0], 0))
    grid_spec = pltpu.PrefetchScalarGridSpec(
        num_scalar_prefetch=3,
        grid=(tiles,),
        in_specs=[
            acc_spec,
            pl.BlockSpec(memory_space=pltpu.MemorySpace.VMEM),
            row_spec,
            row_spec,
            acc_spec,
        ],
        out_specs=pl.BlockSpec((1, part, channels), lambda t, o, c, h: (t, 0, 0)),
        scratch_shapes=[pltpu.VMEM((slots * chunk_len, channels), jnp.bfloat16)],
    )

    def kernel(owner_ref, count_ref, half_ref, *refs):
        attend_kernel(owner_ref, count_ref, *refs, scale=scale, first=False, last=True)

    return pl.pallas_call(
        kernel,
        grid_spec=grid_spec,
        out_shape=jax.ShapeDtypeStruct((tiles, part, channels), jnp.bfloat16),
        compiler_params=pltpu.CompilerParams(vmem_limit_bytes=48 * 1024 * 1024),
    )(slot_owner, counts, half, queries, chunk, *state)


def on_device(frame_one, frame_two, tile_lists, conv_one, conv_two):
    band_rows, band_width, channels = frame_one.shape
    per_device = tile_lists.shape[0]
    tile_cols = band_width // per_device
    tile_size = band_rows * tile_cols
    owners = lax.axis_size("row")
    scale = float(channels) ** (-0.5)

    def band_to_tiles(band):
        return (
            band.reshape(band_rows, per_device, tile_cols, channels)
            .transpose(1, 0, 2, 3)
            .reshape(per_device, tile_size, channels)
        )

    query_tiles = band_to_tiles(frame_one)
    own_keys = band_to_tiles(frame_two)
    valid = tile_lists >= 0
    slot_owner = jnp.maximum(jnp.where(valid, tile_lists, tile_lists[:, :1]), 0) // per_device
    counts = jnp.sum(valid.astype(jnp.int32), axis=1)
    me = lax.axis_index("row")
    lists_everywhere = jnp.tile(tile_lists, (owners, 1))
    lists_of = lax.all_to_all(lists_everywhere, "row", split_axis=0, concat_axis=0, tiled=True)
    lists_of = lists_of.reshape(owners, -1)
    mine = (lists_of >= 0) & (lists_of // per_device == me)
    asked = jnp.max(jnp.where(mine, lists_of % per_device, 0), axis=1)
    edges = [0, tile_size // 2, tile_size]
    state = ()
    previous = None
    for index, (start, stop) in enumerate(zip(edges[:-1], edges[1:])):
        part = own_keys[:, start:stop]
        sending = jnp.broadcast_to(part[0][None], (owners,) + part.shape[1:])
        for local in range(1, per_device):
            sending = jnp.where((asked == local)[:, None, None], part[local][None], sending)
        if previous is not None:
            previous, sending, state = lax.optimization_barrier((previous, sending, state))
        current = lax.all_to_all(sending, "row", split_axis=0, concat_axis=0, tiled=True)
        if previous is not None:
            state = attend_chunk(state, query_tiles, previous, slot_owner, counts, scale, index == 1, False)
        previous = current
    even = me % 2 == 0
    crossing = jnp.where(even, 0, 1).astype(jnp.int32).reshape(1)
    staying = (1 - crossing).astype(jnp.int32)
    crossing_tiles = attend_last_half(state, query_tiles, previous, slot_owner, counts, crossing, scale)
    staying_tiles = attend_last_half(state, query_tiles, previous, slot_owner, counts, staying, scale)

    def to_rows(tiles):
        return tiles.reshape(per_device, -1, tile_cols, channels).transpose(1, 0, 2, 3).reshape(
            -1, band_width, channels
        )

    crossing_rows = to_rows(crossing_tiles)
    staying_rows = to_rows(staying_tiles)
    count = lax.axis_size("row")
    links = [(i, i + 1) for i in range(1, count - 1, 2)] + [(i + 1, i) for i in range(1, count - 1, 2)]
    across = lax.ppermute(crossing_rows, "row", links)
    same_chip = lax.ppermute(staying_rows, "row", [(i, i ^ 1) for i in range(count)])
    warped = jnp.where(
        even,
        jnp.concatenate([crossing_rows, staying_rows], axis=0),
        jnp.concatenate([staying_rows, crossing_rows], axis=0),
    )
    from_above = jnp.where(even, across, same_chip)
    from_below = jnp.where(even, same_chip, across)
    extended = jnp.concatenate([from_above, warped, from_below], axis=0)
    hidden = jax.nn.relu(native_conv(extended, conv_one)).astype(jnp.bfloat16)
    row_ids = jnp.arange(band_rows + 2)
    inside = ((row_ids > 0) | (me > 0)) & ((row_ids < band_rows + 1) | (me < owners - 1))
    hidden = jnp.where(inside[:, None, None], hidden, jnp.zeros_like(hidden))
    branch = native_conv(hidden, conv_two)
    return (frame_one.astype(jnp.float32) + branch).astype(jnp.bfloat16)


def solution(mesh):
    in_specs = (
        P(("pairs", "row"), None, None),
        P(("pairs", "row"), None, None),
        P(("pairs", "row"), None),
        P(),
        P(),
    )
    out_specs = P(("pairs", "row"), None, None)
    return jax.shard_map(
        on_device, mesh=mesh, in_specs=in_specs, out_specs=out_specs, check_vma=False
    )
```
